32 devices in a mesh: row: 4 (over y, x), seq: 8 (over z, core).
Axes of the slice: x: 2, y: 2, z: 4, core: 2. Of those that a mesh axis runs over, the one named last changes fastest.
Arguments:
- inputs: float32 [4, 1024, 1536], P('row', 'seq'), may hold values from -6 to 6
- doc_ids: int32 [4, 1024], P('row'), may hold values from 0 to 3, never falling along the last dimension, each value on 1 to 512 neighbouring positions
- w_query: bfloat16 [1536, 1536], replicated, may hold values from -0.15625 to 0.15625
- w_key: bfloat16 [1536, 1536], replicated, may hold values from -0.15625 to 0.15625
- w_value: bfloat16 [1536, 1536], replicated, may hold values from -0.15625 to 0.15625
- w_out: bfloat16 [1536, 1536], replicated, may hold values from -1 to 1
- gain_attn: float32 [1536], replicated, may hold values from 0.25 to 1.75
- gain_ffn: float32 [1536], replicated, may hold values from 0.25 to 1.75
- conv_taps: float32 [16, 6, 11], replicated, may hold values from -0.9 to 0.9
- head_mix: float32 [8, 2, 2], replicated, may hold values from 0.25 to 1.75
- w_gate: bfloat16 [1536, 4096], P('row', 'seq'), may hold values from -0.15625 to 0.15625
- w_up: bfloat16 [1536, 4096], P('row', 'seq'), may hold values from -0.15625 to 0.15625
- w_down: bfloat16 [4096, 1536], P('seq', 'row'), may hold values from -0.09375 to 0.09375
- cotangent: float32 [4, 1024, 1536], P('row', 'seq'), may hold values from -6 to 6
Outputs:
- outputs: float32 [4, 1024, 1536], P('row', 'seq')
- grad_inputs: float32 [4, 1024, 1536], P('row', 'seq')
- grad_w_query: float32 [1536, 1536], P(('row', 'seq'))
- grad_w_key: float32 [1536, 1536], P(('row', 'seq'))
- grad_w_value: float32 [1536, 1536], P(('row', 'seq'))
- grad_w_out: float32 [1536, 1536], P(('row', 'seq'))
- grad_gain_attn: float32 [1536], P(('row', 'seq'))
- grad_gain_ffn: float32 [1536], P(('row', 'seq'))
- grad_taps: float32 [16, 6, 11], replicated
- grad_mix: float32 [8, 2, 2], replicated
- grad_w_gate: float32 [1536, 4096], P('row', 'seq')
- grad_w_up: float32 [1536, 4096], P('row', 'seq')
- grad_w_down: float32 [4096, 1536], P('seq', 'row')
The draws below stay inside these ranges and needn't reach their ends.
Inputs may be any that keep to these rules, and one draw needn't show every extreme that they name: `doc_ids`: along a row the ids never decrease; each of the 4 ids of a row covers 1 to 512 positions, and one covers exactly 512.
All inputs are finite; a program needn't handle non-finite values.
Results may differ from the reference program's by a relative error of at most 0.017.
Values may be sent and summed in bfloat16 or wider, within the bound.
No kernel may reach another device: no remote copies, remote signals or barrier semaphores. Data moves between devices by JAX's collectives and lax.ppermute only.
A program may use at most 256 MiB of HBM per device.

```python
import math
from functools import partial
import jax
import jax.numpy as jnp
import numpy as np
from jax import lax

D = 1536
HEADS = 16
HD = 96
FF = 4096
QCONV = 6
KCONV = 11
ROWS = 4
L = 1024


def levels(key, dims, split, smallest, high):
    level = 1.0
    for axis_at, blocks in split:
        steps = jax.random.uniform(jax.random.fold_in(jax.random.fold_in(key, 6), axis_at), (blocks,), jnp.float32, smallest / len(split), high / len(split))
        level = level * jnp.repeat(jnp.exp(steps), dims[axis_at] // blocks).reshape((-1,) + (1,) * (len(dims) - 1 - axis_at))
    return level


def split_up(amount, total, most, skew):
    portions = [(1 << 20) // math.isqrt(grade ** skew) + 1 for grade in range(2, amount + 1)]
    rest, holding = total - most - (amount - 1), [1] * (amount - 1)
    while rest > 0:
        free = [i for i in range(amount - 1) if holding[i] < most]
        whole, left = sum([portions[i] for i in free]), rest
        for i in free:
            extra = min(most - holding[i], max(1, left * portions[i] // whole), rest)
            holding[i] = holding[i] + extra
            rest = rest - extra
    return np.array([most] + holding)


def uneven_parts(own_key, count, total, most, skew):
    if count == 2:
        one = jax.random.randint(own_key, (), max(1, total - most), min(most, total - 1) + 1)
        return jnp.stack([one, total - one])
    lengths = jnp.asarray(split_up(count, total, most, skew), jnp.int32)
    twos = (count - 1) // 2
    donor, receiver = lengths[1:1 + 2 * twos:2], lengths[2:2 + 2 * twos:2]
    slack = jnp.minimum(donor - 1, most - receiver)
    shifted = jax.random.randint(jax.random.fold_in(own_key, 1), (twos,), 0, 1 << 20) % (slack + 1)
    lengths = lengths.at[1:1 + 2 * twos:2].set(donor - shifted).at[2:2 + 2 * twos:2].set(receiver + shifted)
    return lengths[jax.random.permutation(jax.random.fold_in(own_key, 2), count)]


def scatter_about(own_key, shape, width, bound, shards=(), held_as=jnp.bfloat16):
    values = width * jax.random.normal(own_key, shape, jnp.float32)
    if shards:
        values = values * levels(own_key, shape, shards, -0.22, 0.18)
    return jnp.clip(values, -bound, bound).astype(held_as)


def setup_inputs(seed: int = 0) -> dict:
    key_list = jax.random.split(jax.random.key(seed), 15)
    return {
        "inputs": scatter_about(key_list[0], (ROWS, L, D), 1.0, 6.0, ((0, 4), (1, 8)), jnp.float32),
        "doc_ids": jax.vmap(lambda own: jnp.searchsorted(jnp.cumsum(uneven_parts(own, 4, L, L // 2, 0)), jnp.arange(L), side="right"))(jax.random.split(key_list[1], ROWS)).reshape((ROWS, L)).astype(jnp.int32),
        "w_query": scatter_about(key_list[2], (D, D), D ** -0.5, 0.15625),
        "w_key": scatter_about(key_list[3], (D, D), D ** -0.5, 0.15625),
        "w_value": scatter_about(key_list[4], (D, D), D ** -0.5, 0.15625),
        "w_out": scatter_about(key_list[5], (D, D), (max(D // 48, 1)) ** -0.5, 1.0),
        "gain_attn": jnp.clip(1.0 + 0.15 * jax.random.normal(key_list[6], (D,), jnp.float32), 0.25, 1.75),
        "gain_ffn": jnp.clip(1.0 + 0.15 * jax.random.normal(key_list[7], (D,), jnp.float32), 0.25, 1.75),
        "conv_taps": scatter_about(key_list[8], (HEADS, QCONV, KCONV), 0.15, 0.9, (), jnp.float32),
        "head_mix": jnp.clip(1.0 + 0.15 * jax.random.normal(key_list[9], (HEADS // 2, 2, 2), jnp.float32), 0.25, 1.75),
        "w_gate": scatter_about(key_list[10], (D, FF), D ** -0.5, 0.15625, ((0, 4), (1, 8))),
        "w_up": scatter_about(key_list[11], (D, FF), D ** -0.5, 0.15625, ((0, 4), (1, 8))),
        "w_down": scatter_about(key_list[12], (FF, D), FF ** -0.5, 0.09375, ((0, 8), (1, 4))),
        "cotangent": scatter_about(key_list[13], (ROWS, L, D), 1.0, 6.0, ((0, 4), (1, 8)), jnp.float32),
    }


@jax.custom_vjp
def low(v):
    return lax.optimization_barrier(v.astype(jnp.bfloat16)).astype(jnp.float32)

@jax.custom_vjp
def low_back(v):
    return v

def low_keep(v):
    return (low(v), None)

def low_pass(kept, grad):
    return (grad,)

def back_keep(v):
    return (v, None)

def back_low(kept, grad):
    return (low(grad),)
low.defvjp(low_keep, low_pass)
low_back.defvjp(back_keep, back_low)

def matmul(left, right):
    return jnp.dot(left, right, precision=lax.Precision.HIGHEST)

def rms_norm(values, gain):
    factor = lax.rsqrt(lax.optimization_barrier(jnp.mean(values * values, axis=-1, keepdims=True)) + 1e-06)
    return values * factor * gain

def group_attention(query_grp, key_grp, value_grp, taps, mixing, allowed):
    scores = jnp.einsum('ihd,jhd->hij', query_grp, key_grp, precision=lax.Precision.HIGHEST) * HD ** (-0.5)
    scores = low_back(scores)
    masked = jnp.where(allowed[None], scores, 0.0)
    padded = jnp.pad(masked, ((0, 0), (QCONV - 1, 0), (KCONV - 1, 0)))
    conv = jnp.zeros((2, L, L), jnp.float32)
    for shift_q in range(QCONV):
        for shift_k in range(KCONV):
            weight = taps[:, shift_q, shift_k][:, None, None]
            top_q = QCONV - 1 - shift_q
            top_k = KCONV - 1 - shift_k
            conv = conv + weight * padded[:, top_q:top_q + L, top_k:top_k + L]
    logits = jnp.where(allowed[None], conv, -jnp.inf)
    highest = lax.optimization_barrier(jnp.max(logits, axis=-1, keepdims=True))
    expd = jnp.exp(logits - highest)
    probs = expd / lax.optimization_barrier(jnp.sum(expd, axis=-1, keepdims=True))
    mixed = mixing[:, 0][:, None, None] * probs[0][None] + mixing[:, 1][:, None, None] * probs[1][None]
    mixed = low(mixed)
    return jnp.einsum('hij,jhd->ihd', mixed, value_grp, precision=lax.Precision.HIGHEST)

def row_attention(query_row, key_row, value_row, doc_row, conv_taps, head_mix):
    positions = jnp.arange(L, dtype=jnp.int32)
    allowed = (positions[None, :] <= positions[:, None]) & (doc_row[None, :] == doc_row[:, None])
    groups = HEADS // 2
    query_g = jnp.moveaxis(query_row.reshape(L, groups, 2, HD), 1, 0)
    key_g = jnp.moveaxis(key_row.reshape(L, groups, 2, HD), 1, 0)
    value_g = jnp.moveaxis(value_row.reshape(L, groups, 2, HD), 1, 0)
    taps_g = conv_taps.reshape(groups, 2, QCONV, KCONV)

    def one_group(items):
        return group_attention(items[0], items[1], items[2], items[3], items[4], allowed)
    results = lax.map(jax.checkpoint(one_group), (query_g, key_g, value_g, taps_g, head_mix))
    return jnp.moveaxis(results, 0, 1).reshape(L, D)

def forward(doc_ids, inputs, w_query, w_key, w_value, w_out, gain_attn, gain_ffn, conv_taps, head_mix, w_gate, w_up, w_down):
    flat = inputs.reshape(ROWS * L, D)
    normed = low(rms_norm(flat, gain_attn))
    queries = low_back(low(matmul(normed, w_query)))
    keys = low_back(low(matmul(normed, w_key)))
    values = low_back(low(matmul(normed, w_value)))

    def per_row(carry, items):
        return (carry, jax.checkpoint(row_attention)(items[0], items[1], items[2], items[3], conv_taps, head_mix))
    _, heads_out = lax.scan(per_row, jnp.zeros((), jnp.float32), (queries.reshape(ROWS, L, D), keys.reshape(ROWS, L, D), values.reshape(ROWS, L, D), doc_ids))
    heads_out = low_back(low(heads_out.reshape(ROWS * L, D)))
    attn = low_back(matmul(heads_out, w_out))
    middle = flat + attn
    normed_ffn = low(rms_norm(middle, gain_ffn))
    gate_vals = low_back(matmul(normed_ffn, w_gate))
    up_vals = low_back(matmul(normed_ffn, w_up))
    hidden = low(jax.nn.silu(gate_vals) * up_vals)
    result = middle + low_back(matmul(hidden, w_down))
    return result.reshape(ROWS, L, D)

def reference(inputs, doc_ids, w_query, w_key, w_value, w_out, gain_attn, gain_ffn, conv_taps, head_mix, w_gate, w_up, w_down, cotangent):
    primal = partial(forward, doc_ids)
    result, pullback = jax.vjp(primal, inputs, w_query.astype(jnp.float32), w_key.astype(jnp.float32), w_value.astype(jnp.float32), w_out.astype(jnp.float32), gain_attn, gain_ffn, conv_taps, head_mix, w_gate.astype(jnp.float32), w_up.astype(jnp.float32), w_down.astype(jnp.float32))
    grads = pullback(cotangent)
    return (result, grads[0], grads[1], grads[2], grads[3], grads[4], grads[5], grads[6], grads[7], grads[8], grads[9], grads[10], grads[11])
```

```python
import jax
import jax.numpy as jnp
from jax import lax
from jax.sharding import PartitionSpec as P

HEADS = 16
HD = 96
QCONV = 6
KCONV = 11
PAD = 8

epsilon = 1e-06


def rms_scale(values):
    return lax.rsqrt(jnp.mean(values * values, axis=-1, keepdims=True) + epsilon)


def project(values, weight):
    return jnp.dot(values, weight, preferred_element_type=jnp.float32)


def contract_rows(left, right):
    return lax.dot_general(
        left, right, (((0,), (0,)), ((), ())), preferred_element_type=jnp.float32
    )


def contract_cols(left, right):
    return lax.dot_general(
        left, right, (((1,), (1,)), ((), ())), preferred_element_type=jnp.float32
    )


def mix_heads(probs, mixing):
    return mixing[:, 0][:, None, None] * probs[0:1] + mixing[:, 1][:, None, None] * probs[1:2]


def mix_back(grads, mixing):
    return mixing[0, :][:, None, None] * grads[0:1] + mixing[1, :][:, None, None] * grads[1:2]


def shards(
    inputs,
    doc_ids,
    w_query,
    w_key,
    w_value,
    w_out,
    gain_attn,
    gain_ffn,
    conv_taps,
    head_mix,
    w_gate,
    w_up,
    w_down,
    cotangent,
):
    row_dev, blk, width = inputs.shape
    assert row_dev == 1
    seq_count = lax.axis_size("seq")
    row_count = lax.axis_size("row")
    seq_index = lax.axis_index("seq")
    row_index = lax.axis_index("row")
    length = blk * seq_count
    groups = HEADS // 2
    assert seq_count % groups == 0
    splits = seq_count // groups
    span = length // splits
    pw = 2 * HD
    ext = span + 2 * PAD
    xrows = span + PAD
    score_scale = HD ** (-0.5)
    pair = seq_index // splits
    part = seq_index % splits
    q0 = part * span

    flat_in = inputs.reshape(blk, width)
    scale_one = rms_scale(flat_in)
    normed = (flat_in * scale_one * gain_attn).astype(jnp.bfloat16)
    normed_all = lax.all_gather(normed, "seq", axis=0, tiled=True)

    wq_g = lax.dynamic_slice_in_dim(w_query, pair * pw, pw, 1)
    wk_g = lax.dynamic_slice_in_dim(w_key, pair * pw, pw, 1)
    wv_g = lax.dynamic_slice_in_dim(w_value, pair * pw, pw, 1)
    wo_g = lax.dynamic_slice_in_dim(w_out, pair * pw, pw, 0)
    taps = lax.dynamic_slice_in_dim(conv_taps, pair * 2, 2, 0)
    mixing = lax.dynamic_index_in_dim(head_mix, pair, 0, keepdims=False)

    normed_pad = jnp.pad(normed_all, ((PAD, PAD), (0, 0)))
    q_ext = project(lax.dynamic_slice_in_dim(normed_pad, q0, ext, 0), wq_g).astype(jnp.bfloat16)
    k_all = project(normed_all, wk_g).astype(jnp.bfloat16)
    v_all = project(normed_all, wv_g).astype(jnp.bfloat16)
    q3 = q_ext.reshape(ext, 2, HD)
    k3 = k_all.reshape(length, 2, HD)
    v3 = v_all.reshape(length, 2, HD)

    docs = doc_ids[0]
    docs_pad = jnp.pad(docs, (PAD, PAD), constant_values=-1)
    ext_docs = lax.dynamic_slice_in_dim(docs_pad, q0, ext, 0)
    ext_pos = q0 - PAD + jnp.arange(ext, dtype=jnp.int32)
    key_pos = jnp.arange(length, dtype=jnp.int32)
    mask_e = (key_pos[None, :] <= ext_pos[:, None]) & (ext_docs[:, None] == docs[None, :])

    scores = jnp.einsum("ihd,jhd->hij", q3, k3, preferred_element_type=jnp.float32) * score_scale
    masked = jnp.where(mask_e[None], scores, 0.0)
    mp = jnp.pad(masked, ((0, 0), (0, 0), (KCONV - 1, 0)))
    conv_x = jnp.zeros((2, xrows, length), jnp.float32)
    for a in range(QCONV):
        for b in range(KCONV):
            weight = taps[:, a, b][:, None, None]
            conv_x = conv_x + weight * mp[:, PAD - a : PAD - a + xrows, KCONV - 1 - b : KCONV - 1 - b + length]
    mask_x = mask_e[PAD : PAD + xrows]
    logits = jnp.where(mask_x[None], conv_x, -jnp.inf)
    highest = jnp.max(logits, axis=-1, keepdims=True)
    highest = jnp.where(highest > -jnp.inf, highest, 0.0)
    expd = jnp.exp(logits - highest)
    denom = jnp.sum(expd, axis=-1, keepdims=True)
    probs_x = expd / jnp.where(denom > 0, denom, 1.0)
    mixed_own = mix_heads(probs_x[:, :span], mixing).astype(jnp.bfloat16)
    heads_own = (
        jnp.einsum("hij,jhd->ihd", mixed_own, v3, preferred_element_type=jnp.float32)
        .astype(jnp.bfloat16)
        .reshape(span, pw)
    )

    def to_tokens(values):
        cols = values.shape[1]
        if splits == 1:
            full = values
        else:
            full = lax.dynamic_update_slice_in_dim(
                jnp.zeros((length, cols), values.dtype), values, q0, 0
            )
        got = lax.all_to_all(full, "seq", 0, 0, tiled=True)
        got = got.reshape(groups, splits, blk, cols)
        if splits > 1:
            got = jnp.sum(got.astype(jnp.float32), axis=1).astype(values.dtype)
        else:
            got = got[:, 0]
        return got

    heads_tok = jnp.transpose(to_tokens(heads_own), (1, 0, 2)).reshape(blk, width)
    middle = flat_in + project(heads_tok, w_out)
    scale_two = rms_scale(middle)
    normed_ffn = (middle * scale_two * gain_ffn).astype(jnp.bfloat16)
    gate_full, up_full, down_full = (
        lax.all_gather(w_gate, "row", axis=0, tiled=True),
        lax.all_gather(w_up, "row", axis=0, tiled=True),
        lax.all_gather(w_down, "row", axis=1, tiled=True),
    )
    hid_width = gate_full.shape[1]
    joint = jnp.concatenate([gate_full, up_full], axis=1)
    ffn_rows = lax.all_gather(normed_ffn, "seq", axis=0, tiled=True)
    gate_up = project(ffn_rows, joint)
    gate_vals = gate_up[:, :hid_width]
    up_vals = gate_up[:, hid_width:]
    hidden = (jax.nn.silu(gate_vals) * up_vals).astype(jnp.bfloat16)
    ffn_out = lax.psum_scatter(
        project(hidden, down_full).astype(jnp.bfloat16), "seq", scatter_dimension=0, tiled=True
    ).astype(jnp.float32)
    outputs = middle + ffn_out
    cot_flat = cotangent.reshape(blk, width)
    cot_low = cot_flat.astype(jnp.bfloat16)
    cot_rows = lax.all_gather(cot_low, "seq", axis=0, tiled=True)
    grad_hidden = contract_cols(cot_rows, down_full)
    grad_down_part = contract_rows(hidden, cot_rows)
    sigmoid_gate = jax.nn.sigmoid(gate_vals)
    grad_gate_vals = grad_hidden * up_vals * sigmoid_gate * (1.0 + gate_vals * (1.0 - sigmoid_gate))
    grad_up_vals = grad_hidden * gate_vals * sigmoid_gate
    grad_joint = jnp.concatenate([grad_gate_vals, grad_up_vals], axis=1).astype(jnp.bfloat16)
    grad_joint_w = contract_rows(ffn_rows, grad_joint)
    grad_normed_ffn = lax.psum_scatter(
        contract_cols(grad_joint, joint).astype(jnp.bfloat16),
        "seq",
        scatter_dimension=0,
        tiled=True,
    ).astype(jnp.float32)
    grad_w_gate, grad_w_up, grad_w_down = (
        lax.psum_scatter(
            grad_joint_w[:, :hid_width].astype(jnp.bfloat16), "row", scatter_dimension=0, tiled=True
        ).astype(jnp.float32),
        lax.psum_scatter(
            grad_joint_w[:, hid_width:].astype(jnp.bfloat16), "row", scatter_dimension=0, tiled=True
        ).astype(jnp.float32),
        lax.psum_scatter(
            grad_down_part.astype(jnp.bfloat16), "row", scatter_dimension=1, tiled=True
        ).astype(jnp.float32),
    )
    gain_ffn_part = jnp.sum(grad_normed_ffn * middle * scale_two, axis=0)
    scaled_two = grad_normed_ffn * gain_ffn
    grad_middle = (
        cot_flat
        + scale_two * scaled_two
        - middle * scale_two**3 * jnp.mean(scaled_two * middle, axis=-1, keepdims=True)
    )
    grad_attn = grad_middle.astype(jnp.bfloat16)
    grad_attn_all = lax.all_gather(grad_attn, "seq", axis=0, tiled=True)
    grad_attn_pad = jnp.pad(grad_attn_all, ((0, PAD), (0, 0)))
    grad_heads_x = contract_cols(
        lax.dynamic_slice_in_dim(grad_attn_pad, q0, xrows, 0), wo_g
    ).astype(jnp.bfloat16)
    gh3 = grad_heads_x.reshape(xrows, 2, HD)
    grad_out_part = contract_rows(heads_own, lax.dynamic_slice_in_dim(grad_attn_all, q0, span, 0))

    grad_mixed = jnp.einsum("ihd,jhd->hij", gh3, v3, preferred_element_type=jnp.float32)
    grad_v_part = jnp.einsum(
        "hij,ihd->jhd", mixed_own, gh3[:span], preferred_element_type=jnp.float32
    ).reshape(length, pw)
    grad_mix_part = jnp.stack(
        [
            jnp.sum(grad_mixed[:, :span] * probs_x[0:1, :span], axis=(1, 2)),
            jnp.sum(grad_mixed[:, :span] * probs_x[1:2, :span], axis=(1, 2)),
        ],
        axis=1,
    )
    grad_probs = mix_back(grad_mixed, mixing)
    inner = jnp.sum(grad_probs * probs_x, axis=-1, keepdims=True)
    grad_conv = probs_x * (grad_probs - inner)
    tap_entries = []
    for a in range(QCONV):
        for b in range(KCONV):
            piece = mp[:, PAD - a : PAD - a + span, KCONV - 1 - b : KCONV - 1 - b + length]
            tap_entries.append(jnp.sum(grad_conv[:, :span] * piece, axis=(1, 2)))
    grad_taps_part = jnp.stack(tap_entries, axis=1).reshape(2, QCONV, KCONV)
    gc_pad = jnp.pad(grad_conv, ((0, 0), (0, 0), (0, KCONV - 1)))
    grad_masked = jnp.zeros((2, span, length), jnp.float32)
    for a in range(QCONV):
        for b in range(KCONV):
            weight = taps[:, a, b][:, None, None]
            grad_masked = grad_masked + weight * gc_pad[:, a : a + span, b : b + length]
    grad_scores = jnp.where(mask_e[None, PAD : PAD + span], grad_masked, 0.0).astype(jnp.bfloat16)
    grad_q_own = (
        jnp.einsum("hij,jhd->ihd", grad_scores, k3, preferred_element_type=jnp.float32) * score_scale
    ).astype(jnp.bfloat16).reshape(span, pw)
    grad_k_part = (
        jnp.einsum("hij,ihd->jhd", grad_scores, q3[PAD : PAD + span], preferred_element_type=jnp.float32)
        * score_scale
    ).reshape(length, pw)

    def split_sum(values):
        if splits == 1:
            return values
        total = values
        for step in range(1, splits):
            route = []
            for s in range(seq_count):
                base = (s // splits) * splits
                route.append((s, base + (s - base + step) % splits))
            total = total + lax.ppermute(values, "seq", route)
        return total

    grad_k_low = split_sum(grad_k_part).astype(jnp.bfloat16)
    grad_v_low = split_sum(grad_v_part).astype(jnp.bfloat16)
    grad_k_own = lax.dynamic_slice_in_dim(grad_k_low, q0, span, 0)
    grad_v_own = lax.dynamic_slice_in_dim(grad_v_low, q0, span, 0)

    normed_own = lax.dynamic_slice_in_dim(normed_all, q0, span, 0)
    rows_per_dev = width // (row_count * seq_count)

    def finish_in(partial):
        red = lax.psum_scatter(partial, "row", scatter_dimension=0, tiled=True)
        got = lax.all_to_all(red, "seq", 0, 0, tiled=True)
        got = got.reshape(groups, splits, rows_per_dev, pw).sum(axis=1)
        return jnp.transpose(got, (1, 0, 2)).reshape(rows_per_dev, width)

    grad_w_query = finish_in(contract_rows(normed_own, grad_q_own))
    grad_w_key = finish_in(contract_rows(normed_own, grad_k_own))
    grad_w_value = finish_in(contract_rows(normed_own, grad_v_own))

    red_out = lax.psum_scatter(grad_out_part, "row", scatter_dimension=0, tiled=True)
    red_out = red_out.reshape(splits, rows_per_dev, width)
    grad_w_out = jnp.zeros((rows_per_dev, width), jnp.float32)
    for src_part in range(splits):
        for j in range(splits):
            route = []
            for r in range(row_count):
                for g in range(groups):
                    src = r * seq_count + g * splits + src_part
                    dst = g * row_count * splits + r * splits + j
                    route.append((src, dst))
            grad_w_out = grad_w_out + lax.ppermute(red_out[j], ("row", "seq"), route)

    grad_tok = to_tokens(jnp.concatenate([grad_q_own, grad_k_own, grad_v_own], axis=1))
    grad_tok = grad_tok.reshape(groups, blk, 3, pw)
    gq_tok = jnp.transpose(grad_tok[:, :, 0], (1, 0, 2)).reshape(blk, width)
    gk_tok = jnp.transpose(grad_tok[:, :, 1], (1, 0, 2)).reshape(blk, width)
    gv_tok = jnp.transpose(grad_tok[:, :, 2], (1, 0, 2)).reshape(blk, width)
    grad_normed = (
        contract_cols(gq_tok, w_query) + contract_cols(gk_tok, w_key) + contract_cols(gv_tok, w_value)
    )
    gain_attn_part = jnp.sum(grad_normed * flat_in * scale_one, axis=0)
    scaled_one = grad_normed * gain_attn
    grad_inputs = (
        grad_middle
        + scale_one * scaled_one
        - flat_in * scale_one**3 * jnp.mean(scaled_one * flat_in, axis=-1, keepdims=True)
    )
    grad_gain_attn, grad_gain_ffn = (
        lax.psum_scatter(gain_attn_part, ("row", "seq"), scatter_dimension=0, tiled=True),
        lax.psum_scatter(gain_ffn_part, ("row", "seq"), scatter_dimension=0, tiled=True),
    )
    taps_full = lax.dynamic_update_slice_in_dim(
        jnp.zeros((HEADS, QCONV, KCONV), jnp.float32), grad_taps_part, pair * 2, 0
    )
    mix_full = lax.dynamic_update_slice_in_dim(
        jnp.zeros((groups, 2, 2), jnp.float32), grad_mix_part[None], pair, 0
    )
    grad_taps, grad_mix = lax.psum((taps_full, mix_full), ("row", "seq"))
    return (
        outputs.reshape(row_dev, blk, width),
        grad_inputs.reshape(row_dev, blk, width),
        grad_w_query,
        grad_w_key,
        grad_w_value,
        grad_w_out,
        grad_gain_attn,
        grad_gain_ffn,
        grad_taps,
        grad_mix,
        grad_w_gate,
        grad_w_up,
        grad_w_down,
    )


def solution(mesh):
    return jax.shard_map(
        shards,
        mesh=mesh,
        in_specs=(
            P("row", "seq", None),
            P("row", None),
            P(),
            P(),
            P(),
            P(),
            P(),
            P(),
            P(),
            P(),
            P("row", "seq"),
            P("row", "seq"),
            P("seq", "row"),
            P("row", "seq", None),
        ),
        out_specs=(
            P("row", "seq", None),
            P("row", "seq", None),
            P(("row", "seq"), None),
            P(("row", "seq"), None),
            P(("row", "seq"), None),
            P(("row", "seq"), None),
            P(("row", "seq")),
            P(("row", "seq")),
            P(),
            P(),
            P("row", "seq"),
            P("row", "seq"),
            P("seq", "row"),
        ),
        check_vma=False,
    )
```

```python
import jax
import jax.numpy as jnp
from jax import lax
from jax.sharding import PartitionSpec as P
from jax.experimental import pallas as pl
from jax.experimental.pallas import tpu as pltpu

HEADS = 16
HD = 96
QCONV = 6
KCONV = 11
PAD = 8
TQ = 128
EXT = TQ + PAD
SCALE = HD ** (-0.5)
TAPS = QCONV * KCONV

epsilon = 1e-06


def rms_scale(values):
    return lax.rsqrt(jnp.mean(values * values, axis=-1, keepdims=True) + epsilon)


def project(values, weight):
    return jnp.dot(values, weight, preferred_element_type=jnp.float32)


def contract_rows(left, right):
    return lax.dot_general(
        left, right, (((0,), (0,)), ((), ())), preferred_element_type=jnp.float32
    )


def contract_cols(left, right):
    return lax.dot_general(
        left, right, (((1,), (1,)), ((), ())), preferred_element_type=jnp.float32
    )


def normed_pad_tail(values, extra):
    return jnp.pad(values, ((PAD, TQ * extra), (0, 0)))


def window_start(block, nw, length):
    return pl.multiple_of(jnp.clip((block - nw + 1) * TQ, 0, length - nw * TQ), TQ)


def tap_accumulate(sh_ref, acc_ref, taps_ref, head, width):
    ncols = width // 128

    def body(idx, carry):
        r0 = pl.multiple_of((idx // ncols) * 8, 8)
        c0 = pl.multiple_of((idx % ncols) * 128, 128)
        tiles = [sh_ref[b, pl.ds(r0, 8), pl.ds(c0, 128)] for b in range(KCONV)]
        for a in range(QCONV):
            base = head * TAPS + a * KCONV
            total = taps_ref[base] * tiles[0]
            for b in range(1, KCONV):
                total = total + taps_ref[base + b] * tiles[b]
            acc_ref[a, pl.ds(r0, 8), pl.ds(c0, 128)] = total
        return carry

    lax.fori_loop(0, (EXT // 8) * ncols, body, 0)


def tap_products(sh_ref, g_ref, width):
    ncols = width // 128
    sums = []
    for b in range(KCONV):

        def body(idx, accs):
            r0 = pl.multiple_of((idx // ncols) * 8, 8)
            c0 = pl.multiple_of((idx % ncols) * 128, 128)
            tile = sh_ref[b, pl.ds(r0, 8), pl.ds(c0, 128)]
            return tuple(
                accs[a] + g_ref[a, pl.ds(r0, 8), pl.ds(c0, 128)] * tile for a in range(QCONV)
            )

        start = tuple(jnp.zeros((8, 128), jnp.float32) for _ in range(QCONV))
        sums.append(lax.fori_loop(0, (EXT // 8) * ncols, body, start))
    return sums


def masks(block, kstart, width, rdoc_ref, kdoc_ref):
    keydoc = kdoc_ref[:, pl.ds(kstart, width)]
    ext_pos = block * TQ - PAD + lax.broadcasted_iota(jnp.int32, (EXT, width), 0)
    key_ext = kstart + lax.broadcasted_iota(jnp.int32, (EXT, width), 1)
    allowed_ext = (key_ext <= ext_pos) & (rdoc_ref[0] == keydoc)
    own_pos = block * TQ + lax.broadcasted_iota(jnp.int32, (TQ, width), 0)
    key_own = kstart + lax.broadcasted_iota(jnp.int32, (TQ, width), 1)
    allowed_own = (key_own <= own_pos) & (rdoc_ref[0, PAD:, :] == keydoc)
    return allowed_ext, allowed_own


def masked_shifts(q_ref, k_ref, head, kstart, width, allowed_ext, sh_ref):
    keys = k_ref[head, pl.ds(kstart, width), :]
    scores = lax.dot_general(
        q_ref[0, head], keys, (((1,), (1,)), ((), ())), preferred_element_type=jnp.float32
    ) * SCALE
    masked = jnp.where(allowed_ext, scores, 0.0)
    col = lax.broadcasted_iota(jnp.int32, (EXT, width), 1)
    sh_ref[0] = masked
    for b in range(1, KCONV):
        sh_ref[b] = jnp.where(col >= b, pltpu.roll(masked, b, 1), 0.0)


def fwd_kernel(toff_ref, taps_ref, mix_ref, q_ref, k_ref, v_ref, rdoc_ref, kdoc_ref,
               heads_ref, probs_ref, sh_ref, acc_ref, *, nw, length):
    width = nw * TQ
    block = toff_ref[0] + pl.program_id(0)
    kstart = window_start(block, nw, length)
    allowed_ext, allowed_own = masks(block, kstart, width, rdoc_ref, kdoc_ref)
    for head in range(2):
        masked_shifts(q_ref, k_ref, head, kstart, width, allowed_ext, sh_ref)
        tap_accumulate(sh_ref, acc_ref, taps_ref, head, width)
        conv = acc_ref[0]
        for a in range(1, QCONV):
            conv = conv + pltpu.roll(acc_ref[a], a, 0)
        logits = jnp.where(allowed_own, conv[PAD:], -jnp.inf)
        highest = jnp.max(logits, axis=1, keepdims=True)
        highest = jnp.where(highest > -jnp.inf, highest, 0.0)
        expd = jnp.exp(logits - highest)
        denom = jnp.sum(expd, axis=1, keepdims=True)
        probs_ref[0, head] = expd / jnp.where(denom > 0.0, denom, 1.0)
    p0 = probs_ref[0, 0]
    p1 = probs_ref[0, 1]
    for c in range(2):
        mixed = (mix_ref[2 * c] * p0 + mix_ref[2 * c + 1] * p1).astype(jnp.bfloat16)
        heads_ref[0, c] = jnp.dot(
            mixed, v_ref[c, pl.ds(kstart, width), :], preferred_element_type=jnp.float32
        ).astype(jnp.bfloat16)


def attention_forward(toff, taps_flat, mix_flat, q_blocks, k_heads, v_heads, row_docs, key_docs, nw, length):
    nb_all = q_blocks.shape[0]
    width = nw * TQ
    smem = pl.BlockSpec(memory_space=pltpu.SMEM)
    flops = nb_all * 2 * (4 * EXT * width * HD + 2 * TAPS * EXT * width)
    return pl.pallas_call(
        lambda *refs: fwd_kernel(*refs, nw=nw, length=length),
        grid=(nb_all,),
        in_specs=[
            smem,
            smem,
            smem,
            pl.BlockSpec((1, 2, EXT, HD), lambda t: (t, 0, 0, 0)),
            pl.BlockSpec((2, length, HD), lambda t: (0, 0, 0)),
            pl.BlockSpec((2, length, HD), lambda t: (0, 0, 0)),
            pl.BlockSpec((1, EXT, 1), lambda t: (t, 0, 0)),
            pl.BlockSpec((1, length), lambda t: (0, 0)),
        ],
        out_specs=[
            pl.BlockSpec((1, 2, TQ, HD), lambda t: (t, 0, 0, 0)),
            pl.BlockSpec((1, 2, TQ, width), lambda t: (t, 0, 0, 0)),
        ],
        out_shape=[
            jax.ShapeDtypeStruct((nb_all, 2, TQ, HD), jnp.bfloat16),
            jax.ShapeDtypeStruct((nb_all, 2, TQ, width), jnp.float32),
        ],
        scratch_shapes=[
            pltpu.VMEM((KCONV, EXT, width), jnp.float32),
            pltpu.VMEM((QCONV, EXT, width), jnp.float32),
        ],
        compiler_params=pltpu.CompilerParams(
            dimension_semantics=("arbitrary",), vmem_limit_bytes=56 * 1024 * 1024
        ),
        cost_estimate=pl.CostEstimate(
            flops=flops, transcendentals=nb_all * 2 * TQ * width,
            bytes_accessed=nb_all * 2 * TQ * width * 4 + 4 * length * HD * 2,
        ),
    )(toff, taps_flat, mix_flat, q_blocks, k_heads, v_heads, row_docs, key_docs)


def bwd_kernel(toff_ref, taps_ref, mix_ref, q_ref, qo_ref, k_ref, v_ref, rdoc_ref, kdoc_ref,
               probs_ref, gh_ref, gq_ref, gk_ref, gv_ref, tacc_ref, macc_ref,
               carry_ref, sh_ref, acc_ref, g_ref, gx_ref, *, nw, length, nb, nb_all):
    width = nw * TQ
    step = pl.program_id(0)
    local = nb_all - 1 - step
    block = toff_ref[0] + local
    kstart = window_start(block, nw, length)

    @pl.when(step == 0)
    def _init():
        gk_ref[...] = jnp.zeros(gk_ref.shape, jnp.float32)
        gv_ref[...] = jnp.zeros(gv_ref.shape, jnp.float32)
        tacc_ref[...] = jnp.zeros(tacc_ref.shape, jnp.float32)
        macc_ref[...] = jnp.zeros(macc_ref.shape, jnp.float32)
        carry_ref[...] = jnp.zeros(carry_ref.shape, jnp.float32)

    allowed_ext, allowed_own = masks(block, kstart, width, rdoc_ref, kdoc_ref)
    gm = [
        lax.dot_general(
            gh_ref[0, c], v_ref[c, pl.ds(kstart, width), :], (((1,), (1,)), ((), ())),
            preferred_element_type=jnp.float32,
        )
        for c in range(2)
    ]
    probs = [probs_ref[0, 0], probs_ref[0, 1]]
    gc = []
    for e in range(2):
        gp = mix_ref[e] * gm[0] + mix_ref[2 + e] * gm[1]
        inner = jnp.sum(gp * probs[e], axis=1, keepdims=True)
        gc.append(probs[e] * (gp - inner))

    def own_sums():
        for c in range(2):
            for e in range(2):
                macc_ref[pl.ds(2 * c + e, 1), :] += jnp.sum(gm[c] * probs[e], axis=0, keepdims=True)
            mixed = (mix_ref[2 * c] * probs[0] + mix_ref[2 * c + 1] * probs[1]).astype(jnp.bfloat16)
            gv_ref[c, pl.ds(kstart, width), :] += lax.dot_general(
                mixed, gh_ref[0, c], (((0,), (0,)), ((), ())), preferred_element_type=jnp.float32
            )

    def head_taps(e):
        masked_shifts(q_ref, k_ref, e, kstart, width, allowed_ext, sh_ref)
        gcp = jnp.concatenate([jnp.zeros((PAD, width), jnp.float32), gc[e]], axis=0)
        g_ref[0] = gcp
        for a in range(1, QCONV):
            g_ref[a] = pltpu.roll(gcp, EXT - a, 0)
        sums = tap_products(sh_ref, g_ref, width)
        for b in range(KCONV):
            for a in range(QCONV):
                tacc_ref[e * TAPS + a * KCONV + b] += sums[b][a]

    def head_keys(e, gs):
        gk_ref[e, pl.ds(kstart, width), :] += lax.dot_general(
            gs, qo_ref[0, e], (((0,), (0,)), ((), ())), preferred_element_type=jnp.float32
        ) * SCALE

    nxt = [carry_ref[e, :, pl.ds(kstart, width + TQ)] for e in range(2)]
    if nb < nb_all:
        pl.when(local < nb)(own_sums)
    else:
        own_sums()
    for e in range(2):
        if nb < nb_all:
            pl.when(local < nb)(lambda: head_taps(e))
        else:
            head_taps(e)
        gx_ref[pl.ds(0, TQ), pl.ds(0, width)] = gc[e]
        gx_ref[pl.ds(0, TQ), pl.ds(width, TQ)] = jnp.zeros((TQ, TQ), jnp.float32)
        gx_ref[pl.ds(TQ, PAD), :] = nxt[e]
        gxv = gx_ref[...]
        sh_ref[0] = gxv[:, :width]
        for b in range(1, KCONV):
            sh_ref[b] = pltpu.roll(gxv, width + TQ - b, 1)[:, :width]
        tap_accumulate(sh_ref, acc_ref, taps_ref, e, width)
        gmk = acc_ref[0]
        for a in range(1, QCONV):
            gmk = gmk + pltpu.roll(acc_ref[a], EXT - a, 0)
        gs = jnp.where(allowed_own, gmk[:TQ], 0.0).astype(jnp.bfloat16)
        gq_ref[0, e] = (
            jnp.dot(gs, k_ref[e, pl.ds(kstart, width), :], preferred_element_type=jnp.float32) * SCALE
        ).astype(jnp.bfloat16)
        if nb < nb_all:
            pl.when(local < nb)(lambda: head_keys(e, gs))
        else:
            head_keys(e, gs)
    carry_ref[...] = jnp.zeros(carry_ref.shape, jnp.float32)
    for e in range(2):
        carry_ref[e, :, pl.ds(kstart, width)] = gc[e][:PAD]


def attention_backward(toff, taps_flat, mix_flat, q_blocks, q_own, k_heads, v_heads, row_docs, key_docs,
                       probs_blk, gh_blocks, nw, length, nb):
    nb_all = q_blocks.shape[0]
    width = nw * TQ
    smem = pl.BlockSpec(memory_space=pltpu.SMEM)
    rev = lambda s: nb_all - 1 - s
    flops = nb_all * 2 * (8 * TQ * width * HD + 6 * TAPS * EXT * width)
    return pl.pallas_call(
        lambda *refs: bwd_kernel(*refs, nw=nw, length=length, nb=nb, nb_all=nb_all),
        grid=(nb_all,),
        in_specs=[
            smem,
            smem,
            smem,
            pl.BlockSpec((1, 2, EXT, HD), lambda s: (rev(s), 0, 0, 0)),
            pl.BlockSpec((1, 2, TQ, HD), lambda s: (rev(s), 0, 0, 0)),
            pl.BlockSpec((2, length, HD), lambda s: (0, 0, 0)),
            pl.BlockSpec((2, length, HD), lambda s: (0, 0, 0)),
            pl.BlockSpec((1, EXT, 1), lambda s: (rev(s), 0, 0)),
            pl.BlockSpec((1, length), lambda s: (0, 0)),
            pl.BlockSpec((1, 2, TQ, width), lambda s: (rev(s), 0, 0, 0)),
            pl.BlockSpec((1, 2, TQ, HD), lambda s: (rev(s), 0, 0, 0)),
        ],
        out_specs=[
            pl.BlockSpec((1, 2, TQ, HD), lambda s: (rev(s), 0, 0, 0)),
            pl.BlockSpec((2, length, HD), lambda s: (0, 0, 0)),
            pl.BlockSpec((2, length, HD), lambda s: (0, 0, 0)),
            pl.BlockSpec((2 * TAPS, 8, 128), lambda s: (0, 0, 0)),
            pl.BlockSpec((4, width), lambda s: (0, 0)),
        ],
        out_shape=[
            jax.ShapeDtypeStruct((nb_all, 2, TQ, HD), jnp.bfloat16),
            jax.ShapeDtypeStruct((2, length, HD), jnp.float32),
            jax.ShapeDtypeStruct((2, length, HD), jnp.float32),
            jax.ShapeDtypeStruct((2 * TAPS, 8, 128), jnp.float32),
            jax.ShapeDtypeStruct((4, width), jnp.float32),
        ],
        scratch_shapes=[
            pltpu.VMEM((2, PAD, length + TQ), jnp.float32),
            pltpu.VMEM((KCONV, EXT, width), jnp.float32),
            pltpu.VMEM((QCONV, EXT, width), jnp.float32),
            pltpu.VMEM((QCONV, EXT, width), jnp.float32),
            pltpu.VMEM((EXT, width + TQ), jnp.float32),
        ],
        compiler_params=pltpu.CompilerParams(
            dimension_semantics=("arbitrary",), vmem_limit_bytes=60 * 1024 * 1024
        ),
        cost_estimate=pl.CostEstimate(
            flops=flops, transcendentals=0,
            bytes_accessed=nb_all * 2 * TQ * width * 4 + 8 * length * HD * 4,
        ),
    )(toff, taps_flat, mix_flat, q_blocks, q_own, k_heads, v_heads, row_docs, key_docs, probs_blk, gh_blocks)


def shards(
    inputs,
    doc_ids,
    w_query,
    w_key,
    w_value,
    w_out,
    gain_attn,
    gain_ffn,
    conv_taps,
    head_mix,
    w_gate,
    w_up,
    w_down,
    cotangent,
):
    row_dev, blk, width = inputs.shape
    assert row_dev == 1
    seq_count = lax.axis_size("seq")
    row_count = lax.axis_size("row")
    seq_index = lax.axis_index("seq")
    row_index = lax.axis_index("row")
    length = blk * seq_count
    groups = HEADS // 2
    assert seq_count % groups == 0
    splits = seq_count // groups
    span = length // splits
    pw = 2 * HD
    pair = seq_index // splits
    part = seq_index % splits
    q0 = part * span

    flat_in = inputs.reshape(blk, width)
    scale_one = rms_scale(flat_in)
    normed = (flat_in * scale_one * gain_attn).astype(jnp.bfloat16)
    normed_all = lax.all_gather(normed, "seq", axis=0, tiled=True)

    wq_g = lax.dynamic_slice_in_dim(w_query, pair * pw, pw, 1)
    wk_g = lax.dynamic_slice_in_dim(w_key, pair * pw, pw, 1)
    wv_g = lax.dynamic_slice_in_dim(w_value, pair * pw, pw, 1)
    wo_g = lax.dynamic_slice_in_dim(w_out, pair * pw, pw, 0)
    taps = lax.dynamic_slice_in_dim(conv_taps, pair * 2, 2, 0)
    mixing = lax.dynamic_index_in_dim(head_mix, pair, 0, keepdims=False)

    k_all = project(normed_all, wk_g).astype(jnp.bfloat16)
    v_all = project(normed_all, wv_g).astype(jnp.bfloat16)
    k3 = k_all.reshape(length, 2, HD)
    v3 = v_all.reshape(length, 2, HD)

    docs = doc_ids[0]
    nb = span // TQ
    extra = 1 if splits > 1 else 0
    nb_all = nb + extra
    doc_cap = length // 2
    nw = min(length // TQ, (doc_cap + QCONV - 2 + TQ - 1) // TQ + 1)
    q_tail = normed_pad_tail(normed_all, extra)
    q_rows = project(lax.dynamic_slice_in_dim(q_tail, q0, nb_all * TQ + PAD, 0), wq_g).astype(jnp.bfloat16)
    q_blocks = jnp.stack([q_rows[t * TQ : t * TQ + EXT] for t in range(nb_all)])
    q_blocks = jnp.transpose(q_blocks.reshape(nb_all, EXT, 2, HD), (0, 2, 1, 3))
    q_own = q_blocks[:, :, PAD:]
    k_heads = jnp.transpose(k3, (1, 0, 2))
    v_heads = jnp.transpose(v3, (1, 0, 2))
    docs_tail = jnp.pad(docs, (PAD, TQ * extra), constant_values=-1)
    doc_rows = lax.dynamic_slice_in_dim(docs_tail, q0, nb_all * TQ + PAD, 0)
    row_docs = jnp.stack([doc_rows[t * TQ : t * TQ + EXT] for t in range(nb_all)])[:, :, None]
    key_docs = docs[None, :]
    toff = (q0 // TQ).astype(jnp.int32).reshape(1)
    taps_flat = taps.reshape(2 * QCONV * KCONV)
    mix_flat = mixing.reshape(4)
    heads_blk, probs_blk = attention_forward(
        toff, taps_flat, mix_flat, q_blocks, k_heads, v_heads, row_docs, key_docs, nw, length
    )
    heads_own = jnp.transpose(heads_blk[:nb], (0, 2, 1, 3)).reshape(span, pw)

    def to_tokens(values):
        cols = values.shape[1]
        if splits == 1:
            full = values
        else:
            full = lax.dynamic_update_slice_in_dim(
                jnp.zeros((length, cols), values.dtype), values, q0, 0
            )
        got = lax.all_to_all(full, "seq", 0, 0, tiled=True)
        got = got.reshape(groups, splits, blk, cols)
        if splits > 1:
            got = jnp.sum(got.astype(jnp.float32), axis=1).astype(values.dtype)
        else:
            got = got[:, 0]
        return got

    heads_tok = jnp.transpose(to_tokens(heads_own), (1, 0, 2)).reshape(blk, width)
    middle = flat_in + project(heads_tok, w_out)
    scale_two = rms_scale(middle)
    normed_ffn = (middle * scale_two * gain_ffn).astype(jnp.bfloat16)
    gate_full, up_full, down_full = (
        lax.all_gather(w_gate, "row", axis=0, tiled=True),
        lax.all_gather(w_up, "row", axis=0, tiled=True),
        lax.all_gather(w_down, "row", axis=1, tiled=True),
    )
    hid_width = gate_full.shape[1]
    joint = jnp.concatenate([gate_full, up_full], axis=1)
    ffn_rows = lax.all_gather(normed_ffn, "seq", axis=0, tiled=True)
    gate_up = project(ffn_rows, joint)
    gate_vals = gate_up[:, :hid_width]
    up_vals = gate_up[:, hid_width:]
    hidden = (jax.nn.silu(gate_vals) * up_vals).astype(jnp.bfloat16)
    ffn_out = lax.psum_scatter(
        project(hidden, down_full).astype(jnp.bfloat16), "seq", scatter_dimension=0, tiled=True
    ).astype(jnp.float32)
    outputs = middle + ffn_out
    cot_flat = cotangent.reshape(blk, width)
    cot_low = cot_flat.astype(jnp.bfloat16)
    cot_rows = lax.all_gather(cot_low, "seq", axis=0, tiled=True)
    grad_hidden = contract_cols(cot_rows, down_full)
    grad_down_part = contract_rows(hidden, cot_rows)
    sigmoid_gate = jax.nn.sigmoid(gate_vals)
    grad_gate_vals = grad_hidden * up_vals * sigmoid_gate * (1.0 + gate_vals * (1.0 - sigmoid_gate))
    grad_up_vals = grad_hidden * gate_vals * sigmoid_gate
    grad_joint = jnp.concatenate([grad_gate_vals, grad_up_vals], axis=1).astype(jnp.bfloat16)
    grad_joint_w = contract_rows(ffn_rows, grad_joint)
    grad_normed_ffn = lax.psum_scatter(
        contract_cols(grad_joint, joint).astype(jnp.bfloat16),
        "seq",
        scatter_dimension=0,
        tiled=True,
    ).astype(jnp.float32)
    grad_w_gate, grad_w_up, grad_w_down = (
        lax.psum_scatter(
            grad_joint_w[:, :hid_width].astype(jnp.bfloat16), "row", scatter_dimension=0, tiled=True
        ).astype(jnp.float32),
        lax.psum_scatter(
            grad_joint_w[:, hid_width:].astype(jnp.bfloat16), "row", scatter_dimension=0, tiled=True
        ).astype(jnp.float32),
        lax.psum_scatter(
            grad_down_part.astype(jnp.bfloat16), "row", scatter_dimension=1, tiled=True
        ).astype(jnp.float32),
    )
    gain_ffn_part = jnp.sum(grad_normed_ffn * middle * scale_two, axis=0)
    scaled_two = grad_normed_ffn * gain_ffn
    grad_middle = (
        cot_flat
        + scale_two * scaled_two
        - middle * scale_two**3 * jnp.mean(scaled_two * middle, axis=-1, keepdims=True)
    )
    grad_attn = grad_middle.astype(jnp.bfloat16)
    grad_attn_all = lax.all_gather(grad_attn, "seq", axis=0, tiled=True)
    grad_attn_tail = jnp.pad(grad_attn_all, ((0, TQ * extra), (0, 0)))
    grad_heads_x = contract_cols(
        lax.dynamic_slice_in_dim(grad_attn_tail, q0, nb_all * TQ, 0), wo_g
    ).astype(jnp.bfloat16)
    gh_blocks = jnp.transpose(grad_heads_x.reshape(nb_all, TQ, 2, HD), (0, 2, 1, 3))
    grad_out_part = contract_rows(heads_own, lax.dynamic_slice_in_dim(grad_attn_all, q0, span, 0))
    gq_blk, gk_heads, gv_heads, tap_acc, mix_acc = attention_backward(
        toff, taps_flat, mix_flat, q_blocks, q_own, k_heads, v_heads, row_docs, key_docs,
        probs_blk, gh_blocks, nw, length, nb,
    )
    grad_q_own = jnp.transpose(gq_blk[:nb], (0, 2, 1, 3)).reshape(span, pw)
    grad_k_part = jnp.transpose(gk_heads, (1, 0, 2)).reshape(length, pw)
    grad_v_part = jnp.transpose(gv_heads, (1, 0, 2)).reshape(length, pw)
    grad_taps_part = jnp.sum(tap_acc, axis=(1, 2)).reshape(2, QCONV, KCONV)
    grad_mix_part = jnp.sum(mix_acc, axis=1).reshape(2, 2)

    def split_sum(values):
        if splits == 1:
            return values
        total = values
        for step in range(1, splits):
            route = []
            for s in range(seq_count):
                base = (s // splits) * splits
                route.append((s, base + (s - base + step) % splits))
            total = total + lax.ppermute(values, "seq", route)
        return total

    grad_k_low = split_sum(grad_k_part).astype(jnp.bfloat16)
    grad_v_low = split_sum(grad_v_part).astype(jnp.bfloat16)
    grad_k_own = lax.dynamic_slice_in_dim(grad_k_low, q0, span, 0)
    grad_v_own = lax.dynamic_slice_in_dim(grad_v_low, q0, span, 0)

    normed_own = lax.dynamic_slice_in_dim(normed_all, q0, span, 0)
    rows_per_dev = width // (row_count * seq_count)

    def finish_in(partial):
        red = lax.psum_scatter(partial, "row", scatter_dimension=0, tiled=True)
        got = lax.all_to_all(red, "seq", 0, 0, tiled=True)
        got = got.reshape(groups, splits, rows_per_dev, pw).sum(axis=1)
        return jnp.transpose(got, (1, 0, 2)).reshape(rows_per_dev, width)

    grad_w_query = finish_in(contract_rows(normed_own, grad_q_own))
    grad_w_key = finish_in(contract_rows(normed_own, grad_k_own))
    grad_w_value = finish_in(contract_rows(normed_own, grad_v_own))

    red_out = lax.psum_scatter(grad_out_part, "row", scatter_dimension=0, tiled=True)
    red_out = red_out.reshape(splits, rows_per_dev, width)
    grad_w_out = jnp.zeros((rows_per_dev, width), jnp.float32)
    for src_part in range(splits):
        for j in range(splits):
            route = []
            for r in range(row_count):
                for g in range(groups):
                    src = r * seq_count + g * splits + src_part
                    dst = g * row_count * splits + r * splits + j
                    route.append((src, dst))
            grad_w_out = grad_w_out + lax.ppermute(red_out[j], ("row", "seq"), route)

    grad_tok = to_tokens(jnp.concatenate([grad_q_own, grad_k_own, grad_v_own], axis=1))
    grad_tok = grad_tok.reshape(groups, blk, 3, pw)
    gq_tok = jnp.transpose(grad_tok[:, :, 0], (1, 0, 2)).reshape(blk, width)
    gk_tok = jnp.transpose(grad_tok[:, :, 1], (1, 0, 2)).reshape(blk, width)
    gv_tok = jnp.transpose(grad_tok[:, :, 2], (1, 0, 2)).reshape(blk, width)
    grad_normed = (
        contract_cols(gq_tok, w_query) + contract_cols(gk_tok, w_key) + contract_cols(gv_tok, w_value)
    )
    gain_attn_part = jnp.sum(grad_normed * flat_in * scale_one, axis=0)
    scaled_one = grad_normed * gain_attn
    grad_inputs = (
        grad_middle
        + scale_one * scaled_one
        - flat_in * scale_one**3 * jnp.mean(scaled_one * flat_in, axis=-1, keepdims=True)
    )
    grad_gain_attn, grad_gain_ffn = (
        lax.psum_scatter(gain_attn_part, ("row", "seq"), scatter_dimension=0, tiled=True),
        lax.psum_scatter(gain_ffn_part, ("row", "seq"), scatter_dimension=0, tiled=True),
    )
    taps_full = lax.dynamic_update_slice_in_dim(
        jnp.zeros((HEADS, QCONV, KCONV), jnp.float32), grad_taps_part, pair * 2, 0
    )
    mix_full = lax.dynamic_update_slice_in_dim(
        jnp.zeros((groups, 2, 2), jnp.float32), grad_mix_part[None], pair, 0
    )
    grad_taps, grad_mix = lax.psum((taps_full, mix_full), ("row", "seq"))
    return (
        outputs.reshape(row_dev, blk, width),
        grad_inputs.reshape(row_dev, blk, width),
        grad_w_query,
        grad_w_key,
        grad_w_value,
        grad_w_out,
        grad_gain_attn,
        grad_gain_ffn,
        grad_taps,
        grad_mix,
        grad_w_gate,
        grad_w_up,
        grad_w_down,
    )


def solution(mesh):
    return jax.shard_map(
        shards,
        mesh=mesh,
        in_specs=(
            P("row", "seq", None),
            P("row", None),
            P(),
            P(),
            P(),
            P(),
            P(),
            P(),
            P(),
            P(),
            P("row", "seq"),
            P("row", "seq"),
            P("seq", "row"),
            P("row", "seq", None),
        ),
        out_specs=(
            P("row", "seq", None),
            P("row", "seq", None),
            P(("row", "seq"), None),
            P(("row", "seq"), None),
            P(("row", "seq"), None),
            P(("row", "seq"), None),
            P(("row", "seq")),
            P(("row", "seq")),
            P(),
            P(),
            P("row", "seq"),
            P("row", "seq"),
            P("seq", "row"),
        ),
        check_vma=False,
    )
```

```python
import jax
import jax.numpy as jnp
from jax import lax
from jax.sharding import PartitionSpec as P
from jax.experimental import pallas as pl
from jax.experimental.pallas import tpu as pltpu

HEADS = 16
HD = 96
QCONV = 6
KCONV = 11
PAD = 8
TQ = 128
EXT = TQ + PAD
SCALE = HD ** (-0.5)
TAPS = QCONV * KCONV

epsilon = 1e-06


def rms_scale(values):
    return lax.rsqrt(jnp.mean(values * values, axis=-1, keepdims=True) + epsilon)


def project(values, weight):
    return jnp.dot(values, weight, preferred_element_type=jnp.float32)


def contract_rows(left, right):
    return lax.dot_general(
        left, right, (((0,), (0,)), ((), ())), preferred_element_type=jnp.float32
    )


def contract_cols(left, right):
    return lax.dot_general(
        left, right, (((1,), (1,)), ((), ())), preferred_element_type=jnp.float32
    )


def normed_pad_tail(values, extra):
    return jnp.pad(values, ((PAD, TQ * extra), (0, 0)))


def window_start(block, nw, length):
    return pl.multiple_of(jnp.clip((block - nw + 1) * TQ, 0, length - nw * TQ), TQ)


def tap_accumulate(sh_ref, acc_ref, taps_ref, head, width):
    cw = 256 if (width // 128) % 2 == 0 else 128
    ncols = width // cw

    def body(idx, carry):
        r0 = pl.multiple_of((idx // ncols) * 8, 8)
        c0 = pl.multiple_of((idx % ncols) * cw, cw)
        tiles = [sh_ref[b, pl.ds(r0, 8), pl.ds(c0, cw)] for b in range(KCONV)]
        for a in range(QCONV):
            base = head * TAPS + a * KCONV
            total = taps_ref[base] * tiles[0]
            for b in range(1, KCONV):
                total = total + taps_ref[base + b] * tiles[b]
            acc_ref[a, pl.ds(r0, 8), pl.ds(c0, cw)] = total
        return carry

    lax.fori_loop(0, (EXT // 8) * ncols, body, 0)


def tap_products(sh_ref, g_ref, width):
    ncols = width // 128
    sums = {}
    for a0 in range(0, QCONV, 2):

        def body(idx, accs):
            r0 = pl.multiple_of((idx // ncols) * 8, 8)
            c0 = pl.multiple_of((idx % ncols) * 128, 128)
            ga = [g_ref[a0 + k, pl.ds(r0, 8), pl.ds(c0, 128)] for k in range(2)]
            out = list(accs)
            for b in range(KCONV):
                tile = sh_ref[b, pl.ds(r0, 8), pl.ds(c0, 128)]
                for k in range(2):
                    out[k * KCONV + b] = out[k * KCONV + b] + ga[k] * tile
            return tuple(out)

        start = tuple(jnp.zeros((8, 128), jnp.float32) for _ in range(2 * KCONV))
        res = lax.fori_loop(0, (EXT // 8) * ncols, body, start)
        for k in range(2):
            for b in range(KCONV):
                sums[(a0 + k, b)] = res[k * KCONV + b]
    return sums


def masks(block, kstart, width, rdoc_ref, kdoc_ref):
    keydoc = kdoc_ref[:, pl.ds(kstart, width)]
    ext_pos = block * TQ - PAD + lax.broadcasted_iota(jnp.int32, (EXT, width), 0)
    key_ext = kstart + lax.broadcasted_iota(jnp.int32, (EXT, width), 1)
    allowed_ext = (key_ext <= ext_pos) & (rdoc_ref[0] == keydoc)
    own_pos = block * TQ + lax.broadcasted_iota(jnp.int32, (TQ, width), 0)
    key_own = kstart + lax.broadcasted_iota(jnp.int32, (TQ, width), 1)
    allowed_own = (key_own <= own_pos) & (rdoc_ref[0, PAD:, :] == keydoc)
    return allowed_ext, allowed_own


def masked_shifts(q_ref, k_ref, head, kstart, width, allowed_ext, sh_ref):
    keys = k_ref[head, pl.ds(kstart, width), :]
    scores = lax.dot_general(
        q_ref[0, head], keys, (((1,), (1,)), ((), ())), preferred_element_type=jnp.float32
    ) * SCALE
    masked = jnp.where(allowed_ext, scores, 0.0)
    col = lax.broadcasted_iota(jnp.int32, (EXT, width), 1)
    sh_ref[0] = masked
    for b in range(1, KCONV):
        sh_ref[b] = jnp.where(col >= b, pltpu.roll(masked, b, 1), 0.0)


def fwd_kernel(toff_ref, taps_ref, mix_ref, q_ref, k_ref, v_ref, rdoc_ref, kdoc_ref,
               heads_ref, probs_ref, sh_ref, acc_ref, *, nw, length):
    width = nw * TQ
    block = toff_ref[0] + pl.program_id(0)
    kstart = window_start(block, nw, length)
    allowed_ext, allowed_own = masks(block, kstart, width, rdoc_ref, kdoc_ref)
    for head in range(2):
        masked_shifts(q_ref, k_ref, head, kstart, width, allowed_ext, sh_ref)
        tap_accumulate(sh_ref, acc_ref, taps_ref, head, width)
        conv = acc_ref[0]
        for a in range(1, QCONV):
            conv = conv + pltpu.roll(acc_ref[a], a, 0)
        logits = jnp.where(allowed_own, conv[PAD:], -jnp.inf)
        highest = jnp.max(logits, axis=1, keepdims=True)
        highest = jnp.where(highest > -jnp.inf, highest, 0.0)
        expd = jnp.exp(logits - highest)
        denom = jnp.sum(expd, axis=1, keepdims=True)
        probs_ref[0, head] = expd / jnp.where(denom > 0.0, denom, 1.0)
    p0 = probs_ref[0, 0]
    p1 = probs_ref[0, 1]
    for c in range(2):
        mixed = (mix_ref[2 * c] * p0 + mix_ref[2 * c + 1] * p1).astype(jnp.bfloat16)
        heads_ref[0, c] = jnp.dot(
            mixed, v_ref[c, pl.ds(kstart, width), :], preferred_element_type=jnp.float32
        ).astype(jnp.bfloat16)


def attention_forward(toff, taps_flat, mix_flat, q_blocks, k_heads, v_heads, row_docs, key_docs, nw, length):
    nb_all = q_blocks.shape[0]
    width = nw * TQ
    smem = pl.BlockSpec(memory_space=pltpu.SMEM)
    flops = nb_all * 2 * (4 * EXT * width * HD + 2 * TAPS * EXT * width)
    return pl.pallas_call(
        lambda *refs: fwd_kernel(*refs, nw=nw, length=length),
        grid=(nb_all,),
        in_specs=[
            smem,
            smem,
            smem,
            pl.BlockSpec((1, 2, EXT, HD), lambda t: (t, 0, 0, 0)),
            pl.BlockSpec((2, length, HD), lambda t: (0, 0, 0)),
            pl.BlockSpec((2, length, HD), lambda t: (0, 0, 0)),
            pl.BlockSpec((1, EXT, 1), lambda t: (t, 0, 0)),
            pl.BlockSpec((1, length), lambda t: (0, 0)),
        ],
        out_specs=[
            pl.BlockSpec((1, 2, TQ, HD), lambda t: (t, 0, 0, 0)),
            pl.BlockSpec((1, 2, TQ, width), lambda t: (t, 0, 0, 0)),
        ],
        out_shape=[
            jax.ShapeDtypeStruct((nb_all, 2, TQ, HD), jnp.bfloat16),
            jax.ShapeDtypeStruct((nb_all, 2, TQ, width), jnp.float32),
        ],
        scratch_shapes=[
            pltpu.VMEM((KCONV, EXT, width), jnp.float32),
            pltpu.VMEM((QCONV, EXT, width), jnp.float32),
        ],
        compiler_params=pltpu.CompilerParams(
            dimension_semantics=("arbitrary",), vmem_limit_bytes=56 * 1024 * 1024
        ),
        cost_estimate=pl.CostEstimate(
            flops=flops, transcendentals=nb_all * 2 * TQ * width,
            bytes_accessed=nb_all * 2 * TQ * width * 4 + 4 * length * HD * 2,
        ),
    )(toff, taps_flat, mix_flat, q_blocks, k_heads, v_heads, row_docs, key_docs)


def bwd_kernel(toff_ref, taps_ref, mix_ref, q_ref, qo_ref, k_ref, v_ref, rdoc_ref, kdoc_ref,
               probs_ref, gh_ref, ght_ref, gq_ref, gk_ref, gv_ref, tacc_ref, macc_ref,
               carry_ref, sh_ref, acc_ref, g_ref, gx_ref, *, nw, length, nb, nb_all):
    width = nw * TQ
    step = pl.program_id(0)
    local = nb_all - 1 - step
    block = toff_ref[0] + local
    kstart = window_start(block, nw, length)

    @pl.when(step == 0)
    def _init():
        gk_ref[...] = jnp.zeros(gk_ref.shape, jnp.float32)
        gv_ref[...] = jnp.zeros(gv_ref.shape, jnp.float32)
        tacc_ref[...] = jnp.zeros(tacc_ref.shape, jnp.float32)
        macc_ref[...] = jnp.zeros(macc_ref.shape, jnp.float32)
        carry_ref[...] = jnp.zeros(carry_ref.shape, jnp.float32)

    allowed_ext, allowed_own = masks(block, kstart, width, rdoc_ref, kdoc_ref)
    gm = [
        lax.dot_general(
            gh_ref[0, c], v_ref[c, pl.ds(kstart, width), :], (((1,), (1,)), ((), ())),
            preferred_element_type=jnp.float32,
        )
        for c in range(2)
    ]
    probs = [probs_ref[0, 0], probs_ref[0, 1]]
    gc = []
    for e in range(2):
        gp = mix_ref[e] * gm[0] + mix_ref[2 + e] * gm[1]
        inner = jnp.sum(gp * probs[e], axis=1, keepdims=True)
        gc.append(probs[e] * (gp - inner))

    def own_sums():
        for c in range(2):
            for e in range(2):
                macc_ref[pl.ds(2 * c + e, 1), :] += jnp.sum(gm[c] * probs[e], axis=0, keepdims=True)
            mixed = (mix_ref[2 * c] * probs[0] + mix_ref[2 * c + 1] * probs[1]).astype(jnp.bfloat16)
            gv_ref[c, :, pl.ds(kstart, width)] += jnp.dot(
                ght_ref[0, c], mixed, preferred_element_type=jnp.float32
            )

    def head_taps(e):
        masked_shifts(q_ref, k_ref, e, kstart, width, allowed_ext, sh_ref)
        gcp = jnp.concatenate([jnp.zeros((PAD, width), jnp.float32), gc[e]], axis=0)
        g_ref[0] = gcp
        for a in range(1, QCONV):
            g_ref[a] = pltpu.roll(gcp, EXT - a, 0)
        sums = tap_products(sh_ref, g_ref, width)
        for b in range(KCONV):
            for a in range(QCONV):
                tacc_ref[e * TAPS + a * KCONV + b] += sums[(a, b)]

    def head_keys(e, gs):
        gk_ref[e, :, pl.ds(kstart, width)] += jnp.dot(
            qo_ref[0, e], gs, preferred_element_type=jnp.float32
        ) * SCALE

    nxt = [carry_ref[e, :, pl.ds(kstart, width + TQ)] for e in range(2)]
    if nb < nb_all:
        pl.when(local < nb)(own_sums)
    else:
        own_sums()
    for e in range(2):
        if nb < nb_all:
            pl.when(local < nb)(lambda: head_taps(e))
        else:
            head_taps(e)
        gx_ref[pl.ds(0, TQ), pl.ds(0, width)] = gc[e]
        gx_ref[pl.ds(0, TQ), pl.ds(width, TQ)] = jnp.zeros((TQ, TQ), jnp.float32)
        gx_ref[pl.ds(TQ, PAD), :] = nxt[e]
        gxv = gx_ref[...]
        sh_ref[0] = gxv[:, :width]
        for b in range(1, KCONV):
            sh_ref[b] = pltpu.roll(gxv, width + TQ - b, 1)[:, :width]
        tap_accumulate(sh_ref, acc_ref, taps_ref, e, width)
        gmk = acc_ref[0]
        for a in range(1, QCONV):
            gmk = gmk + pltpu.roll(acc_ref[a], EXT - a, 0)
        gs = jnp.where(allowed_own, gmk[:TQ], 0.0).astype(jnp.bfloat16)
        gq_ref[0, e] = (
            jnp.dot(gs, k_ref[e, pl.ds(kstart, width), :], preferred_element_type=jnp.float32) * SCALE
        ).astype(jnp.bfloat16)
        if nb < nb_all:
            pl.when(local < nb)(lambda: head_keys(e, gs))
        else:
            head_keys(e, gs)
    carry_ref[...] = jnp.zeros(carry_ref.shape, jnp.float32)
    for e in range(2):
        carry_ref[e, :, pl.ds(kstart, width)] = gc[e][:PAD]


def attention_backward(toff, taps_flat, mix_flat, q_blocks, q_own, k_heads, v_heads, row_docs, key_docs,
                       probs_blk, gh_blocks, nw, length, nb):
    q_own = jnp.swapaxes(q_own, 2, 3)
    gh_t = jnp.swapaxes(gh_blocks, 2, 3)
    nb_all = q_blocks.shape[0]
    width = nw * TQ
    smem = pl.BlockSpec(memory_space=pltpu.SMEM)
    rev = lambda s: nb_all - 1 - s
    flops = nb_all * 2 * (8 * TQ * width * HD + 6 * TAPS * EXT * width)
    return pl.pallas_call(
        lambda *refs: bwd_kernel(*refs, nw=nw, length=length, nb=nb, nb_all=nb_all),
        grid=(nb_all,),
        in_specs=[
            smem,
            smem,
            smem,
            pl.BlockSpec((1, 2, EXT, HD), lambda s: (rev(s), 0, 0, 0)),
            pl.BlockSpec((1, 2, HD, TQ), lambda s: (rev(s), 0, 0, 0)),
            pl.BlockSpec((2, length, HD), lambda s: (0, 0, 0)),
            pl.BlockSpec((2, length, HD), lambda s: (0, 0, 0)),
            pl.BlockSpec((1, EXT, 1), lambda s: (rev(s), 0, 0)),
            pl.BlockSpec((1, length), lambda s: (0, 0)),
            pl.BlockSpec((1, 2, TQ, width), lambda s: (rev(s), 0, 0, 0)),
            pl.BlockSpec((1, 2, TQ, HD), lambda s: (rev(s), 0, 0, 0)),
            pl.BlockSpec((1, 2, HD, TQ), lambda s: (rev(s), 0, 0, 0)),
        ],
        out_specs=[
            pl.BlockSpec((1, 2, TQ, HD), lambda s: (rev(s), 0, 0, 0)),
            pl.BlockSpec((2, HD, length), lambda s: (0, 0, 0)),
            pl.BlockSpec((2, HD, length), lambda s: (0, 0, 0)),
            pl.BlockSpec((2 * TAPS, 8, 128), lambda s: (0, 0, 0)),
            pl.BlockSpec((4, width), lambda s: (0, 0)),
        ],
        out_shape=[
            jax.ShapeDtypeStruct((nb_all, 2, TQ, HD), jnp.bfloat16),
            jax.ShapeDtypeStruct((2, HD, length), jnp.float32),
            jax.ShapeDtypeStruct((2, HD, length), jnp.float32),
            jax.ShapeDtypeStruct((2 * TAPS, 8, 128), jnp.float32),
            jax.ShapeDtypeStruct((4, width), jnp.float32),
        ],
        scratch_shapes=[
            pltpu.VMEM((2, PAD, length + TQ), jnp.float32),
            pltpu.VMEM((KCONV, EXT, width), jnp.float32),
            pltpu.VMEM((QCONV, EXT, width), jnp.float32),
            pltpu.VMEM((QCONV, EXT, width), jnp.float32),
            pltpu.VMEM((EXT, width + TQ), jnp.float32),
        ],
        compiler_params=pltpu.CompilerParams(
            dimension_semantics=("arbitrary",), vmem_limit_bytes=60 * 1024 * 1024
        ),
        cost_estimate=pl.CostEstimate(
            flops=flops, transcendentals=0,
            bytes_accessed=nb_all * 2 * TQ * width * 4 + 8 * length * HD * 4,
        ),
    )(toff, taps_flat, mix_flat, q_blocks, q_own, k_heads, v_heads, row_docs, key_docs, probs_blk, gh_blocks, gh_t)


def shards(
    inputs,
    doc_ids,
    w_query,
    w_key,
    w_value,
    w_out,
    gain_attn,
    gain_ffn,
    conv_taps,
    head_mix,
    w_gate,
    w_up,
    w_down,
    cotangent,
):
    row_dev, blk, width = inputs.shape
    assert row_dev == 1
    seq_count = lax.axis_size("seq")
    row_count = lax.axis_size("row")
    seq_index = lax.axis_index("seq")
    row_index = lax.axis_index("row")
    length = blk * seq_count
    groups = HEADS // 2
    assert seq_count % groups == 0
    splits = seq_count // groups
    span = length // splits
    pw = 2 * HD
    pair = seq_index // splits
    part = seq_index % splits
    q0 = part * span

    flat_in = inputs.reshape(blk, width)
    scale_one = rms_scale(flat_in)
    normed = (flat_in * scale_one * gain_attn).astype(jnp.bfloat16)
    normed_all = lax.all_gather(normed, "seq", axis=0, tiled=True)

    wq_g = lax.dynamic_slice_in_dim(w_query, pair * pw, pw, 1)
    wk_g = lax.dynamic_slice_in_dim(w_key, pair * pw, pw, 1)
    wv_g = lax.dynamic_slice_in_dim(w_value, pair * pw, pw, 1)
    wo_g = lax.dynamic_slice_in_dim(w_out, pair * pw, pw, 0)
    taps = lax.dynamic_slice_in_dim(conv_taps, pair * 2, 2, 0)
    mixing = lax.dynamic_index_in_dim(head_mix, pair, 0, keepdims=False)

    k_all = project(normed_all, wk_g).astype(jnp.bfloat16)
    v_all = project(normed_all, wv_g).astype(jnp.bfloat16)
    k3 = k_all.reshape(length, 2, HD)
    v3 = v_all.reshape(length, 2, HD)

    docs = doc_ids[0]
    nb = span // TQ
    extra = 1 if splits > 1 else 0
    nb_all = nb + extra
    doc_cap = length // 2
    nw = min(length // TQ, (doc_cap + QCONV - 2 + TQ - 1) // TQ + 1)
    q_tail = normed_pad_tail(normed_all, extra)
    q_rows = project(lax.dynamic_slice_in_dim(q_tail, q0, nb_all * TQ + PAD, 0), wq_g).astype(jnp.bfloat16)
    q_blocks = jnp.stack([q_rows[t * TQ : t * TQ + EXT] for t in range(nb_all)])
    q_blocks = jnp.transpose(q_blocks.reshape(nb_all, EXT, 2, HD), (0, 2, 1, 3))
    q_own = q_blocks[:, :, PAD:]
    k_heads = jnp.transpose(k3, (1, 0, 2))
    v_heads = jnp.transpose(v3, (1, 0, 2))
    docs_tail = jnp.pad(docs, (PAD, TQ * extra), constant_values=-1)
    doc_rows = lax.dynamic_slice_in_dim(docs_tail, q0, nb_all * TQ + PAD, 0)
    row_docs = jnp.stack([doc_rows[t * TQ : t * TQ + EXT] for t in range(nb_all)])[:, :, None]
    key_docs = docs[None, :]
    toff = (q0 // TQ).astype(jnp.int32).reshape(1)
    taps_flat = taps.reshape(2 * QCONV * KCONV)
    mix_flat = mixing.reshape(4)
    heads_blk, probs_blk = attention_forward(
        toff, taps_flat, mix_flat, q_blocks, k_heads, v_heads, row_docs, key_docs, nw, length
    )
    heads_own = jnp.transpose(heads_blk[:nb], (0, 2, 1, 3)).reshape(span, pw)

    def to_tokens(values):
        cols = values.shape[1]
        if splits == 1:
            full = values
        else:
            full = lax.dynamic_update_slice_in_dim(
                jnp.zeros((length, cols), values.dtype), values, q0, 0
            )
        got = lax.all_to_all(full, "seq", 0, 0, tiled=True)
        got = got.reshape(groups, splits, blk, cols)
        if splits > 1:
            got = jnp.sum(got.astype(jnp.float32), axis=1).astype(values.dtype)
        else:
            got = got[:, 0]
        return got

    heads_tok = jnp.transpose(to_tokens(heads_own), (1, 0, 2)).reshape(blk, width)
    middle = flat_in + project(heads_tok, w_out)
    scale_two = rms_scale(middle)
    normed_ffn = (middle * scale_two * gain_ffn).astype(jnp.bfloat16)
    gate_full, up_full, down_full = (
        lax.all_gather(w_gate, "row", axis=0, tiled=True),
        lax.all_gather(w_up, "row", axis=0, tiled=True),
        lax.all_gather(w_down, "row", axis=1, tiled=True),
    )
    hid_width = gate_full.shape[1]
    joint = jnp.concatenate([gate_full, up_full], axis=1)
    ffn_rows = lax.all_gather(normed_ffn, "seq", axis=0, tiled=True)
    gate_up = project(ffn_rows, joint)
    gate_vals = gate_up[:, :hid_width]
    up_vals = gate_up[:, hid_width:]
    hidden = (jax.nn.silu(gate_vals) * up_vals).astype(jnp.bfloat16)
    ffn_out = lax.psum_scatter(
        project(hidden, down_full).astype(jnp.bfloat16), "seq", scatter_dimension=0, tiled=True
    ).astype(jnp.float32)
    outputs = middle + ffn_out
    cot_flat = cotangent.reshape(blk, width)
    cot_low = cot_flat.astype(jnp.bfloat16)
    cot_rows = lax.all_gather(cot_low, "seq", axis=0, tiled=True)
    grad_hidden = contract_cols(cot_rows, down_full)
    grad_down_part = contract_rows(hidden, cot_rows)
    sigmoid_gate = jax.nn.sigmoid(gate_vals)
    grad_gate_vals = grad_hidden * up_vals * sigmoid_gate * (1.0 + gate_vals * (1.0 - sigmoid_gate))
    grad_up_vals = grad_hidden * gate_vals * sigmoid_gate
    grad_joint = jnp.concatenate([grad_gate_vals, grad_up_vals], axis=1).astype(jnp.bfloat16)
    grad_joint_w = contract_rows(ffn_rows, grad_joint)
    grad_normed_ffn = lax.psum_scatter(
        contract_cols(grad_joint, joint).astype(jnp.bfloat16),
        "seq",
        scatter_dimension=0,
        tiled=True,
    ).astype(jnp.float32)
    grad_w_gate, grad_w_up, grad_w_down = (
        lax.psum_scatter(
            grad_joint_w[:, :hid_width].astype(jnp.bfloat16), "row", scatter_dimension=0, tiled=True
        ).astype(jnp.float32),
        lax.psum_scatter(
            grad_joint_w[:, hid_width:].astype(jnp.bfloat16), "row", scatter_dimension=0, tiled=True
        ).astype(jnp.float32),
        lax.psum_scatter(
            grad_down_part.astype(jnp.bfloat16), "row", scatter_dimension=1, tiled=True
        ).astype(jnp.float32),
    )
    gain_ffn_part = jnp.sum(grad_normed_ffn * middle * scale_two, axis=0)
    scaled_two = grad_normed_ffn * gain_ffn
    grad_middle = (
        cot_flat
        + scale_two * scaled_two
        - middle * scale_two**3 * jnp.mean(scaled_two * middle, axis=-1, keepdims=True)
    )
    grad_attn = grad_middle.astype(jnp.bfloat16)
    grad_attn_all = lax.all_gather(grad_attn, "seq", axis=0, tiled=True)
    grad_attn_tail = jnp.pad(grad_attn_all, ((0, TQ * extra), (0, 0)))
    grad_heads_x = contract_cols(
        lax.dynamic_slice_in_dim(grad_attn_tail, q0, nb_all * TQ, 0), wo_g
    ).astype(jnp.bfloat16)
    gh_blocks = jnp.transpose(grad_heads_x.reshape(nb_all, TQ, 2, HD), (0, 2, 1, 3))
    grad_out_part = contract_rows(heads_own, lax.dynamic_slice_in_dim(grad_attn_all, q0, span, 0))
    gq_blk, gk_heads, gv_heads, tap_acc, mix_acc = attention_backward(
        toff, taps_flat, mix_flat, q_blocks, q_own, k_heads, v_heads, row_docs, key_docs,
        probs_blk, gh_blocks, nw, length, nb,
    )
    grad_q_own = jnp.transpose(gq_blk[:nb], (0, 2, 1, 3)).reshape(span, pw)
    grad_k_part = jnp.transpose(gk_heads, (2, 0, 1)).reshape(length, pw)
    grad_v_part = jnp.transpose(gv_heads, (2, 0, 1)).reshape(length, pw)
    grad_taps_part = jnp.sum(tap_acc, axis=(1, 2)).reshape(2, QCONV, KCONV)
    grad_mix_part = jnp.sum(mix_acc, axis=1).reshape(2, 2)

    def split_sum(values):
        if splits == 1:
            return values
        total = values
        for step in range(1, splits):
            route = []
            for s in range(seq_count):
                base = (s // splits) * splits
                route.append((s, base + (s - base + step) % splits))
            total = total + lax.ppermute(values, "seq", route)
        return total

    grad_k_low = split_sum(grad_k_part).astype(jnp.bfloat16)
    grad_v_low = split_sum(grad_v_part).astype(jnp.bfloat16)
    grad_k_own = lax.dynamic_slice_in_dim(grad_k_low, q0, span, 0)
    grad_v_own = lax.dynamic_slice_in_dim(grad_v_low, q0, span, 0)

    normed_own = lax.dynamic_slice_in_dim(normed_all, q0, span, 0)
    rows_per_dev = width // (row_count * seq_count)

    def finish_in(partial):
        red = lax.psum_scatter(partial, "row", scatter_dimension=0, tiled=True)
        got = lax.all_to_all(red, "seq", 0, 0, tiled=True)
        got = got.reshape(groups, splits, rows_per_dev, pw).sum(axis=1)
        return jnp.transpose(got, (1, 0, 2)).reshape(rows_per_dev, width)

    grad_w_query = finish_in(contract_rows(normed_own, grad_q_own))
    grad_w_key = finish_in(contract_rows(normed_own, grad_k_own))
    grad_w_value = finish_in(contract_rows(normed_own, grad_v_own))

    red_out = lax.psum_scatter(grad_out_part, "row", scatter_dimension=0, tiled=True)
    red_out = red_out.reshape(splits, rows_per_dev, width)
    grad_w_out = jnp.zeros((rows_per_dev, width), jnp.float32)
    for src_part in range(splits):
        for j in range(splits):
            route = []
            for r in range(row_count):
                for g in range(groups):
                    src = r * seq_count + g * splits + src_part
                    dst = g * row_count * splits + r * splits + j
                    route.append((src, dst))
            grad_w_out = grad_w_out + lax.ppermute(red_out[j], ("row", "seq"), route)

    grad_tok = to_tokens(jnp.concatenate([grad_q_own, grad_k_own, grad_v_own], axis=1))
    grad_tok = grad_tok.reshape(groups, blk, 3, pw)
    gq_tok = jnp.transpose(grad_tok[:, :, 0], (1, 0, 2)).reshape(blk, width)
    gk_tok = jnp.transpose(grad_tok[:, :, 1], (1, 0, 2)).reshape(blk, width)
    gv_tok = jnp.transpose(grad_tok[:, :, 2], (1, 0, 2)).reshape(blk, width)
    grad_normed = (
        contract_cols(gq_tok, w_query) + contract_cols(gk_tok, w_key) + contract_cols(gv_tok, w_value)
    )
    gain_attn_part = jnp.sum(grad_normed * flat_in * scale_one, axis=0)
    scaled_one = grad_normed * gain_attn
    grad_inputs = (
        grad_middle
        + scale_one * scaled_one
        - flat_in * scale_one**3 * jnp.mean(scaled_one * flat_in, axis=-1, keepdims=True)
    )
    grad_gain_attn, grad_gain_ffn = (
        lax.psum_scatter(gain_attn_part, ("row", "seq"), scatter_dimension=0, tiled=True),
        lax.psum_scatter(gain_ffn_part, ("row", "seq"), scatter_dimension=0, tiled=True),
    )
    taps_full = lax.dynamic_update_slice_in_dim(
        jnp.zeros((HEADS, QCONV, KCONV), jnp.float32), grad_taps_part, pair * 2, 0
    )
    mix_full = lax.dynamic_update_slice_in_dim(
        jnp.zeros((groups, 2, 2), jnp.float32), grad_mix_part[None], pair, 0
    )
    grad_taps, grad_mix = lax.psum((taps_full, mix_full), ("row", "seq"))
    return (
        outputs.reshape(row_dev, blk, width),
        grad_inputs.reshape(row_dev, blk, width),
        grad_w_query,
        grad_w_key,
        grad_w_value,
        grad_w_out,
        grad_gain_attn,
        grad_gain_ffn,
        grad_taps,
        grad_mix,
        grad_w_gate,
        grad_w_up,
        grad_w_down,
    )


def solution(mesh):
    return jax.shard_map(
        shards,
        mesh=mesh,
        in_specs=(
            P("row", "seq", None),
            P("row", None),
            P(),
            P(),
            P(),
            P(),
            P(),
            P(),
            P(),
            P(),
            P("row", "seq"),
            P("row", "seq"),
            P("seq", "row"),
            P("row", "seq", None),
        ),
        out_specs=(
            P("row", "seq", None),
            P("row", "seq", None),
            P(("row", "seq"), None),
            P(("row", "seq"), None),
            P(("row", "seq"), None),
            P(("row", "seq"), None),
            P(("row", "seq")),
            P(("row", "seq")),
            P(),
            P(),
            P("row", "seq"),
            P("row", "seq"),
            P("seq", "row"),
        ),
        check_vma=False,
    )
```

```python
import jax
import jax.numpy as jnp
from jax import lax
from jax.sharding import PartitionSpec as P
from jax.experimental import pallas as pl
from jax.experimental.pallas import tpu as pltpu

HEADS = 16
HD = 96
QCONV = 6
KCONV = 11
PAD = 8
TQ = 128
EXT = TQ + PAD
SCALE = HD ** (-0.5)
TAPS = QCONV * KCONV

epsilon = 1e-06


def rms_scale(values):
    return lax.rsqrt(jnp.mean(values * values, axis=-1, keepdims=True) + epsilon)


def project(values, weight):
    return jnp.dot(values, weight, preferred_element_type=jnp.float32)


def contract_rows(left, right):
    return lax.dot_general(
        left, right, (((0,), (0,)), ((), ())), preferred_element_type=jnp.float32
    )


def contract_cols(left, right):
    return lax.dot_general(
        left, right, (((1,), (1,)), ((), ())), preferred_element_type=jnp.float32
    )


def normed_pad_tail(values, extra):
    return jnp.pad(values, ((PAD, TQ * extra), (0, 0)))


def window_start(block, nw, length):
    return pl.multiple_of(jnp.clip((block - nw + 1) * TQ, 0, length - nw * TQ), TQ)


def tap_accumulate(sh_ref, acc_ref, taps_ref, head, width):
    cw = 256 if (width // 128) % 2 == 0 else 128
    ncols = width // cw

    def body(idx, carry):
        r0 = pl.multiple_of((idx // ncols) * 8, 8)
        c0 = pl.multiple_of((idx % ncols) * cw, cw)
        tiles = [sh_ref[b, pl.ds(r0, 8), pl.ds(c0, cw)] for b in range(KCONV)]
        for a in range(QCONV):
            base = head * TAPS + a * KCONV
            total = taps_ref[base] * tiles[0]
            for b in range(1, KCONV):
                total = total + taps_ref[base + b] * tiles[b]
            acc_ref[a, pl.ds(r0, 8), pl.ds(c0, cw)] = total
        return carry

    lax.fori_loop(0, (EXT // 8) * ncols, body, 0)


def tap_products(sh_ref, g_ref, width):
    ncols = width // 128
    sums = {}
    for a0 in range(0, QCONV, 2):

        def body(idx, accs):
            r0 = pl.multiple_of((idx // ncols) * 8, 8)
            c0 = pl.multiple_of((idx % ncols) * 128, 128)
            ga = [g_ref[a0 + k, pl.ds(r0, 8), pl.ds(c0, 128)] for k in range(2)]
            out = list(accs)
            for b in range(KCONV):
                tile = sh_ref[b, pl.ds(r0, 8), pl.ds(c0, 128)]
                for k in range(2):
                    out[k * KCONV + b] = out[k * KCONV + b] + ga[k] * tile
            return tuple(out)

        start = tuple(jnp.zeros((8, 128), jnp.float32) for _ in range(2 * KCONV))
        res = lax.fori_loop(0, (EXT // 8) * ncols, body, start)
        for k in range(2):
            for b in range(KCONV):
                sums[(a0 + k, b)] = res[k * KCONV + b]
    return sums


def masks(block, kstart, width, rdoc_ref, kdoc_ref):
    keydoc = kdoc_ref[:, pl.ds(kstart, width)]
    ext_pos = block * TQ - PAD + lax.broadcasted_iota(jnp.int32, (EXT, width), 0)
    key_ext = kstart + lax.broadcasted_iota(jnp.int32, (EXT, width), 1)
    allowed_ext = (key_ext <= ext_pos) & (rdoc_ref[0] == keydoc)
    own_pos = block * TQ + lax.broadcasted_iota(jnp.int32, (TQ, width), 0)
    key_own = kstart + lax.broadcasted_iota(jnp.int32, (TQ, width), 1)
    allowed_own = (key_own <= own_pos) & (rdoc_ref[0, PAD:, :] == keydoc)
    return allowed_ext, allowed_own


def masked_shifts(q_ref, k_ref, head, kstart, width, allowed_ext, sh_ref):
    keys = k_ref[head, pl.ds(kstart, width), :]
    scores = lax.dot_general(
        q_ref[0, head], keys, (((1,), (1,)), ((), ())), preferred_element_type=jnp.float32
    ) * SCALE
    masked = jnp.where(allowed_ext, scores, 0.0)
    col = lax.broadcasted_iota(jnp.int32, (EXT, width), 1)
    sh_ref[0] = masked
    for b in range(1, KCONV):
        sh_ref[b] = jnp.where(col >= b, pltpu.roll(masked, b, 1), 0.0)


def fwd_kernel(toff_ref, taps_ref, mix_ref, q_ref, k_ref, v_ref, rdoc_ref, kdoc_ref,
               heads_ref, probs_ref, sh_ref, acc_ref, *, nw, length):
    width = nw * TQ
    block = toff_ref[0] + pl.program_id(0)
    kstart = window_start(block, nw, length)
    allowed_ext, allowed_own = masks(block, kstart, width, rdoc_ref, kdoc_ref)
    for head in range(2):
        masked_shifts(q_ref, k_ref, head, kstart, width, allowed_ext, sh_ref)
        tap_accumulate(sh_ref, acc_ref, taps_ref, head, width)
        conv = acc_ref[0]
        for a in range(1, QCONV):
            conv = conv + pltpu.roll(acc_ref[a], a, 0)
        logits = jnp.where(allowed_own, conv[PAD:], -jnp.inf)
        highest = jnp.max(logits, axis=1, keepdims=True)
        highest = jnp.where(highest > -jnp.inf, highest, 0.0)
        expd = jnp.exp(logits - highest)
        denom = jnp.sum(expd, axis=1, keepdims=True)
        probs_ref[0, head] = expd / jnp.where(denom > 0.0, denom, 1.0)
    p0 = probs_ref[0, 0]
    p1 = probs_ref[0, 1]
    for c in range(2):
        mixed = (mix_ref[2 * c] * p0 + mix_ref[2 * c + 1] * p1).astype(jnp.bfloat16)
        heads_ref[0, c] = jnp.dot(
            mixed, v_ref[c, pl.ds(kstart, width), :], preferred_element_type=jnp.float32
        ).astype(jnp.bfloat16)


def attention_forward(toff, taps_flat, mix_flat, q_blocks, k_heads, v_heads, row_docs, key_docs, nw, length):
    nb_all = q_blocks.shape[0]
    width = nw * TQ
    smem = pl.BlockSpec(memory_space=pltpu.SMEM)
    flops = nb_all * 2 * (4 * EXT * width * HD + 2 * TAPS * EXT * width)
    return pl.pallas_call(
        lambda *refs: fwd_kernel(*refs, nw=nw, length=length),
        grid=(nb_all,),
        in_specs=[
            smem,
            smem,
            smem,
            pl.BlockSpec((1, 2, EXT, HD), lambda t: (t, 0, 0, 0)),
            pl.BlockSpec((2, length, HD), lambda t: (0, 0, 0)),
            pl.BlockSpec((2, length, HD), lambda t: (0, 0, 0)),
            pl.BlockSpec((1, EXT, 1), lambda t: (t, 0, 0)),
            pl.BlockSpec((1, length), lambda t: (0, 0)),
        ],
        out_specs=[
            pl.BlockSpec((1, 2, TQ, HD), lambda t: (t, 0, 0, 0)),
            pl.BlockSpec((1, 2, TQ, width), lambda t: (t, 0, 0, 0)),
        ],
        out_shape=[
            jax.ShapeDtypeStruct((nb_all, 2, TQ, HD), jnp.bfloat16),
            jax.ShapeDtypeStruct((nb_all, 2, TQ, width), jnp.float32),
        ],
        scratch_shapes=[
            pltpu.VMEM((KCONV, EXT, width), jnp.float32),
            pltpu.VMEM((QCONV, EXT, width), jnp.float32),
        ],
        compiler_params=pltpu.CompilerParams(
            dimension_semantics=("arbitrary",), vmem_limit_bytes=56 * 1024 * 1024
        ),
        cost_estimate=pl.CostEstimate(
            flops=flops, transcendentals=nb_all * 2 * TQ * width,
            bytes_accessed=nb_all * 2 * TQ * width * 4 + 4 * length * HD * 2,
        ),
    )(toff, taps_flat, mix_flat, q_blocks, k_heads, v_heads, row_docs, key_docs)


def bwd_kernel(toff_ref, taps_ref, mix_ref, q_ref, qo_ref, k_ref, v_ref, rdoc_ref, kdoc_ref,
               probs_ref, gh_ref, ght_ref, gq_ref, gk_ref, gv_ref, tacc_ref, macc_ref,
               carry_ref, sh_ref, acc_ref, g_ref, gx_ref, *, nw, length, nb, nb_all):
    width = nw * TQ
    step = pl.program_id(0)
    local = nb_all - 1 - step
    block = toff_ref[0] + local
    kstart = window_start(block, nw, length)

    @pl.when(step == 0)
    def _init():
        gk_ref[...] = jnp.zeros(gk_ref.shape, jnp.float32)
        gv_ref[...] = jnp.zeros(gv_ref.shape, jnp.float32)
        tacc_ref[...] = jnp.zeros(tacc_ref.shape, jnp.float32)
        macc_ref[...] = jnp.zeros(macc_ref.shape, jnp.float32)
        carry_ref[...] = jnp.zeros(carry_ref.shape, jnp.float32)

    allowed_ext, allowed_own = masks(block, kstart, width, rdoc_ref, kdoc_ref)
    gm = [
        lax.dot_general(
            gh_ref[0, c], v_ref[c, pl.ds(kstart, width), :], (((1,), (1,)), ((), ())),
            preferred_element_type=jnp.float32,
        )
        for c in range(2)
    ]
    probs = [probs_ref[0, 0], probs_ref[0, 1]]
    gc = []
    for e in range(2):
        gp = mix_ref[e] * gm[0] + mix_ref[2 + e] * gm[1]
        inner = jnp.sum(gp * probs[e], axis=1, keepdims=True)
        gc.append(probs[e] * (gp - inner))

    def own_sums():
        for c in range(2):
            for e in range(2):
                macc_ref[pl.ds(2 * c + e, 1), :] += jnp.sum(gm[c] * probs[e], axis=0, keepdims=True)
            mixed = (mix_ref[2 * c] * probs[0] + mix_ref[2 * c + 1] * probs[1]).astype(jnp.bfloat16)
            gv_ref[c, :, pl.ds(kstart, width)] += jnp.dot(
                ght_ref[0, c], mixed, preferred_element_type=jnp.float32
            )

    def head_taps(e):
        masked_shifts(q_ref, k_ref, e, kstart, width, allowed_ext, sh_ref)
        gcp = jnp.concatenate([jnp.zeros((PAD, width), jnp.float32), gc[e]], axis=0)
        g_ref[0] = gcp
        for a in range(1, QCONV):
            g_ref[a] = pltpu.roll(gcp, EXT - a, 0)
        sums = tap_products(sh_ref, g_ref, width)
        for b in range(KCONV):
            for a in range(QCONV):
                tacc_ref[e * TAPS + a * KCONV + b] += sums[(a, b)]

    def head_keys(e, gs):
        gk_ref[e, :, pl.ds(kstart, width)] += jnp.dot(
            qo_ref[0, e], gs, preferred_element_type=jnp.float32
        ) * SCALE

    nxt = [carry_ref[e, :, pl.ds(kstart, width + TQ)] for e in range(2)]
    if nb < nb_all:
        pl.when(local < nb)(own_sums)
    else:
        own_sums()
    for e in range(2):
        if nb < nb_all:
            pl.when(local < nb)(lambda: head_taps(e))
        else:
            head_taps(e)
        gx_ref[pl.ds(0, TQ), pl.ds(0, width)] = gc[e]
        gx_ref[pl.ds(0, TQ), pl.ds(width, TQ)] = jnp.zeros((TQ, TQ), jnp.float32)
        gx_ref[pl.ds(TQ, PAD), :] = nxt[e]
        gxv = gx_ref[...]
        sh_ref[0] = gxv[:, :width]
        for b in range(1, KCONV):
            sh_ref[b] = pltpu.roll(gxv, width + TQ - b, 1)[:, :width]
        tap_accumulate(sh_ref, acc_ref, taps_ref, e, width)
        gmk = acc_ref[0]
        for a in range(1, QCONV):
            gmk = gmk + pltpu.roll(acc_ref[a], EXT - a, 0)
        gs = jnp.where(allowed_own, gmk[:TQ], 0.0).astype(jnp.bfloat16)
        gq_ref[0, e] = (
            jnp.dot(gs, k_ref[e, pl.ds(kstart, width), :], preferred_element_type=jnp.float32) * SCALE
        ).astype(jnp.bfloat16)
        if nb < nb_all:
            pl.when(local < nb)(lambda: head_keys(e, gs))
        else:
            head_keys(e, gs)
    carry_ref[...] = jnp.zeros(carry_ref.shape, jnp.float32)
    for e in range(2):
        carry_ref[e, :, pl.ds(kstart, width)] = gc[e][:PAD]


def attention_backward(toff, taps_flat, mix_flat, q_blocks, q_own, k_heads, v_heads, row_docs, key_docs,
                       probs_blk, gh_blocks, nw, length, nb):
    q_own = jnp.swapaxes(q_own, 2, 3)
    gh_t = jnp.swapaxes(gh_blocks, 2, 3)
    nb_all = q_blocks.shape[0]
    width = nw * TQ
    smem = pl.BlockSpec(memory_space=pltpu.SMEM)
    rev = lambda s: nb_all - 1 - s
    flops = nb_all * 2 * (8 * TQ * width * HD + 6 * TAPS * EXT * width)
    return pl.pallas_call(
        lambda *refs: bwd_kernel(*refs, nw=nw, length=length, nb=nb, nb_all=nb_all),
        grid=(nb_all,),
        in_specs=[
            smem,
            smem,
            smem,
            pl.BlockSpec((1, 2, EXT, HD), lambda s: (rev(s), 0, 0, 0)),
            pl.BlockSpec((1, 2, HD, TQ), lambda s: (rev(s), 0, 0, 0)),
            pl.BlockSpec((2, length, HD), lambda s: (0, 0, 0)),
            pl.BlockSpec((2, length, HD), lambda s: (0, 0, 0)),
            pl.BlockSpec((1, EXT, 1), lambda s: (rev(s), 0, 0)),
            pl.BlockSpec((1, length), lambda s: (0, 0)),
            pl.BlockSpec((1, 2, TQ, width), lambda s: (rev(s), 0, 0, 0)),
            pl.BlockSpec((1, 2, TQ, HD), lambda s: (rev(s), 0, 0, 0)),
            pl.BlockSpec((1, 2, HD, TQ), lambda s: (rev(s), 0, 0, 0)),
        ],
        out_specs=[
            pl.BlockSpec((1, 2, TQ, HD), lambda s: (rev(s), 0, 0, 0)),
            pl.BlockSpec((2, HD, length), lambda s: (0, 0, 0)),
            pl.BlockSpec((2, HD, length), lambda s: (0, 0, 0)),
            pl.BlockSpec((2 * TAPS, 8, 128), lambda s: (0, 0, 0)),
            pl.BlockSpec((4, width), lambda s: (0, 0)),
        ],
        out_shape=[
            jax.ShapeDtypeStruct((nb_all, 2, TQ, HD), jnp.bfloat16),
            jax.ShapeDtypeStruct((2, HD, length), jnp.float32),
            jax.ShapeDtypeStruct((2, HD, length), jnp.float32),
            jax.ShapeDtypeStruct((2 * TAPS, 8, 128), jnp.float32),
            jax.ShapeDtypeStruct((4, width), jnp.float32),
        ],
        scratch_shapes=[
            pltpu.VMEM((2, PAD, length + TQ), jnp.float32),
            pltpu.VMEM((KCONV, EXT, width), jnp.float32),
            pltpu.VMEM((QCONV, EXT, width), jnp.float32),
            pltpu.VMEM((QCONV, EXT, width), jnp.float32),
            pltpu.VMEM((EXT, width + TQ), jnp.float32),
        ],
        compiler_params=pltpu.CompilerParams(
            dimension_semantics=("arbitrary",), vmem_limit_bytes=60 * 1024 * 1024
        ),
        cost_estimate=pl.CostEstimate(
            flops=flops, transcendentals=0,
            bytes_accessed=nb_all * 2 * TQ * width * 4 + 8 * length * HD * 4,
        ),
    )(toff, taps_flat, mix_flat, q_blocks, q_own, k_heads, v_heads, row_docs, key_docs, probs_blk, gh_blocks, gh_t)


def shards_body(
    inputs,
    doc_ids,
    w_query,
    w_key,
    w_value,
    w_out,
    gain_attn,
    gain_ffn,
    conv_taps,
    head_mix,
    w_gate,
    w_up,
    w_down,
    cotangent,
):
    row_dev, blk, width = inputs.shape
    assert row_dev == 1
    seq_count = lax.axis_size("seq")
    row_count = lax.axis_size("row")
    seq_index = lax.axis_index("seq")
    row_index = lax.axis_index("row")
    length = blk * seq_count
    groups = HEADS // 2
    assert seq_count % groups == 0
    splits = seq_count // groups
    span = length // splits
    pw = 2 * HD
    pair = seq_index // splits
    part = seq_index % splits
    q0 = part * span

    flat_in = inputs.reshape(blk, width)
    scale_one = rms_scale(flat_in)
    normed = (flat_in * scale_one * gain_attn).astype(jnp.bfloat16)
    normed_all = lax.all_gather(normed, "seq", axis=0, tiled=True)

    wq_g = lax.dynamic_slice_in_dim(w_query, pair * pw, pw, 1)
    wk_g = lax.dynamic_slice_in_dim(w_key, pair * pw, pw, 1)
    wv_g = lax.dynamic_slice_in_dim(w_value, pair * pw, pw, 1)
    wo_g = lax.dynamic_slice_in_dim(w_out, pair * pw, pw, 0)
    taps = lax.dynamic_slice_in_dim(conv_taps, pair * 2, 2, 0)
    mixing = lax.dynamic_index_in_dim(head_mix, pair, 0, keepdims=False)

    k_all = project(normed_all, wk_g).astype(jnp.bfloat16)
    v_all = project(normed_all, wv_g).astype(jnp.bfloat16)
    k3 = k_all.reshape(length, 2, HD)
    v3 = v_all.reshape(length, 2, HD)

    docs = doc_ids[0]
    nb = span // TQ
    extra = 1 if splits > 1 else 0
    nb_all = nb + extra
    doc_cap = length // 2
    nw = min(length // TQ, (doc_cap + QCONV - 2 + TQ - 1) // TQ + 1)
    q_tail = normed_pad_tail(normed_all, extra)
    q_rows = project(lax.dynamic_slice_in_dim(q_tail, q0, nb_all * TQ + PAD, 0), wq_g).astype(jnp.bfloat16)
    q_blocks = jnp.stack([q_rows[t * TQ : t * TQ + EXT] for t in range(nb_all)])
    q_blocks = jnp.transpose(q_blocks.reshape(nb_all, EXT, 2, HD), (0, 2, 1, 3))
    q_own = q_blocks[:, :, PAD:]
    k_heads = jnp.transpose(k3, (1, 0, 2))
    v_heads = jnp.transpose(v3, (1, 0, 2))
    docs_tail = jnp.pad(docs, (PAD, TQ * extra), constant_values=-1)
    doc_rows = lax.dynamic_slice_in_dim(docs_tail, q0, nb_all * TQ + PAD, 0)
    row_docs = jnp.stack([doc_rows[t * TQ : t * TQ + EXT] for t in range(nb_all)])[:, :, None]
    key_docs = docs[None, :]
    toff = (q0 // TQ).astype(jnp.int32).reshape(1)
    taps_flat = taps.reshape(2 * QCONV * KCONV)
    mix_flat = mixing.reshape(4)
    heads_blk, probs_blk = attention_forward(
        toff, taps_flat, mix_flat, q_blocks, k_heads, v_heads, row_docs, key_docs, nw, length
    )
    heads_own = jnp.transpose(heads_blk[:nb], (0, 2, 1, 3)).reshape(span, pw)

    def to_tokens(values):
        cols = values.shape[1]
        if splits == 1:
            full = values
        else:
            full = lax.dynamic_update_slice_in_dim(
                jnp.zeros((length, cols), values.dtype), values, q0, 0
            )
        got = lax.all_to_all(full, "seq", 0, 0, tiled=True)
        got = got.reshape(groups, splits, blk, cols)
        if splits > 1:
            got = jnp.sum(got.astype(jnp.float32), axis=1).astype(values.dtype)
        else:
            got = got[:, 0]
        return got

    heads_tok = jnp.transpose(to_tokens(heads_own), (1, 0, 2)).reshape(blk, width)
    middle = flat_in + project(heads_tok, w_out)
    scale_two = rms_scale(middle)
    normed_ffn = (middle * scale_two * gain_ffn).astype(jnp.bfloat16)
    gate_full = lax.all_gather(w_gate, "row", axis=0, tiled=True)
    up_full = lax.all_gather(w_up, "row", axis=0, tiled=True)
    down_full = lax.all_gather(w_down, "row", axis=1, tiled=True)
    hid_width = gate_full.shape[1]
    joint = jnp.concatenate([gate_full, up_full], axis=1)
    ffn_rows = lax.all_gather(normed_ffn, "seq", axis=0, tiled=True)
    gate_up = project(ffn_rows, joint)
    gate_vals = gate_up[:, :hid_width]
    up_vals = gate_up[:, hid_width:]
    hidden = (jax.nn.silu(gate_vals) * up_vals).astype(jnp.bfloat16)
    ffn_part = project(hidden, down_full).astype(jnp.bfloat16)
    cot_flat = cotangent.reshape(blk, width)
    cot_low = cot_flat.astype(jnp.bfloat16)
    cot_rows = lax.all_gather(cot_low, "seq", axis=0, tiled=True)
    grad_hidden = contract_cols(cot_rows, down_full)
    grad_down_part = contract_rows(hidden, cot_rows)
    sigmoid_gate = jax.nn.sigmoid(gate_vals)
    grad_gate_vals = grad_hidden * up_vals * sigmoid_gate * (1.0 + gate_vals * (1.0 - sigmoid_gate))
    grad_up_vals = grad_hidden * gate_vals * sigmoid_gate
    grad_joint = jnp.concatenate([grad_gate_vals, grad_up_vals], axis=1).astype(jnp.bfloat16)
    grad_joint_w = contract_rows(ffn_rows, grad_joint)
    grad_normed_ffn = lax.psum_scatter(
        contract_cols(grad_joint, joint).astype(jnp.bfloat16),
        "seq",
        scatter_dimension=0,
        tiled=True,
    ).astype(jnp.float32)
    grad_w_gate, grad_w_up, grad_w_down = (
        lax.psum_scatter(
            grad_joint_w[:, :hid_width].astype(jnp.bfloat16), "row", scatter_dimension=0, tiled=True
        ).astype(jnp.float32),
        lax.psum_scatter(
            grad_joint_w[:, hid_width:].astype(jnp.bfloat16), "row", scatter_dimension=0, tiled=True
        ).astype(jnp.float32),
        lax.psum_scatter(
            grad_down_part.astype(jnp.bfloat16), "row", scatter_dimension=1, tiled=True
        ).astype(jnp.float32),
    )
    gain_ffn_part = jnp.sum(grad_normed_ffn * middle * scale_two, axis=0)
    scaled_two = grad_normed_ffn * gain_ffn
    grad_middle = (
        cot_flat
        + scale_two * scaled_two
        - middle * scale_two**3 * jnp.mean(scaled_two * middle, axis=-1, keepdims=True)
    )
    grad_attn = grad_middle.astype(jnp.bfloat16)
    grad_attn_all = lax.all_gather(grad_attn, "seq", axis=0, tiled=True)
    ffn_part, grad_attn_all = lax.optimization_barrier((ffn_part, grad_attn_all))
    ffn_out = lax.psum_scatter(ffn_part, "seq", scatter_dimension=0, tiled=True).astype(jnp.float32)
    outputs = middle + ffn_out
    grad_attn_tail = jnp.pad(grad_attn_all, ((0, TQ * extra), (0, 0)))
    grad_heads_x = contract_cols(
        lax.dynamic_slice_in_dim(grad_attn_tail, q0, nb_all * TQ, 0), wo_g
    ).astype(jnp.bfloat16)
    gh_blocks = jnp.transpose(grad_heads_x.reshape(nb_all, TQ, 2, HD), (0, 2, 1, 3))
    grad_out_part = contract_rows(heads_own, lax.dynamic_slice_in_dim(grad_attn_all, q0, span, 0))
    gq_blk, gk_heads, gv_heads, tap_acc, mix_acc = attention_backward(
        toff, taps_flat, mix_flat, q_blocks, q_own, k_heads, v_heads, row_docs, key_docs,
        probs_blk, gh_blocks, nw, length, nb,
    )
    grad_q_own = jnp.transpose(gq_blk[:nb], (0, 2, 1, 3)).reshape(span, pw)
    grad_k_part = jnp.transpose(gk_heads, (2, 0, 1)).reshape(length, pw)
    grad_v_part = jnp.transpose(gv_heads, (2, 0, 1)).reshape(length, pw)
    grad_taps_part = jnp.sum(tap_acc, axis=(1, 2)).reshape(2, QCONV, KCONV)
    grad_mix_part = jnp.sum(mix_acc, axis=1).reshape(2, 2)

    def split_sum(values):
        if splits == 1:
            return values
        total = values
        for step in range(1, splits):
            route = []
            for s in range(seq_count):
                base = (s // splits) * splits
                route.append((s, base + (s - base + step) % splits))
            total = total + lax.ppermute(values, "seq", route)
        return total

    grad_k_low = split_sum(grad_k_part).astype(jnp.bfloat16)
    grad_v_low = split_sum(grad_v_part).astype(jnp.bfloat16)
    grad_k_own = lax.dynamic_slice_in_dim(grad_k_low, q0, span, 0)
    grad_v_own = lax.dynamic_slice_in_dim(grad_v_low, q0, span, 0)

    normed_own = lax.dynamic_slice_in_dim(normed_all, q0, span, 0)
    rows_per_dev = width // (row_count * seq_count)

    def finish_in(partial):
        red = lax.psum_scatter(partial, "row", scatter_dimension=0, tiled=True)
        got = lax.all_to_all(red, "seq", 0, 0, tiled=True)
        got = got.reshape(groups, splits, rows_per_dev, pw).sum(axis=1)
        return jnp.transpose(got, (1, 0, 2)).reshape(rows_per_dev, width)

    grad_w_query = finish_in(contract_rows(normed_own, grad_q_own))
    grad_w_key = finish_in(contract_rows(normed_own, grad_k_own))
    grad_w_value = finish_in(contract_rows(normed_own, grad_v_own))

    red_out = lax.psum_scatter(grad_out_part, "row", scatter_dimension=0, tiled=True)
    red_out = red_out.reshape(splits, rows_per_dev, width)
    grad_w_out = jnp.zeros((rows_per_dev, width), jnp.float32)
    for src_part in range(splits):
        for j in range(splits):
            route = []
            for r in range(row_count):
                for g in range(groups):
                    src = r * seq_count + g * splits + src_part
                    dst = g * row_count * splits + r * splits + j
                    route.append((src, dst))
            grad_w_out = grad_w_out + lax.ppermute(red_out[j], ("row", "seq"), route)

    grad_tok = to_tokens(jnp.concatenate([grad_q_own, grad_k_own, grad_v_own], axis=1))
    grad_tok = grad_tok.reshape(groups, blk, 3, pw)
    gq_tok = jnp.transpose(grad_tok[:, :, 0], (1, 0, 2)).reshape(blk, width)
    gk_tok = jnp.transpose(grad_tok[:, :, 1], (1, 0, 2)).reshape(blk, width)
    gv_tok = jnp.transpose(grad_tok[:, :, 2], (1, 0, 2)).reshape(blk, width)
    grad_normed = (
        contract_cols(gq_tok, w_query) + contract_cols(gk_tok, w_key) + contract_cols(gv_tok, w_value)
    )
    gain_attn_part = jnp.sum(grad_normed * flat_in * scale_one, axis=0)
    scaled_one = grad_normed * gain_attn
    grad_inputs = (
        grad_middle
        + scale_one * scaled_one
        - flat_in * scale_one**3 * jnp.mean(scaled_one * flat_in, axis=-1, keepdims=True)
    )
    taps_full = lax.dynamic_update_slice_in_dim(
        jnp.zeros((HEADS, QCONV, KCONV), jnp.float32), grad_taps_part, pair * 2, 0
    )
    mix_full = lax.dynamic_update_slice_in_dim(
        jnp.zeros((groups, 2, 2), jnp.float32), grad_mix_part[None], pair, 0
    )
    small = jnp.concatenate(
        [gain_attn_part, gain_ffn_part, taps_full.reshape(-1), mix_full.reshape(-1)]
    )
    small = lax.psum(lax.psum(small, "seq"), "row")
    gain_rows = width // (row_count * seq_count)
    gain_at = (row_index * seq_count + seq_index) * gain_rows
    grad_gain_attn = lax.dynamic_slice_in_dim(small, gain_at, gain_rows, 0)
    grad_gain_ffn = lax.dynamic_slice_in_dim(small, width + gain_at, gain_rows, 0)
    grad_taps = small[2 * width : 2 * width + HEADS * TAPS].reshape(HEADS, QCONV, KCONV)
    grad_mix = small[2 * width + HEADS * TAPS :].reshape(groups, 2, 2)
    return (
        outputs.reshape(row_dev, blk, width),
        grad_inputs.reshape(row_dev, blk, width),
        grad_w_query,
        grad_w_key,
        grad_w_value,
        grad_w_out,
        grad_gain_attn,
        grad_gain_ffn,
        grad_taps,
        grad_mix,
        grad_w_gate,
        grad_w_up,
        grad_w_down,
    )


def solution(mesh):
    return jax.shard_map(
        shards_body,
        mesh=mesh,
        in_specs=(
            P("row", "seq", None),
            P("row", None),
            P(),
            P(),
            P(),
            P(),
            P(),
            P(),
            P(),
            P(),
            P("row", "seq"),
            P("row", "seq"),
            P("seq", "row"),
            P("row", "seq", None),
        ),
        out_specs=(
            P("row", "seq", None),
            P("row", "seq", None),
            P(("row", "seq"), None),
            P(("row", "seq"), None),
            P(("row", "seq"), None),
            P(("row", "seq"), None),
            P(("row", "seq")),
            P(("row", "seq")),
            P(),
            P(),
            P("row", "seq"),
            P("row", "seq"),
            P("seq", "row"),
        ),
        check_vma=False,
    )
```

```python
import jax
import jax.numpy as jnp
from jax import lax
from jax.sharding import PartitionSpec as P
from jax.experimental import pallas as pl
from jax.experimental.pallas import tpu as pltpu

HEADS = 16
HD = 96
QCONV = 6
KCONV = 11
PAD = 8
TQ = 128
EXT = TQ + PAD
SCALE = HD ** (-0.5)
TAPS = QCONV * KCONV

epsilon = 1e-06


def rms_scale(values):
    return lax.rsqrt(jnp.mean(values * values, axis=-1, keepdims=True) + epsilon)


def project(values, weight):
    return jnp.dot(values, weight, preferred_element_type=jnp.float32)


def contract_rows(left, right):
    return lax.dot_general(
        left, right, (((0,), (0,)), ((), ())), preferred_element_type=jnp.float32
    )


def contract_cols(left, right):
    return lax.dot_general(
        left, right, (((1,), (1,)), ((), ())), preferred_element_type=jnp.float32
    )


def normed_pad_tail(values, extra):
    return jnp.pad(values, ((PAD, TQ * extra), (0, 0)))


def window_start(block, nw, length):
    return pl.multiple_of(jnp.clip((block - nw + 1) * TQ, 0, length - nw * TQ), TQ)


def tap_accumulate(sh_ref, acc_ref, taps_ref, head, width):
    cw = 256 if (width // 128) % 2 == 0 else 128
    ncols = width // cw

    def body(idx, carry):
        r0 = pl.multiple_of((idx // ncols) * 8, 8)
        c0 = pl.multiple_of((idx % ncols) * cw, cw)
        tiles = [sh_ref[b, pl.ds(r0, 8), pl.ds(c0, cw)] for b in range(KCONV)]
        for a in range(QCONV):
            base = head * TAPS + a * KCONV
            total = taps_ref[base] * tiles[0]
            for b in range(1, KCONV):
                total = total + taps_ref[base + b] * tiles[b]
            acc_ref[a, pl.ds(r0, 8), pl.ds(c0, cw)] = total
        return carry

    lax.fori_loop(0, (EXT // 8) * ncols, body, 0)


def tap_products(sh_ref, g_ref, width):
    ncols = width // 128
    sums = {}
    for a0 in range(0, QCONV, 2):

        def body(idx, accs):
            r0 = pl.multiple_of((idx // ncols) * 8, 8)
            c0 = pl.multiple_of((idx % ncols) * 128, 128)
            ga = [g_ref[a0 + k, pl.ds(r0, 8), pl.ds(c0, 128)] for k in range(2)]
            out = list(accs)
            for b in range(KCONV):
                tile = sh_ref[b, pl.ds(r0, 8), pl.ds(c0, 128)]
                for k in range(2):
                    out[k * KCONV + b] = out[k * KCONV + b] + ga[k] * tile
            return tuple(out)

        start = tuple(jnp.zeros((8, 128), jnp.float32) for _ in range(2 * KCONV))
        res = lax.fori_loop(0, (EXT // 8) * ncols, body, start)
        for k in range(2):
            for b in range(KCONV):
                sums[(a0 + k, b)] = res[k * KCONV + b]
    return sums


def masks(block, kstart, width, rdoc_ref, kdoc_ref):
    keydoc = kdoc_ref[:, pl.ds(kstart, width)]
    ext_pos = block * TQ - PAD + lax.broadcasted_iota(jnp.int32, (EXT, width), 0)
    key_ext = kstart + lax.broadcasted_iota(jnp.int32, (EXT, width), 1)
    allowed_ext = (key_ext <= ext_pos) & (rdoc_ref[0] == keydoc)
    own_pos = block * TQ + lax.broadcasted_iota(jnp.int32, (TQ, width), 0)
    key_own = kstart + lax.broadcasted_iota(jnp.int32, (TQ, width), 1)
    allowed_own = (key_own <= own_pos) & (rdoc_ref[0, PAD:, :] == keydoc)
    return allowed_ext, allowed_own


def masked_shifts(q_ref, k_ref, head, kstart, width, allowed_ext, sh_ref):
    keys = k_ref[head, pl.ds(kstart, width), :]
    scores = lax.dot_general(
        q_ref[0, head], keys, (((1,), (1,)), ((), ())), preferred_element_type=jnp.float32
    ) * SCALE
    masked = jnp.where(allowed_ext, scores, 0.0)
    col = lax.broadcasted_iota(jnp.int32, (EXT, width), 1)
    sh_ref[0] = masked
    for b in range(1, KCONV):
        sh_ref[b] = jnp.where(col >= b, pltpu.roll(masked, b, 1), 0.0)


def fwd_kernel(toff_ref, taps_ref, mix_ref, q_ref, k_ref, v_ref, rdoc_ref, kdoc_ref,
               heads_ref, probs_ref, sh_ref, acc_ref, *, nw, length):
    width = nw * TQ
    block = toff_ref[0] + pl.program_id(0)
    kstart = window_start(block, nw, length)
    allowed_ext, allowed_own = masks(block, kstart, width, rdoc_ref, kdoc_ref)
    for head in range(2):
        masked_shifts(q_ref, k_ref, head, kstart, width, allowed_ext, sh_ref)
        tap_accumulate(sh_ref, acc_ref, taps_ref, head, width)
        conv = acc_ref[0]
        for a in range(1, QCONV):
            conv = conv + pltpu.roll(acc_ref[a], a, 0)
        logits = jnp.where(allowed_own, conv[PAD:], -jnp.inf)
        highest = jnp.max(logits, axis=1, keepdims=True)
        highest = jnp.where(highest > -jnp.inf, highest, 0.0)
        expd = jnp.exp(logits - highest)
        denom = jnp.sum(expd, axis=1, keepdims=True)
        probs_ref[0, head] = expd / jnp.where(denom > 0.0, denom, 1.0)
    p0 = probs_ref[0, 0]
    p1 = probs_ref[0, 1]
    for c in range(2):
        mixed = (mix_ref[2 * c] * p0 + mix_ref[2 * c + 1] * p1).astype(jnp.bfloat16)
        heads_ref[0, c] = jnp.dot(
            mixed, v_ref[c, pl.ds(kstart, width), :], preferred_element_type=jnp.float32
        ).astype(jnp.bfloat16)


def attention_forward(toff, taps_flat, mix_flat, q_blocks, k_heads, v_heads, row_docs, key_docs, nw, length):
    nb_all = q_blocks.shape[0]
    width = nw * TQ
    smem = pl.BlockSpec(memory_space=pltpu.SMEM)
    flops = nb_all * 2 * (4 * EXT * width * HD + 2 * TAPS * EXT * width)
    return pl.pallas_call(
        lambda *refs: fwd_kernel(*refs, nw=nw, length=length),
        grid=(nb_all,),
        in_specs=[
            smem,
            smem,
            smem,
            pl.BlockSpec((1, 2, EXT, HD), lambda t: (t, 0, 0, 0)),
            pl.BlockSpec((2, length, HD), lambda t: (0, 0, 0)),
            pl.BlockSpec((2, length, HD), lambda t: (0, 0, 0)),
            pl.BlockSpec((1, EXT, 1), lambda t: (t, 0, 0)),
            pl.BlockSpec((1, length), lambda t: (0, 0)),
        ],
        out_specs=[
            pl.BlockSpec((1, 2, TQ, HD), lambda t: (t, 0, 0, 0)),
            pl.BlockSpec((1, 2, TQ, width), lambda t: (t, 0, 0, 0)),
        ],
        out_shape=[
            jax.ShapeDtypeStruct((nb_all, 2, TQ, HD), jnp.bfloat16),
            jax.ShapeDtypeStruct((nb_all, 2, TQ, width), jnp.float32),
        ],
        scratch_shapes=[
            pltpu.VMEM((KCONV, EXT, width), jnp.float32),
            pltpu.VMEM((QCONV, EXT, width), jnp.float32),
        ],
        compiler_params=pltpu.CompilerParams(
            dimension_semantics=("arbitrary",), vmem_limit_bytes=56 * 1024 * 1024
        ),
        cost_estimate=pl.CostEstimate(
            flops=flops, transcendentals=nb_all * 2 * TQ * width,
            bytes_accessed=nb_all * 2 * TQ * width * 4 + 4 * length * HD * 2,
        ),
    )(toff, taps_flat, mix_flat, q_blocks, k_heads, v_heads, row_docs, key_docs)


def bwd_kernel(toff_ref, taps_ref, mix_ref, q_ref, qo_ref, k_ref, v_ref, rdoc_ref, kdoc_ref,
               probs_ref, gh_ref, ght_ref, gq_ref, gk_ref, gv_ref, tacc_ref, macc_ref,
               carry_ref, sh_ref, acc_ref, g_ref, gx_ref, *, nw, length, nb, nb_all):
    width = nw * TQ
    step = pl.program_id(0)
    local = nb_all - 1 - step
    block = toff_ref[0] + local
    kstart = window_start(block, nw, length)

    @pl.when(step == 0)
    def _init():
        gk_ref[...] = jnp.zeros(gk_ref.shape, jnp.float32)
        gv_ref[...] = jnp.zeros(gv_ref.shape, jnp.float32)
        tacc_ref[...] = jnp.zeros(tacc_ref.shape, jnp.float32)
        macc_ref[...] = jnp.zeros(macc_ref.shape, jnp.float32)
        carry_ref[...] = jnp.zeros(carry_ref.shape, jnp.float32)

    allowed_ext, allowed_own = masks(block, kstart, width, rdoc_ref, kdoc_ref)
    gm = [
        lax.dot_general(
            gh_ref[0, c], v_ref[c, pl.ds(kstart, width), :], (((1,), (1,)), ((), ())),
            preferred_element_type=jnp.float32,
        )
        for c in range(2)
    ]
    probs = [probs_ref[0, 0], probs_ref[0, 1]]
    gc = []
    for e in range(2):
        gp = mix_ref[e] * gm[0] + mix_ref[2 + e] * gm[1]
        inner = jnp.sum(gp * probs[e], axis=1, keepdims=True)
        gc.append(probs[e] * (gp - inner))

    def own_sums():
        for c in range(2):
            for e in range(2):
                macc_ref[pl.ds(2 * c + e, 1), :] += jnp.sum(gm[c] * probs[e], axis=0, keepdims=True)
            mixed = (mix_ref[2 * c] * probs[0] + mix_ref[2 * c + 1] * probs[1]).astype(jnp.bfloat16)
            gv_ref[c, :, pl.ds(kstart, width)] += jnp.dot(
                ght_ref[0, c], mixed, preferred_element_type=jnp.float32
            )

    def head_taps(e):
        masked_shifts(q_ref, k_ref, e, kstart, width, allowed_ext, sh_ref)
        gcp = jnp.concatenate([jnp.zeros((PAD, width), jnp.float32), gc[e]], axis=0)
        g_ref[0] = gcp
        for a in range(1, QCONV):
            g_ref[a] = pltpu.roll(gcp, EXT - a, 0)
        sums = tap_products(sh_ref, g_ref, width)
        for b in range(KCONV):
            for a in range(QCONV):
                tacc_ref[e * TAPS + a * KCONV + b] += sums[(a, b)]

    def head_keys(e, gs):
        gk_ref[e, :, pl.ds(kstart, width)] += jnp.dot(
            qo_ref[0, e], gs, preferred_element_type=jnp.float32
        ) * SCALE

    nxt = [carry_ref[e, :, pl.ds(kstart, width + TQ)] for e in range(2)]
    if nb < nb_all:
        pl.when(local < nb)(own_sums)
    else:
        own_sums()
    for e in range(2):
        if nb < nb_all:
            pl.when(local < nb)(lambda: head_taps(e))
        else:
            head_taps(e)
        gx_ref[pl.ds(0, TQ), pl.ds(0, width)] = gc[e]
        gx_ref[pl.ds(0, TQ), pl.ds(width, TQ)] = jnp.zeros((TQ, TQ), jnp.float32)
        gx_ref[pl.ds(TQ, PAD), :] = nxt[e]
        gxv = gx_ref[...]
        sh_ref[0] = gxv[:, :width]
        for b in range(1, KCONV):
            sh_ref[b] = pltpu.roll(gxv, width + TQ - b, 1)[:, :width]
        tap_accumulate(sh_ref, acc_ref, taps_ref, e, width)
        gmk = acc_ref[0]
        for a in range(1, QCONV):
            gmk = gmk + pltpu.roll(acc_ref[a], EXT - a, 0)
        gs = jnp.where(allowed_own, gmk[:TQ], 0.0).astype(jnp.bfloat16)
        gq_ref[0, e] = (
            jnp.dot(gs, k_ref[e, pl.ds(kstart, width), :], preferred_element_type=jnp.float32) * SCALE
        ).astype(jnp.bfloat16)
        if nb < nb_all:
            pl.when(local < nb)(lambda: head_keys(e, gs))
        else:
            head_keys(e, gs)
    carry_ref[...] = jnp.zeros(carry_ref.shape, jnp.float32)
    for e in range(2):
        carry_ref[e, :, pl.ds(kstart, width)] = gc[e][:PAD]


def attention_backward(toff, taps_flat, mix_flat, q_blocks, q_own, k_heads, v_heads, row_docs, key_docs,
                       probs_blk, gh_blocks, nw, length, nb):
    q_own = jnp.swapaxes(q_own, 2, 3)
    gh_t = jnp.swapaxes(gh_blocks, 2, 3)
    nb_all = q_blocks.shape[0]
    width = nw * TQ
    smem = pl.BlockSpec(memory_space=pltpu.SMEM)
    rev = lambda s: nb_all - 1 - s
    flops = nb_all * 2 * (8 * TQ * width * HD + 6 * TAPS * EXT * width)
    return pl.pallas_call(
        lambda *refs: bwd_kernel(*refs, nw=nw, length=length, nb=nb, nb_all=nb_all),
        grid=(nb_all,),
        in_specs=[
            smem,
            smem,
            smem,
            pl.BlockSpec((1, 2, EXT, HD), lambda s: (rev(s), 0, 0, 0)),
            pl.BlockSpec((1, 2, HD, TQ), lambda s: (rev(s), 0, 0, 0)),
            pl.BlockSpec((2, length, HD), lambda s: (0, 0, 0)),
            pl.BlockSpec((2, length, HD), lambda s: (0, 0, 0)),
            pl.BlockSpec((1, EXT, 1), lambda s: (rev(s), 0, 0)),
            pl.BlockSpec((1, length), lambda s: (0, 0)),
            pl.BlockSpec((1, 2, TQ, width), lambda s: (rev(s), 0, 0, 0)),
            pl.BlockSpec((1, 2, TQ, HD), lambda s: (rev(s), 0, 0, 0)),
            pl.BlockSpec((1, 2, HD, TQ), lambda s: (rev(s), 0, 0, 0)),
        ],
        out_specs=[
            pl.BlockSpec((1, 2, TQ, HD), lambda s: (rev(s), 0, 0, 0)),
            pl.BlockSpec((2, HD, length), lambda s: (0, 0, 0)),
            pl.BlockSpec((2, HD, length), lambda s: (0, 0, 0)),
            pl.BlockSpec((2 * TAPS, 8, 128), lambda s: (0, 0, 0)),
            pl.BlockSpec((4, width), lambda s: (0, 0)),
        ],
        out_shape=[
            jax.ShapeDtypeStruct((nb_all, 2, TQ, HD), jnp.bfloat16),
            jax.ShapeDtypeStruct((2, HD, length), jnp.float32),
            jax.ShapeDtypeStruct((2, HD, length), jnp.float32),
            jax.ShapeDtypeStruct((2 * TAPS, 8, 128), jnp.float32),
            jax.ShapeDtypeStruct((4, width), jnp.float32),
        ],
        scratch_shapes=[
            pltpu.VMEM((2, PAD, length + TQ), jnp.float32),
            pltpu.VMEM((KCONV, EXT, width), jnp.float32),
            pltpu.VMEM((QCONV, EXT, width), jnp.float32),
            pltpu.VMEM((QCONV, EXT, width), jnp.float32),
            pltpu.VMEM((EXT, width + TQ), jnp.float32),
        ],
        compiler_params=pltpu.CompilerParams(
            dimension_semantics=("arbitrary",), vmem_limit_bytes=60 * 1024 * 1024
        ),
        cost_estimate=pl.CostEstimate(
            flops=flops, transcendentals=0,
            bytes_accessed=nb_all * 2 * TQ * width * 4 + 8 * length * HD * 4,
        ),
    )(toff, taps_flat, mix_flat, q_blocks, q_own, k_heads, v_heads, row_docs, key_docs, probs_blk, gh_blocks, gh_t)


def shards_body(
    inputs,
    doc_ids,
    w_query,
    w_key,
    w_value,
    w_out,
    gain_attn,
    gain_ffn,
    conv_taps,
    head_mix,
    w_gate,
    w_up,
    w_down,
    cotangent,
):
    row_dev, blk, width = inputs.shape
    assert row_dev == 1
    seq_count = lax.axis_size("seq")
    row_count = lax.axis_size("row")
    seq_index = lax.axis_index("seq")
    row_index = lax.axis_index("row")
    length = blk * seq_count
    groups = HEADS // 2
    assert seq_count % groups == 0
    splits = seq_count // groups
    span = length // splits
    pw = 2 * HD
    pair = seq_index // splits
    part = seq_index % splits
    q0 = part * span

    flat_in = inputs.reshape(blk, width)
    scale_one = rms_scale(flat_in)
    normed = (flat_in * scale_one * gain_attn).astype(jnp.bfloat16)
    normed_all = lax.all_gather(normed, "seq", axis=0, tiled=True)

    wq_g = lax.dynamic_slice_in_dim(w_query, pair * pw, pw, 1)
    wk_g = lax.dynamic_slice_in_dim(w_key, pair * pw, pw, 1)
    wv_g = lax.dynamic_slice_in_dim(w_value, pair * pw, pw, 1)
    wo_g = lax.dynamic_slice_in_dim(w_out, pair * pw, pw, 0)
    taps = lax.dynamic_slice_in_dim(conv_taps, pair * 2, 2, 0)
    mixing = lax.dynamic_index_in_dim(head_mix, pair, 0, keepdims=False)

    k_all = project(normed_all, wk_g).astype(jnp.bfloat16)
    v_all = project(normed_all, wv_g).astype(jnp.bfloat16)
    k3 = k_all.reshape(length, 2, HD)
    v3 = v_all.reshape(length, 2, HD)

    docs = doc_ids[0]
    nb = span // TQ
    extra = 1 if splits > 1 else 0
    nb_all = nb + extra
    doc_cap = length // 2
    nw = min(length // TQ, (doc_cap + QCONV - 2 + TQ - 1) // TQ + 1)
    q_tail = normed_pad_tail(normed_all, extra)
    q_rows = project(lax.dynamic_slice_in_dim(q_tail, q0, nb_all * TQ + PAD, 0), wq_g).astype(jnp.bfloat16)
    q_blocks = jnp.stack([q_rows[t * TQ : t * TQ + EXT] for t in range(nb_all)])
    q_blocks = jnp.transpose(q_blocks.reshape(nb_all, EXT, 2, HD), (0, 2, 1, 3))
    q_own = q_blocks[:, :, PAD:]
    k_heads = jnp.transpose(k3, (1, 0, 2))
    v_heads = jnp.transpose(v3, (1, 0, 2))
    docs_tail = jnp.pad(docs, (PAD, TQ * extra), constant_values=-1)
    doc_rows = lax.dynamic_slice_in_dim(docs_tail, q0, nb_all * TQ + PAD, 0)
    row_docs = jnp.stack([doc_rows[t * TQ : t * TQ + EXT] for t in range(nb_all)])[:, :, None]
    key_docs = docs[None, :]
    toff = (q0 // TQ).astype(jnp.int32).reshape(1)
    taps_flat = taps.reshape(2 * QCONV * KCONV)
    mix_flat = mixing.reshape(4)
    heads_blk, probs_blk = attention_forward(
        toff, taps_flat, mix_flat, q_blocks, k_heads, v_heads, row_docs, key_docs, nw, length
    )
    heads_own = jnp.transpose(heads_blk[:nb], (0, 2, 1, 3)).reshape(span, pw)

    def to_tokens(values):
        cols = values.shape[1]
        if splits == 1:
            full = values
        else:
            full = lax.dynamic_update_slice_in_dim(
                jnp.zeros((length, cols), values.dtype), values, q0, 0
            )
        got = lax.all_to_all(full, "seq", 0, 0, tiled=True)
        got = got.reshape(groups, splits, blk, cols)
        if splits > 1:
            got = jnp.sum(got.astype(jnp.float32), axis=1).astype(values.dtype)
        else:
            got = got[:, 0]
        return got

    heads_tok = jnp.transpose(to_tokens(heads_own), (1, 0, 2)).reshape(blk, width)
    middle = flat_in + project(heads_tok, w_out)
    scale_two = rms_scale(middle)
    normed_ffn = (middle * scale_two * gain_ffn).astype(jnp.bfloat16)
    gate_full = lax.all_gather(w_gate, "row", axis=0, tiled=True)
    up_full = lax.all_gather(w_up, "row", axis=0, tiled=True)
    down_full = lax.all_gather(w_down, "row", axis=1, tiled=True)
    hid_width = gate_full.shape[1]
    joint = jnp.concatenate([gate_full, up_full], axis=1)
    ffn_rows = lax.all_gather(normed_ffn, "seq", axis=0, tiled=True)
    gate_up = project(ffn_rows, joint)
    gate_vals = gate_up[:, :hid_width]
    up_vals = gate_up[:, hid_width:]
    hidden = (jax.nn.silu(gate_vals) * up_vals).astype(jnp.bfloat16)
    ffn_part = project(hidden, down_full).astype(jnp.bfloat16)
    cot_flat = cotangent.reshape(blk, width)
    cot_low = cot_flat.astype(jnp.bfloat16)
    cot_rows = lax.all_gather(cot_low, "seq", axis=0, tiled=True)
    grad_hidden = contract_cols(cot_rows, down_full)
    grad_down_part = contract_rows(hidden, cot_rows)
    sigmoid_gate = jax.nn.sigmoid(gate_vals)
    grad_gate_vals = grad_hidden * up_vals * sigmoid_gate * (1.0 + gate_vals * (1.0 - sigmoid_gate))
    grad_up_vals = grad_hidden * gate_vals * sigmoid_gate
    grad_joint = jnp.concatenate([grad_gate_vals, grad_up_vals], axis=1).astype(jnp.bfloat16)
    grad_joint_w = contract_rows(ffn_rows, grad_joint)
    grad_normed_ffn = lax.psum_scatter(
        contract_cols(grad_joint, joint).astype(jnp.bfloat16),
        "seq",
        scatter_dimension=0,
        tiled=True,
    ).astype(jnp.float32)
    grad_w_gate, grad_w_up, grad_w_down = (
        lax.psum_scatter(
            grad_joint_w[:, :hid_width].astype(jnp.bfloat16), "row", scatter_dimension=0, tiled=True
        ).astype(jnp.float32),
        lax.psum_scatter(
            grad_joint_w[:, hid_width:].astype(jnp.bfloat16), "row", scatter_dimension=0, tiled=True
        ).astype(jnp.float32),
        lax.psum_scatter(
            grad_down_part.astype(jnp.bfloat16), "row", scatter_dimension=1, tiled=True
        ).astype(jnp.float32),
    )
    gain_ffn_part = jnp.sum(grad_normed_ffn * middle * scale_two, axis=0)
    scaled_two = grad_normed_ffn * gain_ffn
    grad_middle = (
        cot_flat
        + scale_two * scaled_two
        - middle * scale_two**3 * jnp.mean(scaled_two * middle, axis=-1, keepdims=True)
    )
    grad_attn = grad_middle.astype(jnp.bfloat16)
    grad_attn_all = lax.all_gather(grad_attn, "seq", axis=0, tiled=True)
    ffn_part, grad_attn_all = lax.optimization_barrier((ffn_part, grad_attn_all))
    ffn_out = lax.psum_scatter(ffn_part, "seq", scatter_dimension=0, tiled=True).astype(jnp.float32)
    outputs = middle + ffn_out
    grad_attn_tail = jnp.pad(grad_attn_all, ((0, TQ * extra), (0, 0)))
    grad_heads_x = contract_cols(
        lax.dynamic_slice_in_dim(grad_attn_tail, q0, nb_all * TQ, 0), wo_g
    ).astype(jnp.bfloat16)
    gh_blocks = jnp.transpose(grad_heads_x.reshape(nb_all, TQ, 2, HD), (0, 2, 1, 3))
    grad_out_part = contract_rows(heads_own, lax.dynamic_slice_in_dim(grad_attn_all, q0, span, 0))
    gq_blk, gk_heads, gv_heads, tap_acc, mix_acc = attention_backward(
        toff, taps_flat, mix_flat, q_blocks, q_own, k_heads, v_heads, row_docs, key_docs,
        probs_blk, gh_blocks, nw, length, nb,
    )
    grad_q_own = jnp.transpose(gq_blk[:nb], (0, 2, 1, 3)).reshape(span, pw)
    grad_k_part = jnp.transpose(gk_heads, (2, 0, 1)).reshape(length, pw)
    grad_v_part = jnp.transpose(gv_heads, (2, 0, 1)).reshape(length, pw)
    grad_taps_part = jnp.sum(tap_acc, axis=(1, 2)).reshape(2, QCONV, KCONV)
    grad_mix_part = jnp.sum(mix_acc, axis=1).reshape(2, 2)

    def split_sum(values):
        if splits == 1:
            return values
        total = values
        for step in range(1, splits):
            route = []
            for s in range(seq_count):
                base = (s // splits) * splits
                route.append((s, base + (s - base + step) % splits))
            total = total + lax.ppermute(values, "seq", route)
        return total

    grad_k_low = split_sum(grad_k_part).astype(jnp.bfloat16)
    grad_v_low = split_sum(grad_v_part).astype(jnp.bfloat16)
    grad_k_own = lax.dynamic_slice_in_dim(grad_k_low, q0, span, 0)
    grad_v_own = lax.dynamic_slice_in_dim(grad_v_low, q0, span, 0)

    normed_own = lax.dynamic_slice_in_dim(normed_all, q0, span, 0)
    rows_per_dev = width // (row_count * seq_count)

    partials = jnp.stack(
        [
            contract_rows(normed_own, grad_q_own),
            contract_rows(normed_own, grad_k_own),
            contract_rows(normed_own, grad_v_own),
        ]
    )
    red = lax.psum_scatter(partials, "row", scatter_dimension=1, tiled=True)
    got = lax.all_to_all(red, "seq", 1, 1, tiled=True)
    got = got.reshape(3, groups, splits, rows_per_dev, pw).sum(axis=2)
    got = jnp.transpose(got, (0, 2, 1, 3)).reshape(3, rows_per_dev, width)
    grad_w_query, grad_w_key, grad_w_value = got[0], got[1], got[2]

    red_out = lax.psum_scatter(grad_out_part, "row", scatter_dimension=0, tiled=True)
    red_out = red_out.reshape(splits, rows_per_dev, width)
    grad_w_out = jnp.zeros((rows_per_dev, width), jnp.float32)
    for src_part in range(splits):
        for j in range(splits):
            route = []
            for r in range(row_count):
                for g in range(groups):
                    src = r * seq_count + g * splits + src_part
                    dst = g * row_count * splits + r * splits + j
                    route.append((src, dst))
            grad_w_out = grad_w_out + lax.ppermute(red_out[j], ("row", "seq"), route)

    grad_tok = to_tokens(jnp.concatenate([grad_q_own, grad_k_own, grad_v_own], axis=1))
    grad_tok = grad_tok.reshape(groups, blk, 3, pw)
    gq_tok = jnp.transpose(grad_tok[:, :, 0], (1, 0, 2)).reshape(blk, width)
    gk_tok = jnp.transpose(grad_tok[:, :, 1], (1, 0, 2)).reshape(blk, width)
    gv_tok = jnp.transpose(grad_tok[:, :, 2], (1, 0, 2)).reshape(blk, width)
    grad_normed = (
        contract_cols(gq_tok, w_query) + contract_cols(gk_tok, w_key) + contract_cols(gv_tok, w_value)
    )
    gain_attn_part = jnp.sum(grad_normed * flat_in * scale_one, axis=0)
    scaled_one = grad_normed * gain_attn
    grad_inputs = (
        grad_middle
        + scale_one * scaled_one
        - flat_in * scale_one**3 * jnp.mean(scaled_one * flat_in, axis=-1, keepdims=True)
    )
    taps_full = lax.dynamic_update_slice_in_dim(
        jnp.zeros((HEADS, QCONV, KCONV), jnp.float32), grad_taps_part, pair * 2, 0
    )
    mix_full = lax.dynamic_update_slice_in_dim(
        jnp.zeros((groups, 2, 2), jnp.float32), grad_mix_part[None], pair, 0
    )
    small = jnp.concatenate([taps_full.reshape(-1), mix_full.reshape(-1), gain_ffn_part])
    small = jnp.sum(lax.all_gather(small, ("row", "seq"), axis=0, tiled=False), axis=0)
    gain_rows = width // (row_count * seq_count)
    gain_at = (row_index * seq_count + seq_index) * gain_rows
    grad_taps = small[: HEADS * TAPS].reshape(HEADS, QCONV, KCONV)
    grad_mix = small[HEADS * TAPS : HEADS * TAPS + groups * 4].reshape(groups, 2, 2)
    grad_gain_ffn = lax.dynamic_slice_in_dim(small, HEADS * TAPS + groups * 4 + gain_at, gain_rows, 0)
    grad_gain_attn = lax.psum_scatter(gain_attn_part, ("row", "seq"), scatter_dimension=0, tiled=True)
    return (
        outputs.reshape(row_dev, blk, width),
        grad_inputs.reshape(row_dev, blk, width),
        grad_w_query,
        grad_w_key,
        grad_w_value,
        grad_w_out,
        grad_gain_attn,
        grad_gain_ffn,
        grad_taps,
        grad_mix,
        grad_w_gate,
        grad_w_up,
        grad_w_down,
    )


def solution(mesh):
    return jax.shard_map(
        shards_body,
        mesh=mesh,
        in_specs=(
            P("row", "seq", None),
            P("row", None),
            P(),
            P(),
            P(),
            P(),
            P(),
            P(),
            P(),
            P(),
            P("row", "seq"),
            P("row", "seq"),
            P("seq", "row"),
            P("row", "seq", None),
        ),
        out_specs=(
            P("row", "seq", None),
            P("row", "seq", None),
            P(("row", "seq"), None),
            P(("row", "seq"), None),
            P(("row", "seq"), None),
            P(("row", "seq"), None),
            P(("row", "seq")),
            P(("row", "seq")),
            P(),
            P(),
            P("row", "seq"),
            P("row", "seq"),
            P("seq", "row"),
        ),
        check_vma=False,
    )
```

```python
import jax
import jax.numpy as jnp
from jax import lax
from jax.sharding import PartitionSpec as P
from jax.experimental import pallas as pl
from jax.experimental.pallas import tpu as pltpu

HEADS = 16
HD = 96
QCONV = 6
KCONV = 11
PAD = 8
TQ = 128
EXT = TQ + PAD
SCALE = HD ** (-0.5)
TAPS = QCONV * KCONV

epsilon = 1e-06


def rms_scale(values):
    return lax.rsqrt(jnp.mean(values * values, axis=-1, keepdims=True) + epsilon)


def project(values, weight):
    return jnp.dot(values, weight, preferred_element_type=jnp.float32)


def contract_rows(left, right):
    return lax.dot_general(
        left, right, (((0,), (0,)), ((), ())), preferred_element_type=jnp.float32
    )


def contract_cols(left, right):
    return lax.dot_general(
        left, right, (((1,), (1,)), ((), ())), preferred_element_type=jnp.float32
    )


def normed_pad_tail(values, extra):
    return jnp.pad(values, ((PAD, TQ * extra), (0, 0)))


def window_start(block, nw, length):
    return pl.multiple_of(jnp.clip((block - nw + 1) * TQ, 0, length - nw * TQ), TQ)


def tap_accumulate(sh_ref, acc_ref, taps_ref, head, width):
    cw = 256 if (width // 128) % 2 == 0 else 128

    def body(chunk, carry):
        r0 = pl.multiple_of(chunk * 8, 8)
        for c0 in range(0, width, cw):
            tiles = [sh_ref[b, pl.ds(r0, 8), pl.ds(c0, cw)] for b in range(KCONV)]
            for a in range(QCONV):
                base = head * TAPS + a * KCONV
                total = taps_ref[base] * tiles[0]
                for b in range(1, KCONV):
                    total = total + taps_ref[base + b] * tiles[b]
                acc_ref[a, pl.ds(r0, 8), pl.ds(c0, cw)] = total
        return carry

    lax.fori_loop(0, EXT // 8, body, 0)


def tap_products(sh_ref, g_ref, width):
    sums = {}
    for a0 in range(0, QCONV, 2):

        def body(chunk, accs):
            r0 = pl.multiple_of(chunk * 8, 8)
            out = list(accs)
            for c0 in range(0, width, 128):
                ga = [g_ref[a0 + k, pl.ds(r0, 8), pl.ds(c0, 128)] for k in range(2)]
                for b in range(KCONV):
                    tile = sh_ref[b, pl.ds(r0, 8), pl.ds(c0, 128)]
                    for k in range(2):
                        out[k * KCONV + b] = out[k * KCONV + b] + ga[k] * tile
            return tuple(out)

        start = tuple(jnp.zeros((8, 128), jnp.float32) for _ in range(2 * KCONV))
        res = lax.fori_loop(0, EXT // 8, body, start)
        for k in range(2):
            for b in range(KCONV):
                sums[(a0 + k, b)] = res[k * KCONV + b]
    return sums


def masks(block, kstart, width, rdoc_ref, kdoc_ref):
    keydoc = kdoc_ref[:, pl.ds(kstart, width)]
    ext_pos = block * TQ - PAD + lax.broadcasted_iota(jnp.int32, (EXT, width), 0)
    key_ext = kstart + lax.broadcasted_iota(jnp.int32, (EXT, width), 1)
    allowed_ext = (key_ext <= ext_pos) & (rdoc_ref[0] == keydoc)
    own_pos = block * TQ + lax.broadcasted_iota(jnp.int32, (TQ, width), 0)
    key_own = kstart + lax.broadcasted_iota(jnp.int32, (TQ, width), 1)
    allowed_own = (key_own <= own_pos) & (rdoc_ref[0, PAD:, :] == keydoc)
    return allowed_ext, allowed_own


def masked_shifts(q_ref, k_ref, head, kstart, width, allowed_ext, sh_ref):
    keys = k_ref[head, pl.ds(kstart, width), :]
    scores = lax.dot_general(
        q_ref[0, head], keys, (((1,), (1,)), ((), ())), preferred_element_type=jnp.float32
    ) * SCALE
    masked = jnp.where(allowed_ext, scores, 0.0)
    col = lax.broadcasted_iota(jnp.int32, (EXT, width), 1)
    sh_ref[0] = masked
    for b in range(1, KCONV):
        sh_ref[b] = jnp.where(col >= b, pltpu.roll(masked, b, 1), 0.0)


def fwd_kernel(toff_ref, taps_ref, mix_ref, q_ref, k_ref, v_ref, rdoc_ref, kdoc_ref,
               heads_ref, probs_ref, sh_ref, acc_ref, *, nw, length):
    width = nw * TQ
    block = toff_ref[0] + pl.program_id(0)
    kstart = window_start(block, nw, length)
    allowed_ext, allowed_own = masks(block, kstart, width, rdoc_ref, kdoc_ref)
    for head in range(2):
        masked_shifts(q_ref, k_ref, head, kstart, width, allowed_ext, sh_ref)
        tap_accumulate(sh_ref, acc_ref, taps_ref, head, width)
        conv = acc_ref[0]
        for a in range(1, QCONV):
            conv = conv + pltpu.roll(acc_ref[a], a, 0)
        logits = jnp.where(allowed_own, conv[PAD:], -jnp.inf)
        highest = jnp.max(logits, axis=1, keepdims=True)
        highest = jnp.where(highest > -jnp.inf, highest, 0.0)
        expd = jnp.exp(logits - highest)
        denom = jnp.sum(expd, axis=1, keepdims=True)
        probs_ref[0, head] = expd / jnp.where(denom > 0.0, denom, 1.0)
    p0 = probs_ref[0, 0]
    p1 = probs_ref[0, 1]
    for c in range(2):
        mixed = (mix_ref[2 * c] * p0 + mix_ref[2 * c + 1] * p1).astype(jnp.bfloat16)
        heads_ref[0, c] = jnp.dot(
            mixed, v_ref[c, pl.ds(kstart, width), :], preferred_element_type=jnp.float32
        ).astype(jnp.bfloat16)


def attention_forward(toff, taps_flat, mix_flat, q_blocks, k_heads, v_heads, row_docs, key_docs, nw, length):
    nb_all = q_blocks.shape[0]
    width = nw * TQ
    smem = pl.BlockSpec(memory_space=pltpu.SMEM)
    flops = nb_all * 2 * (4 * EXT * width * HD + 2 * TAPS * EXT * width)
    return pl.pallas_call(
        lambda *refs: fwd_kernel(*refs, nw=nw, length=length),
        grid=(nb_all,),
        in_specs=[
            smem,
            smem,
            smem,
            pl.BlockSpec((1, 2, EXT, HD), lambda t: (t, 0, 0, 0)),
            pl.BlockSpec((2, length, HD), lambda t: (0, 0, 0)),
            pl.BlockSpec((2, length, HD), lambda t: (0, 0, 0)),
            pl.BlockSpec((1, EXT, 1), lambda t: (t, 0, 0)),
            pl.BlockSpec((1, length), lambda t: (0, 0)),
        ],
        out_specs=[
            pl.BlockSpec((1, 2, TQ, HD), lambda t: (t, 0, 0, 0)),
            pl.BlockSpec((1, 2, TQ, width), lambda t: (t, 0, 0, 0)),
        ],
        out_shape=[
            jax.ShapeDtypeStruct((nb_all, 2, TQ, HD), jnp.bfloat16),
            jax.ShapeDtypeStruct((nb_all, 2, TQ, width), jnp.float32),
        ],
        scratch_shapes=[
            pltpu.VMEM((KCONV, EXT, width), jnp.float32),
            pltpu.VMEM((QCONV, EXT, width), jnp.float32),
        ],
        compiler_params=pltpu.CompilerParams(
            dimension_semantics=("arbitrary",), vmem_limit_bytes=56 * 1024 * 1024
        ),
        cost_estimate=pl.CostEstimate(
            flops=flops, transcendentals=nb_all * 2 * TQ * width,
            bytes_accessed=nb_all * 2 * TQ * width * 4 + 4 * length * HD * 2,
        ),
    )(toff, taps_flat, mix_flat, q_blocks, k_heads, v_heads, row_docs, key_docs)


def bwd_kernel(toff_ref, taps_ref, mix_ref, q_ref, qo_ref, k_ref, v_ref, rdoc_ref, kdoc_ref,
               probs_ref, gh_ref, ght_ref, gq_ref, gk_ref, gv_ref, tacc_ref, macc_ref,
               carry_ref, sh_ref, acc_ref, g_ref, gx_ref, *, nw, length, nb, nb_all):
    width = nw * TQ
    step = pl.program_id(0)
    local = nb_all - 1 - step
    block = toff_ref[0] + local
    kstart = window_start(block, nw, length)

    @pl.when(step == 0)
    def _init():
        gk_ref[...] = jnp.zeros(gk_ref.shape, jnp.float32)
        gv_ref[...] = jnp.zeros(gv_ref.shape, jnp.float32)
        tacc_ref[...] = jnp.zeros(tacc_ref.shape, jnp.float32)
        macc_ref[...] = jnp.zeros(macc_ref.shape, jnp.float32)
        carry_ref[...] = jnp.zeros(carry_ref.shape, jnp.float32)

    allowed_ext, allowed_own = masks(block, kstart, width, rdoc_ref, kdoc_ref)
    gm = [
        lax.dot_general(
            gh_ref[0, c], v_ref[c, pl.ds(kstart, width), :], (((1,), (1,)), ((), ())),
            preferred_element_type=jnp.float32,
        )
        for c in range(2)
    ]
    probs = [probs_ref[0, 0], probs_ref[0, 1]]
    gc = []
    for e in range(2):
        gp = mix_ref[e] * gm[0] + mix_ref[2 + e] * gm[1]
        inner = jnp.sum(gp * probs[e], axis=1, keepdims=True)
        gc.append(probs[e] * (gp - inner))

    def own_sums():
        for c in range(2):
            for e in range(2):
                macc_ref[pl.ds(2 * c + e, 1), :] += jnp.sum(gm[c] * probs[e], axis=0, keepdims=True)
            mixed = (mix_ref[2 * c] * probs[0] + mix_ref[2 * c + 1] * probs[1]).astype(jnp.bfloat16)
            gv_ref[c, :, pl.ds(kstart, width)] += jnp.dot(
                ght_ref[0, c], mixed, preferred_element_type=jnp.float32
            )

    def head_taps(e):
        masked_shifts(q_ref, k_ref, e, kstart, width, allowed_ext, sh_ref)
        gcp = jnp.concatenate([jnp.zeros((PAD, width), jnp.float32), gc[e]], axis=0)
        g_ref[0] = gcp
        for a in range(1, QCONV):
            g_ref[a] = pltpu.roll(gcp, EXT - a, 0)
        sums = tap_products(sh_ref, g_ref, width)
        for b in range(KCONV):
            for a in range(QCONV):
                tacc_ref[e * TAPS + a * KCONV + b] += sums[(a, b)]

    def head_keys(e, gs):
        gk_ref[e, :, pl.ds(kstart, width)] += jnp.dot(
            qo_ref[0, e], gs, preferred_element_type=jnp.float32
        ) * SCALE

    nxt = [carry_ref[e, :, pl.ds(kstart, width + TQ)] for e in range(2)]
    if nb < nb_all:
        pl.when(local < nb)(own_sums)
    else:
        own_sums()
    for e in range(2):
        if nb < nb_all:
            pl.when(local < nb)(lambda: head_taps(e))
        else:
            head_taps(e)
        gx_ref[pl.ds(0, TQ), pl.ds(0, width)] = gc[e]
        gx_ref[pl.ds(0, TQ), pl.ds(width, TQ)] = jnp.zeros((TQ, TQ), jnp.float32)
        gx_ref[pl.ds(TQ, PAD), :] = nxt[e]
        gxv = gx_ref[...]
        sh_ref[0] = gxv[:, :width]
        for b in range(1, KCONV):
            sh_ref[b] = pltpu.roll(gxv, width + TQ - b, 1)[:, :width]
        tap_accumulate(sh_ref, acc_ref, taps_ref, e, width)
        gmk = acc_ref[0]
        for a in range(1, QCONV):
            gmk = gmk + pltpu.roll(acc_ref[a], EXT - a, 0)
        gs = jnp.where(allowed_own, gmk[:TQ], 0.0).astype(jnp.bfloat16)
        gq_ref[0, e] = (
            jnp.dot(gs, k_ref[e, pl.ds(kstart, width), :], preferred_element_type=jnp.float32) * SCALE
        ).astype(jnp.bfloat16)
        if nb < nb_all:
            pl.when(local < nb)(lambda: head_keys(e, gs))
        else:
            head_keys(e, gs)
    carry_ref[...] = jnp.zeros(carry_ref.shape, jnp.float32)
    for e in range(2):
        carry_ref[e, :, pl.ds(kstart, width)] = gc[e][:PAD]


def attention_backward(toff, taps_flat, mix_flat, q_blocks, q_own, k_heads, v_heads, row_docs, key_docs,
                       probs_blk, gh_blocks, nw, length, nb):
    q_own = jnp.swapaxes(q_own, 2, 3)
    gh_t = jnp.swapaxes(gh_blocks, 2, 3)
    nb_all = q_blocks.shape[0]
    width = nw * TQ
    smem = pl.BlockSpec(memory_space=pltpu.SMEM)
    rev = lambda s: nb_all - 1 - s
    flops = nb_all * 2 * (8 * TQ * width * HD + 6 * TAPS * EXT * width)
    return pl.pallas_call(
        lambda *refs: bwd_kernel(*refs, nw=nw, length=length, nb=nb, nb_all=nb_all),
        grid=(nb_all,),
        in_specs=[
            smem,
            smem,
            smem,
            pl.BlockSpec((1, 2, EXT, HD), lambda s: (rev(s), 0, 0, 0)),
            pl.BlockSpec((1, 2, HD, TQ), lambda s: (rev(s), 0, 0, 0)),
            pl.BlockSpec((2, length, HD), lambda s: (0, 0, 0)),
            pl.BlockSpec((2, length, HD), lambda s: (0, 0, 0)),
            pl.BlockSpec((1, EXT, 1), lambda s: (rev(s), 0, 0)),
            pl.BlockSpec((1, length), lambda s: (0, 0)),
            pl.BlockSpec((1, 2, TQ, width), lambda s: (rev(s), 0, 0, 0)),
            pl.BlockSpec((1, 2, TQ, HD), lambda s: (rev(s), 0, 0, 0)),
            pl.BlockSpec((1, 2, HD, TQ), lambda s: (rev(s), 0, 0, 0)),
        ],
        out_specs=[
            pl.BlockSpec((1, 2, TQ, HD), lambda s: (rev(s), 0, 0, 0)),
            pl.BlockSpec((2, HD, length), lambda s: (0, 0, 0)),
            pl.BlockSpec((2, HD, length), lambda s: (0, 0, 0)),
            pl.BlockSpec((2 * TAPS, 8, 128), lambda s: (0, 0, 0)),
            pl.BlockSpec((4, width), lambda s: (0, 0)),
        ],
        out_shape=[
            jax.ShapeDtypeStruct((nb_all, 2, TQ, HD), jnp.bfloat16),
            jax.ShapeDtypeStruct((2, HD, length), jnp.float32),
            jax.ShapeDtypeStruct((2, HD, length), jnp.float32),
            jax.ShapeDtypeStruct((2 * TAPS, 8, 128), jnp.float32),
            jax.ShapeDtypeStruct((4, width), jnp.float32),
        ],
        scratch_shapes=[
            pltpu.VMEM((2, PAD, length + TQ), jnp.float32),
            pltpu.VMEM((KCONV, EXT, width), jnp.float32),
            pltpu.VMEM((QCONV, EXT, width), jnp.float32),
            pltpu.VMEM((QCONV, EXT, width), jnp.float32),
            pltpu.VMEM((EXT, width + TQ), jnp.float32),
        ],
        compiler_params=pltpu.CompilerParams(
            dimension_semantics=("arbitrary",), vmem_limit_bytes=60 * 1024 * 1024
        ),
        cost_estimate=pl.CostEstimate(
            flops=flops, transcendentals=0,
            bytes_accessed=nb_all * 2 * TQ * width * 4 + 8 * length * HD * 4,
        ),
    )(toff, taps_flat, mix_flat, q_blocks, q_own, k_heads, v_heads, row_docs, key_docs, probs_blk, gh_blocks, gh_t)


def shards_body(
    inputs,
    doc_ids,
    w_query,
    w_key,
    w_value,
    w_out,
    gain_attn,
    gain_ffn,
    conv_taps,
    head_mix,
    w_gate,
    w_up,
    w_down,
    cotangent,
):
    row_dev, blk, width = inputs.shape
    assert row_dev == 1
    seq_count = lax.axis_size("seq")
    row_count = lax.axis_size("row")
    seq_index = lax.axis_index("seq")
    row_index = lax.axis_index("row")
    length = blk * seq_count
    groups = HEADS // 2
    assert seq_count % groups == 0
    splits = seq_count // groups
    span = length // splits
    pw = 2 * HD
    pair = seq_index // splits
    part = seq_index % splits
    q0 = part * span

    flat_in = inputs.reshape(blk, width)
    scale_one = rms_scale(flat_in)
    normed = (flat_in * scale_one * gain_attn).astype(jnp.bfloat16)
    normed_all = lax.all_gather(normed, "seq", axis=0, tiled=True)

    wq_g = lax.dynamic_slice_in_dim(w_query, pair * pw, pw, 1)
    wk_g = lax.dynamic_slice_in_dim(w_key, pair * pw, pw, 1)
    wv_g = lax.dynamic_slice_in_dim(w_value, pair * pw, pw, 1)
    wo_g = lax.dynamic_slice_in_dim(w_out, pair * pw, pw, 0)
    taps = lax.dynamic_slice_in_dim(conv_taps, pair * 2, 2, 0)
    mixing = lax.dynamic_index_in_dim(head_mix, pair, 0, keepdims=False)

    k_all = project(normed_all, wk_g).astype(jnp.bfloat16)
    v_all = project(normed_all, wv_g).astype(jnp.bfloat16)
    k3 = k_all.reshape(length, 2, HD)
    v3 = v_all.reshape(length, 2, HD)

    docs = doc_ids[0]
    nb = span // TQ
    extra = 1 if splits > 1 else 0
    nb_all = nb + extra
    doc_cap = length // 2
    nw = min(length // TQ, (doc_cap + QCONV - 2 + TQ - 1) // TQ + 1)
    q_tail = normed_pad_tail(normed_all, extra)
    q_rows = project(lax.dynamic_slice_in_dim(q_tail, q0, nb_all * TQ + PAD, 0), wq_g).astype(jnp.bfloat16)
    q_blocks = jnp.stack([q_rows[t * TQ : t * TQ + EXT] for t in range(nb_all)])
    q_blocks = jnp.transpose(q_blocks.reshape(nb_all, EXT, 2, HD), (0, 2, 1, 3))
    q_own = q_blocks[:, :, PAD:]
    k_heads = jnp.transpose(k3, (1, 0, 2))
    v_heads = jnp.transpose(v3, (1, 0, 2))
    docs_tail = jnp.pad(docs, (PAD, TQ * extra), constant_values=-1)
    doc_rows = lax.dynamic_slice_in_dim(docs_tail, q0, nb_all * TQ + PAD, 0)
    row_docs = jnp.stack([doc_rows[t * TQ : t * TQ + EXT] for t in range(nb_all)])[:, :, None]
    key_docs = docs[None, :]
    toff = (q0 // TQ).astype(jnp.int32).reshape(1)
    taps_flat = taps.reshape(2 * QCONV * KCONV)
    mix_flat = mixing.reshape(4)
    heads_blk, probs_blk = attention_forward(
        toff, taps_flat, mix_flat, q_blocks, k_heads, v_heads, row_docs, key_docs, nw, length
    )
    heads_own = jnp.transpose(heads_blk[:nb], (0, 2, 1, 3)).reshape(span, pw)

    def to_tokens(values):
        cols = values.shape[1]
        if splits == 1:
            full = values
        else:
            full = lax.dynamic_update_slice_in_dim(
                jnp.zeros((length, cols), values.dtype), values, q0, 0
            )
        got = lax.all_to_all(full, "seq", 0, 0, tiled=True)
        got = got.reshape(groups, splits, blk, cols)
        if splits > 1:
            got = jnp.sum(got.astype(jnp.float32), axis=1).astype(values.dtype)
        else:
            got = got[:, 0]
        return got

    heads_tok = jnp.transpose(to_tokens(heads_own), (1, 0, 2)).reshape(blk, width)
    middle = flat_in + project(heads_tok, w_out)
    scale_two = rms_scale(middle)
    normed_ffn = (middle * scale_two * gain_ffn).astype(jnp.bfloat16)
    gate_full = lax.all_gather(w_gate, "row", axis=0, tiled=True)
    up_full = lax.all_gather(w_up, "row", axis=0, tiled=True)
    down_full = lax.all_gather(w_down, "row", axis=1, tiled=True)
    hid_width = gate_full.shape[1]
    joint = jnp.concatenate([gate_full, up_full], axis=1)
    ffn_rows = lax.all_gather(normed_ffn, "seq", axis=0, tiled=True)
    gate_up = project(ffn_rows, joint)
    gate_vals = gate_up[:, :hid_width]
    up_vals = gate_up[:, hid_width:]
    hidden = (jax.nn.silu(gate_vals) * up_vals).astype(jnp.bfloat16)
    ffn_part = project(hidden, down_full).astype(jnp.bfloat16)
    cot_flat = cotangent.reshape(blk, width)
    cot_low = cot_flat.astype(jnp.bfloat16)
    cot_rows = lax.all_gather(cot_low, "seq", axis=0, tiled=True)
    grad_hidden = contract_cols(cot_rows, down_full)
    grad_down_part = contract_rows(hidden, cot_rows)
    sigmoid_gate = jax.nn.sigmoid(gate_vals)
    grad_gate_vals = grad_hidden * up_vals * sigmoid_gate * (1.0 + gate_vals * (1.0 - sigmoid_gate))
    grad_up_vals = grad_hidden * gate_vals * sigmoid_gate
    grad_joint = jnp.concatenate([grad_gate_vals, grad_up_vals], axis=1).astype(jnp.bfloat16)
    grad_joint_w = contract_rows(ffn_rows, grad_joint)
    grad_normed_ffn = lax.psum_scatter(
        contract_cols(grad_joint, joint).astype(jnp.bfloat16),
        "seq",
        scatter_dimension=0,
        tiled=True,
    ).astype(jnp.float32)
    grad_w_gate, grad_w_up, grad_w_down = (
        lax.psum_scatter(
            grad_joint_w[:, :hid_width].astype(jnp.bfloat16), "row", scatter_dimension=0, tiled=True
        ).astype(jnp.float32),
        lax.psum_scatter(
            grad_joint_w[:, hid_width:].astype(jnp.bfloat16), "row", scatter_dimension=0, tiled=True
        ).astype(jnp.float32),
        lax.psum_scatter(
            grad_down_part.astype(jnp.bfloat16), "row", scatter_dimension=1, tiled=True
        ).astype(jnp.float32),
    )
    gain_ffn_part = jnp.sum(grad_normed_ffn * middle * scale_two, axis=0)
    scaled_two = grad_normed_ffn * gain_ffn
    grad_middle = (
        cot_flat
        + scale_two * scaled_two
        - middle * scale_two**3 * jnp.mean(scaled_two * middle, axis=-1, keepdims=True)
    )
    grad_attn = grad_middle.astype(jnp.bfloat16)
    grad_attn_all = lax.all_gather(grad_attn, "seq", axis=0, tiled=True)
    ffn_part, grad_attn_all = lax.optimization_barrier((ffn_part, grad_attn_all))
    ffn_out = lax.psum_scatter(ffn_part, "seq", scatter_dimension=0, tiled=True).astype(jnp.float32)
    outputs = middle + ffn_out
    grad_attn_tail = jnp.pad(grad_attn_all, ((0, TQ * extra), (0, 0)))
    grad_heads_x = contract_cols(
        lax.dynamic_slice_in_dim(grad_attn_tail, q0, nb_all * TQ, 0), wo_g
    ).astype(jnp.bfloat16)
    gh_blocks = jnp.transpose(grad_heads_x.reshape(nb_all, TQ, 2, HD), (0, 2, 1, 3))
    grad_out_part = contract_rows(heads_own, lax.dynamic_slice_in_dim(grad_attn_all, q0, span, 0))
    gq_blk, gk_heads, gv_heads, tap_acc, mix_acc = attention_backward(
        toff, taps_flat, mix_flat, q_blocks, q_own, k_heads, v_heads, row_docs, key_docs,
        probs_blk, gh_blocks, nw, length, nb,
    )
    grad_q_own = jnp.transpose(gq_blk[:nb], (0, 2, 1, 3)).reshape(span, pw)
    grad_k_part = jnp.transpose(gk_heads, (2, 0, 1)).reshape(length, pw)
    grad_v_part = jnp.transpose(gv_heads, (2, 0, 1)).reshape(length, pw)
    grad_taps_part = jnp.sum(tap_acc, axis=(1, 2)).reshape(2, QCONV, KCONV)
    grad_mix_part = jnp.sum(mix_acc, axis=1).reshape(2, 2)

    def split_sum(values):
        if splits == 1:
            return values
        total = values
        for step in range(1, splits):
            route = []
            for s in range(seq_count):
                base = (s // splits) * splits
                route.append((s, base + (s - base + step) % splits))
            total = total + lax.ppermute(values, "seq", route)
        return total

    grad_k_low = split_sum(grad_k_part).astype(jnp.bfloat16)
    grad_v_low = split_sum(grad_v_part).astype(jnp.bfloat16)
    grad_k_own = lax.dynamic_slice_in_dim(grad_k_low, q0, span, 0)
    grad_v_own = lax.dynamic_slice_in_dim(grad_v_low, q0, span, 0)

    normed_own = lax.dynamic_slice_in_dim(normed_all, q0, span, 0)
    rows_per_dev = width // (row_count * seq_count)

    partials = jnp.stack(
        [
            contract_rows(normed_own, grad_q_own),
            contract_rows(normed_own, grad_k_own),
            contract_rows(normed_own, grad_v_own),
        ]
    )
    red = lax.psum_scatter(partials, "row", scatter_dimension=1, tiled=True)
    got = lax.all_to_all(red, "seq", 1, 1, tiled=True)
    got = got.reshape(3, groups, splits, rows_per_dev, pw).sum(axis=2)
    got = jnp.transpose(got, (0, 2, 1, 3)).reshape(3, rows_per_dev, width)
    grad_w_query, grad_w_key, grad_w_value = got[0], got[1], got[2]

    red_out = lax.psum_scatter(grad_out_part, "row", scatter_dimension=0, tiled=True)
    red_out = red_out.reshape(splits, rows_per_dev, width)
    grad_w_out = jnp.zeros((rows_per_dev, width), jnp.float32)
    for src_part in range(splits):
        for j in range(splits):
            route = []
            for r in range(row_count):
                for g in range(groups):
                    src = r * seq_count + g * splits + src_part
                    dst = g * row_count * splits + r * splits + j
                    route.append((src, dst))
            grad_w_out = grad_w_out + lax.ppermute(red_out[j], ("row", "seq"), route)

    grad_tok = to_tokens(jnp.concatenate([grad_q_own, grad_k_own, grad_v_own], axis=1))
    grad_tok = grad_tok.reshape(groups, blk, 3, pw)
    gq_tok = jnp.transpose(grad_tok[:, :, 0], (1, 0, 2)).reshape(blk, width)
    gk_tok = jnp.transpose(grad_tok[:, :, 1], (1, 0, 2)).reshape(blk, width)
    gv_tok = jnp.transpose(grad_tok[:, :, 2], (1, 0, 2)).reshape(blk, width)
    grad_normed = (
        contract_cols(gq_tok, w_query) + contract_cols(gk_tok, w_key) + contract_cols(gv_tok, w_value)
    )
    gain_attn_part = jnp.sum(grad_normed * flat_in * scale_one, axis=0)
    scaled_one = grad_normed * gain_attn
    grad_inputs = (
        grad_middle
        + scale_one * scaled_one
        - flat_in * scale_one**3 * jnp.mean(scaled_one * flat_in, axis=-1, keepdims=True)
    )
    taps_full = lax.dynamic_update_slice_in_dim(
        jnp.zeros((HEADS, QCONV, KCONV), jnp.float32), grad_taps_part, pair * 2, 0
    )
    mix_full = lax.dynamic_update_slice_in_dim(
        jnp.zeros((groups, 2, 2), jnp.float32), grad_mix_part[None], pair, 0
    )
    small = jnp.concatenate(
        [gain_attn_part, gain_ffn_part, taps_full.reshape(-1), mix_full.reshape(-1)]
    )
    small = lax.psum(small, ("row", "seq"))
    gain_rows = width // (row_count * seq_count)
    gain_at = (row_index * seq_count + seq_index) * gain_rows
    grad_gain_attn = lax.dynamic_slice_in_dim(small, gain_at, gain_rows, 0)
    grad_gain_ffn = lax.dynamic_slice_in_dim(small, width + gain_at, gain_rows, 0)
    grad_taps = small[2 * width : 2 * width + HEADS * TAPS].reshape(HEADS, QCONV, KCONV)
    grad_mix = small[2 * width + HEADS * TAPS :].reshape(groups, 2, 2)
    return (
        outputs.reshape(row_dev, blk, width),
        grad_inputs.reshape(row_dev, blk, width),
        grad_w_query,
        grad_w_key,
        grad_w_value,
        grad_w_out,
        grad_gain_attn,
        grad_gain_ffn,
        grad_taps,
        grad_mix,
        grad_w_gate,
        grad_w_up,
        grad_w_down,
    )


def solution(mesh):
    return jax.shard_map(
        shards_body,
        mesh=mesh,
        in_specs=(
            P("row", "seq", None),
            P("row", None),
            P(),
            P(),
            P(),
            P(),
            P(),
            P(),
            P(),
            P(),
            P("row", "seq"),
            P("row", "seq"),
            P("seq", "row"),
            P("row", "seq", None),
        ),
        out_specs=(
            P("row", "seq", None),
            P("row", "seq", None),
            P(("row", "seq"), None),
            P(("row", "seq"), None),
            P(("row", "seq"), None),
            P(("row", "seq"), None),
            P(("row", "seq")),
            P(("row", "seq")),
            P(),
            P(),
            P("row", "seq"),
            P("row", "seq"),
            P("seq", "row"),
        ),
        check_vma=False,
    )
```

```python
import jax
import jax.numpy as jnp
from jax import lax
from jax.sharding import PartitionSpec as P
from jax.experimental import pallas as pl
from jax.experimental.pallas import tpu as pltpu

HEADS = 16
HD = 96
QCONV = 6
KCONV = 11
PAD = 8
TQ = 128
EXT = TQ + PAD
SCALE = HD ** (-0.5)
TAPS = QCONV * KCONV

epsilon = 1e-06


def rms_scale(values):
    return lax.rsqrt(jnp.mean(values * values, axis=-1, keepdims=True) + epsilon)


def project(values, weight):
    return jnp.dot(values, weight, preferred_element_type=jnp.float32)


def contract_rows(left, right):
    return lax.dot_general(
        left, right, (((0,), (0,)), ((), ())), preferred_element_type=jnp.float32
    )


def contract_cols(left, right):
    return lax.dot_general(
        left, right, (((1,), (1,)), ((), ())), preferred_element_type=jnp.float32
    )


def normed_pad_tail(values, extra):
    return jnp.pad(values, ((PAD, TQ * extra), (0, 0)))


def window_start(block, nw, length):
    return pl.multiple_of(jnp.clip((block - nw + 1) * TQ, 0, length - nw * TQ), TQ)


def tap_accumulate(sh_ref, acc_ref, taps_ref, head, width):
    cw = 256 if (width // 128) % 2 == 0 else 128

    def body(chunk, carry):
        r0 = pl.multiple_of(chunk * 8, 8)
        for c0 in range(0, width, cw):
            tiles = [sh_ref[b, pl.ds(r0, 8), pl.ds(c0, cw)] for b in range(KCONV)]
            for a in range(QCONV):
                base = head * TAPS + a * KCONV
                total = taps_ref[base] * tiles[0]
                for b in range(1, KCONV):
                    total = total + taps_ref[base + b] * tiles[b]
                acc_ref[a, pl.ds(r0, 8), pl.ds(c0, cw)] = total
        return carry

    lax.fori_loop(0, EXT // 8, body, 0)


def tap_products(sh_ref, g_ref, width):
    sums = {}
    for a0 in range(0, QCONV, 2):

        def body(chunk, accs):
            r0 = pl.multiple_of(chunk * 8, 8)
            out = list(accs)
            for c0 in range(0, width, 128):
                ga = [g_ref[a0 + k, pl.ds(r0, 8), pl.ds(c0, 128)] for k in range(2)]
                for b in range(KCONV):
                    tile = sh_ref[b, pl.ds(r0, 8), pl.ds(c0, 128)]
                    for k in range(2):
                        out[k * KCONV + b] = out[k * KCONV + b] + ga[k] * tile
            return tuple(out)

        start = tuple(jnp.zeros((8, 128), jnp.float32) for _ in range(2 * KCONV))
        res = lax.fori_loop(0, EXT // 8, body, start)
        for k in range(2):
            for b in range(KCONV):
                sums[(a0 + k, b)] = res[k * KCONV + b]
    return sums


def masks(block, kstart, width, rdoc_ref, kdoc_ref):
    keydoc = kdoc_ref[:, pl.ds(kstart, width)]
    ext_pos = block * TQ - PAD + lax.broadcasted_iota(jnp.int32, (EXT, width), 0)
    key_ext = kstart + lax.broadcasted_iota(jnp.int32, (EXT, width), 1)
    allowed_ext = (key_ext <= ext_pos) & (rdoc_ref[0] == keydoc)
    own_pos = block * TQ + lax.broadcasted_iota(jnp.int32, (TQ, width), 0)
    key_own = kstart + lax.broadcasted_iota(jnp.int32, (TQ, width), 1)
    allowed_own = (key_own <= own_pos) & (rdoc_ref[0, PAD:, :] == keydoc)
    return allowed_ext, allowed_own


def masked_shifts(q_ref, k_ref, head, kstart, width, allowed_ext, sh_ref):
    keys = k_ref[head, pl.ds(kstart, width), :]
    scores = lax.dot_general(
        q_ref[0, head], keys, (((1,), (1,)), ((), ())), preferred_element_type=jnp.float32
    ) * SCALE
    masked = jnp.where(allowed_ext, scores, 0.0)
    col = lax.broadcasted_iota(jnp.int32, (EXT, width), 1)
    sh_ref[0] = masked
    for b in range(1, KCONV):
        sh_ref[b] = jnp.where(col >= b, pltpu.roll(masked, b, 1), 0.0)


def fwd_kernel(toff_ref, taps_ref, mix_ref, q_ref, k_ref, v_ref, rdoc_ref, kdoc_ref,
               heads_ref, probs_ref, sh_ref, acc_ref, *, nw, length):
    width = nw * TQ
    block = toff_ref[0] + pl.program_id(0)
    kstart = window_start(block, nw, length)
    allowed_ext, allowed_own = masks(block, kstart, width, rdoc_ref, kdoc_ref)
    for head in range(2):
        masked_shifts(q_ref, k_ref, head, kstart, width, allowed_ext, sh_ref)
        tap_accumulate(sh_ref, acc_ref, taps_ref, head, width)
        conv = acc_ref[0]
        for a in range(1, QCONV):
            conv = conv + pltpu.roll(acc_ref[a], a, 0)
        logits = jnp.where(allowed_own, conv[PAD:], -jnp.inf)
        highest = jnp.max(logits, axis=1, keepdims=True)
        highest = jnp.where(highest > -jnp.inf, highest, 0.0)
        expd = jnp.exp(logits - highest)
        denom = jnp.sum(expd, axis=1, keepdims=True)
        probs_ref[0, head] = expd / jnp.where(denom > 0.0, denom, 1.0)
    p0 = probs_ref[0, 0]
    p1 = probs_ref[0, 1]
    for c in range(2):
        mixed = (mix_ref[2 * c] * p0 + mix_ref[2 * c + 1] * p1).astype(jnp.bfloat16)
        heads_ref[0, c] = jnp.dot(
            mixed, v_ref[c, pl.ds(kstart, width), :], preferred_element_type=jnp.float32
        ).astype(jnp.bfloat16)


def attention_forward(toff, taps_flat, mix_flat, q_blocks, k_heads, v_heads, row_docs, key_docs, nw, length):
    nb_all = q_blocks.shape[0]
    width = nw * TQ
    smem = pl.BlockSpec(memory_space=pltpu.SMEM)
    flops = nb_all * 2 * (4 * EXT * width * HD + 2 * TAPS * EXT * width)
    return pl.pallas_call(
        lambda *refs: fwd_kernel(*refs, nw=nw, length=length),
        grid=(nb_all,),
        in_specs=[
            smem,
            smem,
            smem,
            pl.BlockSpec((1, 2, EXT, HD), lambda t: (t, 0, 0, 0)),
            pl.BlockSpec((2, length, HD), lambda t: (0, 0, 0)),
            pl.BlockSpec((2, length, HD), lambda t: (0, 0, 0)),
            pl.BlockSpec((1, EXT, 1), lambda t: (t, 0, 0)),
            pl.BlockSpec((1, length), lambda t: (0, 0)),
        ],
        out_specs=[
            pl.BlockSpec((1, 2, TQ, HD), lambda t: (t, 0, 0, 0)),
            pl.BlockSpec((1, 2, TQ, width), lambda t: (t, 0, 0, 0)),
        ],
        out_shape=[
            jax.ShapeDtypeStruct((nb_all, 2, TQ, HD), jnp.bfloat16),
            jax.ShapeDtypeStruct((nb_all, 2, TQ, width), jnp.float32),
        ],
        scratch_shapes=[
            pltpu.VMEM((KCONV, EXT, width), jnp.float32),
            pltpu.VMEM((QCONV, EXT, width), jnp.float32),
        ],
        compiler_params=pltpu.CompilerParams(
            dimension_semantics=("arbitrary",), vmem_limit_bytes=56 * 1024 * 1024
        ),
        cost_estimate=pl.CostEstimate(
            flops=flops, transcendentals=nb_all * 2 * TQ * width,
            bytes_accessed=nb_all * 2 * TQ * width * 4 + 4 * length * HD * 2,
        ),
    )(toff, taps_flat, mix_flat, q_blocks, k_heads, v_heads, row_docs, key_docs)


def bwd_kernel(toff_ref, taps_ref, mix_ref, q_ref, qo_ref, k_ref, v_ref, rdoc_ref, kdoc_ref,
               probs_ref, gh_ref, ght_ref, gq_ref, gk_ref, gv_ref, tacc_ref, macc_ref,
               carry_ref, sh_ref, acc_ref, g_ref, gx_ref, *, nw, length, nb, nb_all):
    width = nw * TQ
    step = pl.program_id(0)
    local = nb_all - 1 - step
    block = toff_ref[0] + local
    kstart = window_start(block, nw, length)

    @pl.when(step == 0)
    def _init():
        gk_ref[...] = jnp.zeros(gk_ref.shape, jnp.float32)
        gv_ref[...] = jnp.zeros(gv_ref.shape, jnp.float32)
        tacc_ref[...] = jnp.zeros(tacc_ref.shape, jnp.float32)
        macc_ref[...] = jnp.zeros(macc_ref.shape, jnp.float32)
        carry_ref[...] = jnp.zeros(carry_ref.shape, jnp.float32)

    allowed_ext, allowed_own = masks(block, kstart, width, rdoc_ref, kdoc_ref)
    gm = [
        lax.dot_general(
            gh_ref[0, c], v_ref[c, pl.ds(kstart, width), :], (((1,), (1,)), ((), ())),
            preferred_element_type=jnp.float32,
        )
        for c in range(2)
    ]
    probs = [probs_ref[0, 0], probs_ref[0, 1]]
    gc = []
    for e in range(2):
        gp = mix_ref[e] * gm[0] + mix_ref[2 + e] * gm[1]
        inner = jnp.sum(gp * probs[e], axis=1, keepdims=True)
        gc.append(probs[e] * (gp - inner))

    def own_sums():
        for c in range(2):
            for e in range(2):
                macc_ref[pl.ds(2 * c + e, 1), :] += jnp.sum(gm[c] * probs[e], axis=0, keepdims=True)
            mixed = (mix_ref[2 * c] * probs[0] + mix_ref[2 * c + 1] * probs[1]).astype(jnp.bfloat16)
            gv_ref[c, :, pl.ds(kstart, width)] += jnp.dot(
                ght_ref[0, c], mixed, preferred_element_type=jnp.float32
            )

    def head_taps(e):
        masked_shifts(q_ref, k_ref, e, kstart, width, allowed_ext, sh_ref)
        gcp = jnp.concatenate([jnp.zeros((PAD, width), jnp.float32), gc[e]], axis=0)
        g_ref[0] = gcp
        for a in range(1, QCONV):
            g_ref[a] = pltpu.roll(gcp, EXT - a, 0)
        sums = tap_products(sh_ref, g_ref, width)
        for b in range(KCONV):
            for a in range(QCONV):
                tacc_ref[e * TAPS + a * KCONV + b] += sums[(a, b)]

    def head_keys(e, gs):
        gk_ref[e, :, pl.ds(kstart, width)] += jnp.dot(
            qo_ref[0, e], gs, preferred_element_type=jnp.float32
        ) * SCALE

    nxt = [carry_ref[e, :, pl.ds(kstart, width + TQ)] for e in range(2)]
    if nb < nb_all:
        pl.when(local < nb)(own_sums)
    else:
        own_sums()
    for e in range(2):
        if nb < nb_all:
            pl.when(local < nb)(lambda: head_taps(e))
        else:
            head_taps(e)
        gx_ref[pl.ds(0, TQ), pl.ds(0, width)] = gc[e]
        gx_ref[pl.ds(0, TQ), pl.ds(width, TQ)] = jnp.zeros((TQ, TQ), jnp.float32)
        gx_ref[pl.ds(TQ, PAD), :] = nxt[e]
        gxv = gx_ref[...]
        sh_ref[0] = gxv[:, :width]
        for b in range(1, KCONV):
            sh_ref[b] = pltpu.roll(gxv, width + TQ - b, 1)[:, :width]
        tap_accumulate(sh_ref, acc_ref, taps_ref, e, width)
        gmk = acc_ref[0]
        for a in range(1, QCONV):
            gmk = gmk + pltpu.roll(acc_ref[a], EXT - a, 0)
        gs = jnp.where(allowed_own, gmk[:TQ], 0.0).astype(jnp.bfloat16)
        gq_ref[0, e] = (
            jnp.dot(gs, k_ref[e, pl.ds(kstart, width), :], preferred_element_type=jnp.float32) * SCALE
        ).astype(jnp.bfloat16)
        if nb < nb_all:
            pl.when(local < nb)(lambda: head_keys(e, gs))
        else:
            head_keys(e, gs)
    carry_ref[...] = jnp.zeros(carry_ref.shape, jnp.float32)
    for e in range(2):
        carry_ref[e, :, pl.ds(kstart, width)] = gc[e][:PAD]


def attention_backward(toff, taps_flat, mix_flat, q_blocks, q_own, k_heads, v_heads, row_docs, key_docs,
                       probs_blk, gh_blocks, nw, length, nb):
    q_own = jnp.swapaxes(q_own, 2, 3)
    gh_t = jnp.swapaxes(gh_blocks, 2, 3)
    nb_all = q_blocks.shape[0]
    width = nw * TQ
    smem = pl.BlockSpec(memory_space=pltpu.SMEM)
    rev = lambda s: nb_all - 1 - s
    flops = nb_all * 2 * (8 * TQ * width * HD + 6 * TAPS * EXT * width)
    return pl.pallas_call(
        lambda *refs: bwd_kernel(*refs, nw=nw, length=length, nb=nb, nb_all=nb_all),
        grid=(nb_all,),
        in_specs=[
            smem,
            smem,
            smem,
            pl.BlockSpec((1, 2, EXT, HD), lambda s: (rev(s), 0, 0, 0)),
            pl.BlockSpec((1, 2, HD, TQ), lambda s: (rev(s), 0, 0, 0)),
            pl.BlockSpec((2, length, HD), lambda s: (0, 0, 0)),
            pl.BlockSpec((2, length, HD), lambda s: (0, 0, 0)),
            pl.BlockSpec((1, EXT, 1), lambda s: (rev(s), 0, 0)),
            pl.BlockSpec((1, length), lambda s: (0, 0)),
            pl.BlockSpec((1, 2, TQ, width), lambda s: (rev(s), 0, 0, 0)),
            pl.BlockSpec((1, 2, TQ, HD), lambda s: (rev(s), 0, 0, 0)),
            pl.BlockSpec((1, 2, HD, TQ), lambda s: (rev(s), 0, 0, 0)),
        ],
        out_specs=[
            pl.BlockSpec((1, 2, TQ, HD), lambda s: (rev(s), 0, 0, 0)),
            pl.BlockSpec((2, HD, length), lambda s: (0, 0, 0)),
            pl.BlockSpec((2, HD, length), lambda s: (0, 0, 0)),
            pl.BlockSpec((2 * TAPS, 8, 128), lambda s: (0, 0, 0)),
            pl.BlockSpec((4, width), lambda s: (0, 0)),
        ],
        out_shape=[
            jax.ShapeDtypeStruct((nb_all, 2, TQ, HD), jnp.bfloat16),
            jax.ShapeDtypeStruct((2, HD, length), jnp.float32),
            jax.ShapeDtypeStruct((2, HD, length), jnp.float32),
            jax.ShapeDtypeStruct((2 * TAPS, 8, 128), jnp.float32),
            jax.ShapeDtypeStruct((4, width), jnp.float32),
        ],
        scratch_shapes=[
            pltpu.VMEM((2, PAD, length + TQ), jnp.float32),
            pltpu.VMEM((KCONV, EXT, width), jnp.float32),
            pltpu.VMEM((QCONV, EXT, width), jnp.float32),
            pltpu.VMEM((QCONV, EXT, width), jnp.float32),
            pltpu.VMEM((EXT, width + TQ), jnp.float32),
        ],
        compiler_params=pltpu.CompilerParams(
            dimension_semantics=("arbitrary",), vmem_limit_bytes=60 * 1024 * 1024
        ),
        cost_estimate=pl.CostEstimate(
            flops=flops, transcendentals=0,
            bytes_accessed=nb_all * 2 * TQ * width * 4 + 8 * length * HD * 4,
        ),
    )(toff, taps_flat, mix_flat, q_blocks, q_own, k_heads, v_heads, row_docs, key_docs, probs_blk, gh_blocks, gh_t)


def shards_body(
    inputs,
    doc_ids,
    w_query,
    w_key,
    w_value,
    w_out,
    gain_attn,
    gain_ffn,
    conv_taps,
    head_mix,
    w_gate,
    w_up,
    w_down,
    cotangent,
):
    row_dev, blk, width = inputs.shape
    assert row_dev == 1
    seq_count = lax.axis_size("seq")
    row_count = lax.axis_size("row")
    seq_index = lax.axis_index("seq")
    row_index = lax.axis_index("row")
    length = blk * seq_count
    groups = HEADS // 2
    assert seq_count % groups == 0
    splits = seq_count // groups
    span = length // splits
    pw = 2 * HD
    pair = seq_index // splits
    part = seq_index % splits
    q0 = part * span

    flat_in = inputs.reshape(blk, width)
    scale_one = rms_scale(flat_in)
    normed = (flat_in * scale_one * gain_attn).astype(jnp.bfloat16)
    normed_all = lax.all_gather(normed, "seq", axis=0, tiled=True)

    wq_g = lax.dynamic_slice_in_dim(w_query, pair * pw, pw, 1)
    wk_g = lax.dynamic_slice_in_dim(w_key, pair * pw, pw, 1)
    wv_g = lax.dynamic_slice_in_dim(w_value, pair * pw, pw, 1)
    wo_g = lax.dynamic_slice_in_dim(w_out, pair * pw, pw, 0)
    taps = lax.dynamic_slice_in_dim(conv_taps, pair * 2, 2, 0)
    mixing = lax.dynamic_index_in_dim(head_mix, pair, 0, keepdims=False)

    k_all = project(normed_all, wk_g).astype(jnp.bfloat16)
    v_all = project(normed_all, wv_g).astype(jnp.bfloat16)
    k3 = k_all.reshape(length, 2, HD)
    v3 = v_all.reshape(length, 2, HD)

    docs = doc_ids[0]
    nb = span // TQ
    extra = 1 if splits > 1 else 0
    nb_all = nb + extra
    doc_cap = length // 2
    nw = min(length // TQ, (doc_cap + QCONV - 2 + TQ - 1) // TQ + 1)
    q_tail = normed_pad_tail(normed_all, extra)
    q_rows = project(lax.dynamic_slice_in_dim(q_tail, q0, nb_all * TQ + PAD, 0), wq_g).astype(jnp.bfloat16)
    q_blocks = jnp.stack([q_rows[t * TQ : t * TQ + EXT] for t in range(nb_all)])
    q_blocks = jnp.transpose(q_blocks.reshape(nb_all, EXT, 2, HD), (0, 2, 1, 3))
    q_own = q_blocks[:, :, PAD:]
    k_heads = jnp.transpose(k3, (1, 0, 2))
    v_heads = jnp.transpose(v3, (1, 0, 2))
    docs_tail = jnp.pad(docs, (PAD, TQ * extra), constant_values=-1)
    doc_rows = lax.dynamic_slice_in_dim(docs_tail, q0, nb_all * TQ + PAD, 0)
    row_docs = jnp.stack([doc_rows[t * TQ : t * TQ + EXT] for t in range(nb_all)])[:, :, None]
    key_docs = docs[None, :]
    toff = (q0 // TQ).astype(jnp.int32).reshape(1)
    taps_flat = taps.reshape(2 * QCONV * KCONV)
    mix_flat = mixing.reshape(4)
    heads_blk, probs_blk = attention_forward(
        toff, taps_flat, mix_flat, q_blocks, k_heads, v_heads, row_docs, key_docs, nw, length
    )
    heads_own = jnp.transpose(heads_blk[:nb], (0, 2, 1, 3)).reshape(span, pw)

    def to_tokens(values):
        cols = values.shape[1]
        if splits == 1:
            full = values
        else:
            full = lax.dynamic_update_slice_in_dim(
                jnp.zeros((length, cols), values.dtype), values, q0, 0
            )
        got = lax.all_to_all(full, "seq", 0, 0, tiled=True)
        got = got.reshape(groups, splits, blk, cols)
        if splits > 1:
            got = jnp.sum(got.astype(jnp.float32), axis=1).astype(values.dtype)
        else:
            got = got[:, 0]
        return got

    heads_tok = jnp.transpose(to_tokens(heads_own), (1, 0, 2)).reshape(blk, width)
    middle = flat_in + project(heads_tok, w_out)
    scale_two = rms_scale(middle)
    normed_ffn = (middle * scale_two * gain_ffn).astype(jnp.bfloat16)
    hid_width = w_gate.shape[1]
    packed = jnp.concatenate([w_gate, w_up, jnp.transpose(w_down)], axis=1)
    pieces = [packed]
    for k in range(1, row_count):
        route = [(i, (i + k) % row_count) for i in range(row_count)]
        pieces.append(lax.ppermute(packed, "row", route))
    rev = jnp.stack(pieces[::-1] + pieces[::-1])
    full_w = lax.dynamic_slice_in_dim(rev, row_count - 1 - row_index, row_count, 0)
    full_w = full_w.reshape(row_count * packed.shape[0], packed.shape[1])
    joint = full_w[:, : 2 * hid_width]
    down_full = jnp.transpose(full_w[:, 2 * hid_width :])
    ffn_rows = lax.all_gather(normed_ffn, "seq", axis=0, tiled=True)
    gate_up = project(ffn_rows, joint)
    gate_vals = gate_up[:, :hid_width]
    up_vals = gate_up[:, hid_width:]
    hidden = (jax.nn.silu(gate_vals) * up_vals).astype(jnp.bfloat16)
    ffn_part = project(hidden, down_full).astype(jnp.bfloat16)
    cot_flat = cotangent.reshape(blk, width)
    cot_low = cot_flat.astype(jnp.bfloat16)
    cot_rows = lax.all_gather(cot_low, "seq", axis=0, tiled=True)
    grad_hidden = contract_cols(cot_rows, down_full)
    grad_down_part = contract_rows(hidden, cot_rows)
    sigmoid_gate = jax.nn.sigmoid(gate_vals)
    grad_gate_vals = grad_hidden * up_vals * sigmoid_gate * (1.0 + gate_vals * (1.0 - sigmoid_gate))
    grad_up_vals = grad_hidden * gate_vals * sigmoid_gate
    grad_joint = jnp.concatenate([grad_gate_vals, grad_up_vals], axis=1).astype(jnp.bfloat16)
    grad_joint_w = contract_rows(ffn_rows, grad_joint)
    grad_normed_ffn = lax.psum_scatter(
        contract_cols(grad_joint, joint).astype(jnp.bfloat16),
        "seq",
        scatter_dimension=0,
        tiled=True,
    ).astype(jnp.float32)
    grad_pack = jnp.concatenate([grad_joint_w, jnp.transpose(grad_down_part)], axis=1)
    band = grad_pack.shape[0] // row_count
    grad_blocks = grad_pack.reshape(row_count, band, grad_pack.shape[1]).astype(jnp.bfloat16)
    ffn_grad = lax.dynamic_index_in_dim(grad_blocks, row_index, 0, keepdims=False).astype(jnp.float32)
    for k in range(1, row_count):
        route = [(i, (i + k) % row_count) for i in range(row_count)]
        sent = lax.dynamic_index_in_dim(grad_blocks, (row_index + k) % row_count, 0, keepdims=False)
        ffn_grad = ffn_grad + lax.ppermute(sent, "row", route).astype(jnp.float32)
    grad_w_gate = ffn_grad[:, :hid_width]
    grad_w_up = ffn_grad[:, hid_width : 2 * hid_width]
    grad_w_down = jnp.transpose(ffn_grad[:, 2 * hid_width :])
    gain_ffn_part = jnp.sum(grad_normed_ffn * middle * scale_two, axis=0)
    scaled_two = grad_normed_ffn * gain_ffn
    grad_middle = (
        cot_flat
        + scale_two * scaled_two
        - middle * scale_two**3 * jnp.mean(scaled_two * middle, axis=-1, keepdims=True)
    )
    grad_attn = grad_middle.astype(jnp.bfloat16)
    grad_attn_all = lax.all_gather(grad_attn, "seq", axis=0, tiled=True)
    ffn_part, grad_attn_all = lax.optimization_barrier((ffn_part, grad_attn_all))
    ffn_out = lax.psum_scatter(ffn_part, "seq", scatter_dimension=0, tiled=True).astype(jnp.float32)
    outputs = middle + ffn_out
    grad_attn_tail = jnp.pad(grad_attn_all, ((0, TQ * extra), (0, 0)))
    grad_heads_x = contract_cols(
        lax.dynamic_slice_in_dim(grad_attn_tail, q0, nb_all * TQ, 0), wo_g
    ).astype(jnp.bfloat16)
    gh_blocks = jnp.transpose(grad_heads_x.reshape(nb_all, TQ, 2, HD), (0, 2, 1, 3))
    grad_out_part = contract_rows(heads_own, lax.dynamic_slice_in_dim(grad_attn_all, q0, span, 0))
    gq_blk, gk_heads, gv_heads, tap_acc, mix_acc = attention_backward(
        toff, taps_flat, mix_flat, q_blocks, q_own, k_heads, v_heads, row_docs, key_docs,
        probs_blk, gh_blocks, nw, length, nb,
    )
    grad_q_own = jnp.transpose(gq_blk[:nb], (0, 2, 1, 3)).reshape(span, pw)
    grad_k_part = jnp.transpose(gk_heads, (2, 0, 1)).reshape(length, pw)
    grad_v_part = jnp.transpose(gv_heads, (2, 0, 1)).reshape(length, pw)
    grad_taps_part = jnp.sum(tap_acc, axis=(1, 2)).reshape(2, QCONV, KCONV)
    grad_mix_part = jnp.sum(mix_acc, axis=1).reshape(2, 2)

    def split_sum(values):
        if splits == 1:
            return values
        total = values
        for step in range(1, splits):
            route = []
            for s in range(seq_count):
                base = (s // splits) * splits
                route.append((s, base + (s - base + step) % splits))
            total = total + lax.ppermute(values, "seq", route)
        return total

    grad_k_low = split_sum(grad_k_part).astype(jnp.bfloat16)
    grad_v_low = split_sum(grad_v_part).astype(jnp.bfloat16)
    grad_k_own = lax.dynamic_slice_in_dim(grad_k_low, q0, span, 0)
    grad_v_own = lax.dynamic_slice_in_dim(grad_v_low, q0, span, 0)

    normed_own = lax.dynamic_slice_in_dim(normed_all, q0, span, 0)
    rows_per_dev = width // (row_count * seq_count)

    partials = jnp.stack(
        [
            contract_rows(normed_own, grad_q_own),
            contract_rows(normed_own, grad_k_own),
            contract_rows(normed_own, grad_v_own),
        ]
    )
    red = lax.psum_scatter(partials, "row", scatter_dimension=1, tiled=True)
    got = lax.all_to_all(red, "seq", 1, 1, tiled=True)
    got = got.reshape(3, groups, splits, rows_per_dev, pw).sum(axis=2)
    got = jnp.transpose(got, (0, 2, 1, 3)).reshape(3, rows_per_dev, width)
    grad_w_query, grad_w_key, grad_w_value = got[0], got[1], got[2]

    red_out = lax.psum_scatter(grad_out_part, "row", scatter_dimension=0, tiled=True)
    red_out = red_out.reshape(splits, rows_per_dev, width)
    grad_w_out = jnp.zeros((rows_per_dev, width), jnp.float32)
    for src_part in range(splits):
        for j in range(splits):
            route = []
            for r in range(row_count):
                for g in range(groups):
                    src = r * seq_count + g * splits + src_part
                    dst = g * row_count * splits + r * splits + j
                    route.append((src, dst))
            grad_w_out = grad_w_out + lax.ppermute(red_out[j], ("row", "seq"), route)

    grad_tok = to_tokens(jnp.concatenate([grad_q_own, grad_k_own, grad_v_own], axis=1))
    grad_tok = grad_tok.reshape(groups, blk, 3, pw)
    gq_tok = jnp.transpose(grad_tok[:, :, 0], (1, 0, 2)).reshape(blk, width)
    gk_tok = jnp.transpose(grad_tok[:, :, 1], (1, 0, 2)).reshape(blk, width)
    gv_tok = jnp.transpose(grad_tok[:, :, 2], (1, 0, 2)).reshape(blk, width)
    grad_normed = (
        contract_cols(gq_tok, w_query) + contract_cols(gk_tok, w_key) + contract_cols(gv_tok, w_value)
    )
    gain_attn_part = jnp.sum(grad_normed * flat_in * scale_one, axis=0)
    scaled_one = grad_normed * gain_attn
    grad_inputs = (
        grad_middle
        + scale_one * scaled_one
        - flat_in * scale_one**3 * jnp.mean(scaled_one * flat_in, axis=-1, keepdims=True)
    )
    taps_full = lax.dynamic_update_slice_in_dim(
        jnp.zeros((HEADS, QCONV, KCONV), jnp.float32), grad_taps_part, pair * 2, 0
    )
    mix_full = lax.dynamic_update_slice_in_dim(
        jnp.zeros((groups, 2, 2), jnp.float32), grad_mix_part[None], pair, 0
    )
    small = jnp.concatenate(
        [gain_attn_part, gain_ffn_part, taps_full.reshape(-1), mix_full.reshape(-1)]
    )
    small = lax.psum(small, ("row", "seq"))
    gain_rows = width // (row_count * seq_count)
    gain_at = (row_index * seq_count + seq_index) * gain_rows
    grad_gain_attn = lax.dynamic_slice_in_dim(small, gain_at, gain_rows, 0)
    grad_gain_ffn = lax.dynamic_slice_in_dim(small, width + gain_at, gain_rows, 0)
    grad_taps = small[2 * width : 2 * width + HEADS * TAPS].reshape(HEADS, QCONV, KCONV)
    grad_mix = small[2 * width + HEADS * TAPS :].reshape(groups, 2, 2)
    return (
        outputs.reshape(row_dev, blk, width),
        grad_inputs.reshape(row_dev, blk, width),
        grad_w_query,
        grad_w_key,
        grad_w_value,
        grad_w_out,
        grad_gain_attn,
        grad_gain_ffn,
        grad_taps,
        grad_mix,
        grad_w_gate,
        grad_w_up,
        grad_w_down,
    )


def solution(mesh):
    return jax.shard_map(
        shards_body,
        mesh=mesh,
        in_specs=(
            P("row", "seq", None),
            P("row", None),
            P(),
            P(),
            P(),
            P(),
            P(),
            P(),
            P(),
            P(),
            P("row", "seq"),
            P("row", "seq"),
            P("seq", "row"),
            P("row", "seq", None),
        ),
        out_specs=(
            P("row", "seq", None),
            P("row", "seq", None),
            P(("row", "seq"), None),
            P(("row", "seq"), None),
            P(("row", "seq"), None),
            P(("row", "seq"), None),
            P(("row", "seq")),
            P(("row", "seq")),
            P(),
            P(),
            P("row", "seq"),
            P("row", "seq"),
            P("seq", "row"),
        ),
        check_vma=False,
    )
```

```python
import jax
import jax.numpy as jnp
from jax import lax
from jax.sharding import PartitionSpec as P
from jax.experimental import pallas as pl
from jax.experimental.pallas import tpu as pltpu

HEADS = 16
HD = 96
QCONV = 6
KCONV = 11
PAD = 8
TQ = 128
EXT = TQ + PAD
SCALE = HD ** (-0.5)
TAPS = QCONV * KCONV

epsilon = 1e-06


def rms_scale(values):
    return lax.rsqrt(jnp.mean(values * values, axis=-1, keepdims=True) + epsilon)


def project(values, weight):
    return jnp.dot(values, weight, preferred_element_type=jnp.float32)


def contract_rows(left, right):
    return lax.dot_general(
        left, right, (((0,), (0,)), ((), ())), preferred_element_type=jnp.float32
    )


def contract_cols(left, right):
    return lax.dot_general(
        left, right, (((1,), (1,)), ((), ())), preferred_element_type=jnp.float32
    )


def normed_pad_tail(values, extra):
    return jnp.pad(values, ((PAD, TQ * extra), (0, 0)))


def window_start(block, nw, length):
    return pl.multiple_of(jnp.clip((block - nw + 1) * TQ, 0, length - nw * TQ), TQ)


def tap_accumulate(sh_ref, acc_ref, taps_ref, head, width):
    cw = 256 if (width // 128) % 2 == 0 else 128

    def body(chunk, carry):
        r0 = pl.multiple_of(chunk * 8, 8)
        for c0 in range(0, width, cw):
            tiles = [sh_ref[b, pl.ds(r0, 8), pl.ds(c0, cw)] for b in range(KCONV)]
            for a in range(QCONV):
                base = head * TAPS + a * KCONV
                total = taps_ref[base] * tiles[0]
                for b in range(1, KCONV):
                    total = total + taps_ref[base + b] * tiles[b]
                acc_ref[a, pl.ds(r0, 8), pl.ds(c0, cw)] = total
        return carry

    lax.fori_loop(0, EXT // 8, body, 0)


def tap_products(sh_ref, g_ref, width):
    sums = {}
    for a0 in range(0, QCONV, 2):

        def body(chunk, accs):
            r0 = pl.multiple_of(chunk * 8, 8)
            out = list(accs)
            for c0 in range(0, width, 128):
                ga = [g_ref[a0 + k, pl.ds(r0, 8), pl.ds(c0, 128)] for k in range(2)]
                for b in range(KCONV):
                    tile = sh_ref[b, pl.ds(r0, 8), pl.ds(c0, 128)]
                    for k in range(2):
                        out[k * KCONV + b] = out[k * KCONV + b] + ga[k] * tile
            return tuple(out)

        start = tuple(jnp.zeros((8, 128), jnp.float32) for _ in range(2 * KCONV))
        res = lax.fori_loop(0, EXT // 8, body, start)
        for k in range(2):
            for b in range(KCONV):
                sums[(a0 + k, b)] = res[k * KCONV + b]
    return sums


def masks(block, kstart, width, rdoc_ref, kdoc_ref):
    keydoc = kdoc_ref[:, pl.ds(kstart, width)]
    ext_pos = block * TQ - PAD + lax.broadcasted_iota(jnp.int32, (EXT, width), 0)
    key_ext = kstart + lax.broadcasted_iota(jnp.int32, (EXT, width), 1)
    allowed_ext = (key_ext <= ext_pos) & (rdoc_ref[0] == keydoc)
    own_pos = block * TQ + lax.broadcasted_iota(jnp.int32, (TQ, width), 0)
    key_own = kstart + lax.broadcasted_iota(jnp.int32, (TQ, width), 1)
    allowed_own = (key_own <= own_pos) & (rdoc_ref[0, PAD:, :] == keydoc)
    return allowed_ext, allowed_own


def masked_shifts(q_ref, k_ref, head, kstart, width, allowed_ext, sh_ref):
    keys = k_ref[head, pl.ds(kstart, width), :]
    scores = lax.dot_general(
        q_ref[0, head], keys, (((1,), (1,)), ((), ())), preferred_element_type=jnp.float32
    ) * SCALE
    masked = jnp.where(allowed_ext, scores, 0.0)
    col = lax.broadcasted_iota(jnp.int32, (EXT, width), 1)
    sh_ref[0] = masked
    for b in range(1, KCONV):
        sh_ref[b] = jnp.where(col >= b, pltpu.roll(masked, b, 1), 0.0)


def fwd_kernel(toff_ref, taps_ref, mix_ref, q_ref, k_ref, v_ref, rdoc_ref, kdoc_ref,
               heads_ref, probs_ref, sh_ref, acc_ref, *, nw, length):
    width = nw * TQ
    block = toff_ref[0] + pl.program_id(0)
    kstart = window_start(block, nw, length)
    allowed_ext, allowed_own = masks(block, kstart, width, rdoc_ref, kdoc_ref)
    for head in range(2):
        masked_shifts(q_ref, k_ref, head, kstart, width, allowed_ext, sh_ref)
        tap_accumulate(sh_ref, acc_ref, taps_ref, head, width)
        conv = acc_ref[0]
        for a in range(1, QCONV):
            conv = conv + pltpu.roll(acc_ref[a], a, 0)
        logits = jnp.where(allowed_own, conv[PAD:], -jnp.inf)
        highest = jnp.max(logits, axis=1, keepdims=True)
        highest = jnp.where(highest > -jnp.inf, highest, 0.0)
        expd = jnp.exp(logits - highest)
        denom = jnp.sum(expd, axis=1, keepdims=True)
        probs_ref[0, head] = expd / jnp.where(denom > 0.0, denom, 1.0)
    p0 = probs_ref[0, 0]
    p1 = probs_ref[0, 1]
    for c in range(2):
        mixed = (mix_ref[2 * c] * p0 + mix_ref[2 * c + 1] * p1).astype(jnp.bfloat16)
        heads_ref[0, c] = jnp.dot(
            mixed, v_ref[c, pl.ds(kstart, width), :], preferred_element_type=jnp.float32
        ).astype(jnp.bfloat16)


def attention_forward(toff, taps_flat, mix_flat, q_blocks, k_heads, v_heads, row_docs, key_docs, nw, length):
    nb_all = q_blocks.shape[0]
    width = nw * TQ
    smem = pl.BlockSpec(memory_space=pltpu.SMEM)
    flops = nb_all * 2 * (4 * EXT * width * HD + 2 * TAPS * EXT * width)
    return pl.pallas_call(
        lambda *refs: fwd_kernel(*refs, nw=nw, length=length),
        grid=(nb_all,),
        in_specs=[
            smem,
            smem,
            smem,
            pl.BlockSpec((1, 2, EXT, HD), lambda t: (t, 0, 0, 0)),
            pl.BlockSpec((2, length, HD), lambda t: (0, 0, 0)),
            pl.BlockSpec((2, length, HD), lambda t: (0, 0, 0)),
            pl.BlockSpec((1, EXT, 1), lambda t: (t, 0, 0)),
            pl.BlockSpec((1, length), lambda t: (0, 0)),
        ],
        out_specs=[
            pl.BlockSpec((1, 2, TQ, HD), lambda t: (t, 0, 0, 0)),
            pl.BlockSpec((1, 2, TQ, width), lambda t: (t, 0, 0, 0)),
        ],
        out_shape=[
            jax.ShapeDtypeStruct((nb_all, 2, TQ, HD), jnp.bfloat16),
            jax.ShapeDtypeStruct((nb_all, 2, TQ, width), jnp.float32),
        ],
        scratch_shapes=[
            pltpu.VMEM((KCONV, EXT, width), jnp.float32),
            pltpu.VMEM((QCONV, EXT, width), jnp.float32),
        ],
        compiler_params=pltpu.CompilerParams(
            dimension_semantics=("arbitrary",), vmem_limit_bytes=56 * 1024 * 1024
        ),
        cost_estimate=pl.CostEstimate(
            flops=flops, transcendentals=nb_all * 2 * TQ * width,
            bytes_accessed=nb_all * 2 * TQ * width * 4 + 4 * length * HD * 2,
        ),
    )(toff, taps_flat, mix_flat, q_blocks, k_heads, v_heads, row_docs, key_docs)


def bwd_kernel(toff_ref, taps_ref, mix_ref, q_ref, qo_ref, k_ref, v_ref, rdoc_ref, kdoc_ref,
               probs_ref, gh_ref, ght_ref, gq_ref, gk_ref, gv_ref, tacc_ref, macc_ref,
               carry_ref, sh_ref, acc_ref, g_ref, gx_ref, *, nw, length, nb, nb_all):
    width = nw * TQ
    step = pl.program_id(0)
    local = nb_all - 1 - step
    block = toff_ref[0] + local
    kstart = window_start(block, nw, length)

    @pl.when(step == 0)
    def _init():
        gk_ref[...] = jnp.zeros(gk_ref.shape, jnp.float32)
        gv_ref[...] = jnp.zeros(gv_ref.shape, jnp.float32)
        tacc_ref[...] = jnp.zeros(tacc_ref.shape, jnp.float32)
        macc_ref[...] = jnp.zeros(macc_ref.shape, jnp.float32)
        carry_ref[...] = jnp.zeros(carry_ref.shape, jnp.float32)

    allowed_ext, allowed_own = masks(block, kstart, width, rdoc_ref, kdoc_ref)
    gm = [
        lax.dot_general(
            gh_ref[0, c], v_ref[c, pl.ds(kstart, width), :], (((1,), (1,)), ((), ())),
            preferred_element_type=jnp.float32,
        )
        for c in range(2)
    ]
    probs = [probs_ref[0, 0], probs_ref[0, 1]]
    gc = []
    for e in range(2):
        gp = mix_ref[e] * gm[0] + mix_ref[2 + e] * gm[1]
        inner = jnp.sum(gp * probs[e], axis=1, keepdims=True)
        gc.append(probs[e] * (gp - inner))

    def own_sums():
        for c in range(2):
            for e in range(2):
                macc_ref[pl.ds(2 * c + e, 1), :] += jnp.sum(gm[c] * probs[e], axis=0, keepdims=True)
            mixed = (mix_ref[2 * c] * probs[0] + mix_ref[2 * c + 1] * probs[1]).astype(jnp.bfloat16)
            gv_ref[c, :, pl.ds(kstart, width)] += jnp.dot(
                ght_ref[0, c], mixed, preferred_element_type=jnp.float32
            )

    def head_taps(e):
        masked_shifts(q_ref, k_ref, e, kstart, width, allowed_ext, sh_ref)
        gcp = jnp.concatenate([jnp.zeros((PAD, width), jnp.float32), gc[e]], axis=0)
        g_ref[0] = gcp
        for a in range(1, QCONV):
            g_ref[a] = pltpu.roll(gcp, EXT - a, 0)
        sums = tap_products(sh_ref, g_ref, width)
        for b in range(KCONV):
            for a in range(QCONV):
                tacc_ref[e * TAPS + a * KCONV + b] += sums[(a, b)]

    def head_keys(e, gs):
        gk_ref[e, :, pl.ds(kstart, width)] += jnp.dot(
            qo_ref[0, e], gs, preferred_element_type=jnp.float32
        ) * SCALE

    nxt = [carry_ref[e, :, pl.ds(kstart, width + TQ)] for e in range(2)]
    if nb < nb_all:
        pl.when(local < nb)(own_sums)
    else:
        own_sums()
    for e in range(2):
        if nb < nb_all:
            pl.when(local < nb)(lambda: head_taps(e))
        else:
            head_taps(e)
        gx_ref[pl.ds(0, TQ), pl.ds(0, width)] = gc[e]
        gx_ref[pl.ds(0, TQ), pl.ds(width, TQ)] = jnp.zeros((TQ, TQ), jnp.float32)
        gx_ref[pl.ds(TQ, PAD), :] = nxt[e]
        gxv = gx_ref[...]
        sh_ref[0] = gxv[:, :width]
        for b in range(1, KCONV):
            sh_ref[b] = pltpu.roll(gxv, width + TQ - b, 1)[:, :width]
        tap_accumulate(sh_ref, acc_ref, taps_ref, e, width)
        gmk = acc_ref[0]
        for a in range(1, QCONV):
            gmk = gmk + pltpu.roll(acc_ref[a], EXT - a, 0)
        gs = jnp.where(allowed_own, gmk[:TQ], 0.0).astype(jnp.bfloat16)
        gq_ref[0, e] = (
            jnp.dot(gs, k_ref[e, pl.ds(kstart, width), :], preferred_element_type=jnp.float32) * SCALE
        ).astype(jnp.bfloat16)
        if nb < nb_all:
            pl.when(local < nb)(lambda: head_keys(e, gs))
        else:
            head_keys(e, gs)
    carry_ref[...] = jnp.zeros(carry_ref.shape, jnp.float32)
    for e in range(2):
        carry_ref[e, :, pl.ds(kstart, width)] = gc[e][:PAD]


def attention_backward(toff, taps_flat, mix_flat, q_blocks, q_own, k_heads, v_heads, row_docs, key_docs,
                       probs_blk, gh_blocks, nw, length, nb):
    q_own = jnp.swapaxes(q_own, 2, 3)
    gh_t = jnp.swapaxes(gh_blocks, 2, 3)
    nb_all = q_blocks.shape[0]
    width = nw * TQ
    smem = pl.BlockSpec(memory_space=pltpu.SMEM)
    rev = lambda s: nb_all - 1 - s
    flops = nb_all * 2 * (8 * TQ * width * HD + 6 * TAPS * EXT * width)
    return pl.pallas_call(
        lambda *refs: bwd_kernel(*refs, nw=nw, length=length, nb=nb, nb_all=nb_all),
        grid=(nb_all,),
        in_specs=[
            smem,
            smem,
            smem,
            pl.BlockSpec((1, 2, EXT, HD), lambda s: (rev(s), 0, 0, 0)),
            pl.BlockSpec((1, 2, HD, TQ), lambda s: (rev(s), 0, 0, 0)),
            pl.BlockSpec((2, length, HD), lambda s: (0, 0, 0)),
            pl.BlockSpec((2, length, HD), lambda s: (0, 0, 0)),
            pl.BlockSpec((1, EXT, 1), lambda s: (rev(s), 0, 0)),
            pl.BlockSpec((1, length), lambda s: (0, 0)),
            pl.BlockSpec((1, 2, TQ, width), lambda s: (rev(s), 0, 0, 0)),
            pl.BlockSpec((1, 2, TQ, HD), lambda s: (rev(s), 0, 0, 0)),
            pl.BlockSpec((1, 2, HD, TQ), lambda s: (rev(s), 0, 0, 0)),
        ],
        out_specs=[
            pl.BlockSpec((1, 2, TQ, HD), lambda s: (rev(s), 0, 0, 0)),
            pl.BlockSpec((2, HD, length), lambda s: (0, 0, 0)),
            pl.BlockSpec((2, HD, length), lambda s: (0, 0, 0)),
            pl.BlockSpec((2 * TAPS, 8, 128), lambda s: (0, 0, 0)),
            pl.BlockSpec((4, width), lambda s: (0, 0)),
        ],
        out_shape=[
            jax.ShapeDtypeStruct((nb_all, 2, TQ, HD), jnp.bfloat16),
            jax.ShapeDtypeStruct((2, HD, length), jnp.float32),
            jax.ShapeDtypeStruct((2, HD, length), jnp.float32),
            jax.ShapeDtypeStruct((2 * TAPS, 8, 128), jnp.float32),
            jax.ShapeDtypeStruct((4, width), jnp.float32),
        ],
        scratch_shapes=[
            pltpu.VMEM((2, PAD, length + TQ), jnp.float32),
            pltpu.VMEM((KCONV, EXT, width), jnp.float32),
            pltpu.VMEM((QCONV, EXT, width), jnp.float32),
            pltpu.VMEM((QCONV, EXT, width), jnp.float32),
            pltpu.VMEM((EXT, width + TQ), jnp.float32),
        ],
        compiler_params=pltpu.CompilerParams(
            dimension_semantics=("arbitrary",), vmem_limit_bytes=60 * 1024 * 1024
        ),
        cost_estimate=pl.CostEstimate(
            flops=flops, transcendentals=0,
            bytes_accessed=nb_all * 2 * TQ * width * 4 + 8 * length * HD * 4,
        ),
    )(toff, taps_flat, mix_flat, q_blocks, q_own, k_heads, v_heads, row_docs, key_docs, probs_blk, gh_blocks, gh_t)


def shards_body(
    inputs,
    doc_ids,
    w_query,
    w_key,
    w_value,
    w_out,
    gain_attn,
    gain_ffn,
    conv_taps,
    head_mix,
    w_gate,
    w_up,
    w_down,
    cotangent,
):
    row_dev, blk, width = inputs.shape
    assert row_dev == 1
    seq_count = lax.axis_size("seq")
    row_count = lax.axis_size("row")
    seq_index = lax.axis_index("seq")
    row_index = lax.axis_index("row")
    length = blk * seq_count
    groups = HEADS // 2
    assert seq_count % groups == 0
    splits = seq_count // groups
    span = length // splits
    pw = 2 * HD
    pair = seq_index // splits
    part = seq_index % splits
    q0 = part * span

    flat_in = inputs.reshape(blk, width)
    scale_one = rms_scale(flat_in)
    normed = (flat_in * scale_one * gain_attn).astype(jnp.bfloat16)
    normed_all = lax.all_gather(normed, "seq", axis=0, tiled=True)

    wq_g = lax.dynamic_slice_in_dim(w_query, pair * pw, pw, 1)
    wk_g = lax.dynamic_slice_in_dim(w_key, pair * pw, pw, 1)
    wv_g = lax.dynamic_slice_in_dim(w_value, pair * pw, pw, 1)
    wo_g = lax.dynamic_slice_in_dim(w_out, pair * pw, pw, 0)
    taps = lax.dynamic_slice_in_dim(conv_taps, pair * 2, 2, 0)
    mixing = lax.dynamic_index_in_dim(head_mix, pair, 0, keepdims=False)

    k_all = project(normed_all, wk_g).astype(jnp.bfloat16)
    v_all = project(normed_all, wv_g).astype(jnp.bfloat16)
    k3 = k_all.reshape(length, 2, HD)
    v3 = v_all.reshape(length, 2, HD)

    docs = doc_ids[0]
    nb = span // TQ
    extra = 1 if splits > 1 else 0
    nb_all = nb + extra
    doc_cap = length // 2
    nw = min(length // TQ, (doc_cap + QCONV - 2 + TQ - 1) // TQ + 1)
    q_tail = normed_pad_tail(normed_all, extra)
    q_rows = project(lax.dynamic_slice_in_dim(q_tail, q0, nb_all * TQ + PAD, 0), wq_g).astype(jnp.bfloat16)
    q_blocks = jnp.stack([q_rows[t * TQ : t * TQ + EXT] for t in range(nb_all)])
    q_blocks = jnp.transpose(q_blocks.reshape(nb_all, EXT, 2, HD), (0, 2, 1, 3))
    q_own = q_blocks[:, :, PAD:]
    k_heads = jnp.transpose(k3, (1, 0, 2))
    v_heads = jnp.transpose(v3, (1, 0, 2))
    docs_tail = jnp.pad(docs, (PAD, TQ * extra), constant_values=-1)
    doc_rows = lax.dynamic_slice_in_dim(docs_tail, q0, nb_all * TQ + PAD, 0)
    row_docs = jnp.stack([doc_rows[t * TQ : t * TQ + EXT] for t in range(nb_all)])[:, :, None]
    key_docs = docs[None, :]
    toff = (q0 // TQ).astype(jnp.int32).reshape(1)
    taps_flat = taps.reshape(2 * QCONV * KCONV)
    mix_flat = mixing.reshape(4)
    heads_blk, probs_blk = attention_forward(
        toff, taps_flat, mix_flat, q_blocks, k_heads, v_heads, row_docs, key_docs, nw, length
    )
    heads_own = jnp.transpose(heads_blk[:nb], (0, 2, 1, 3)).reshape(span, pw)

    def to_tokens(values):
        cols = values.shape[1]
        if splits == 1:
            full = values
        else:
            full = lax.dynamic_update_slice_in_dim(
                jnp.zeros((length, cols), values.dtype), values, q0, 0
            )
        got = lax.all_to_all(full, "seq", 0, 0, tiled=True)
        got = got.reshape(groups, splits, blk, cols)
        if splits > 1:
            got = jnp.sum(got.astype(jnp.float32), axis=1).astype(values.dtype)
        else:
            got = got[:, 0]
        return got

    heads_tok = jnp.transpose(to_tokens(heads_own), (1, 0, 2)).reshape(blk, width)
    middle = flat_in + project(heads_tok, w_out)
    scale_two = rms_scale(middle)
    normed_ffn = (middle * scale_two * gain_ffn).astype(jnp.bfloat16)
    hid_width = w_gate.shape[1]
    packed = jnp.concatenate([w_gate, w_up, jnp.transpose(w_down)], axis=1)
    pieces = [packed]
    for k in range(1, row_count):
        route = [(i, (i + k) % row_count) for i in range(row_count)]
        pieces.append(lax.ppermute(packed, "row", route))
    rev = jnp.stack(pieces[::-1] + pieces[::-1])
    full_w = lax.dynamic_slice_in_dim(rev, row_count - 1 - row_index, row_count, 0)
    full_w = full_w.reshape(row_count * packed.shape[0], packed.shape[1])
    joint = full_w[:, : 2 * hid_width]
    down_full = jnp.transpose(full_w[:, 2 * hid_width :])
    ffn_rows = lax.all_gather(normed_ffn, "seq", axis=0, tiled=True)
    gate_up = project(ffn_rows, joint)
    gate_vals = gate_up[:, :hid_width]
    up_vals = gate_up[:, hid_width:]
    hidden = (jax.nn.silu(gate_vals) * up_vals).astype(jnp.bfloat16)
    ffn_part = project(hidden, down_full).astype(jnp.bfloat16)
    cot_flat = cotangent.reshape(blk, width)
    cot_low = cot_flat.astype(jnp.bfloat16)
    cot_rows = lax.all_gather(cot_low, "seq", axis=0, tiled=True)
    grad_hidden = contract_cols(cot_rows, down_full)
    grad_down_part = contract_rows(hidden, cot_rows)
    sigmoid_gate = jax.nn.sigmoid(gate_vals)
    grad_gate_vals = grad_hidden * up_vals * sigmoid_gate * (1.0 + gate_vals * (1.0 - sigmoid_gate))
    grad_up_vals = grad_hidden * gate_vals * sigmoid_gate
    grad_joint = jnp.concatenate([grad_gate_vals, grad_up_vals], axis=1).astype(jnp.bfloat16)
    grad_joint_w = contract_rows(ffn_rows, grad_joint)
    grad_normed_ffn = lax.psum_scatter(
        contract_cols(grad_joint, joint).astype(jnp.bfloat16),
        "seq",
        scatter_dimension=0,
        tiled=True,
    ).astype(jnp.float32)
    grad_pack = jnp.concatenate([grad_joint_w, jnp.transpose(grad_down_part)], axis=1)
    band = grad_pack.shape[0] // row_count
    grad_blocks = grad_pack.reshape(row_count, band, grad_pack.shape[1]).astype(jnp.bfloat16)
    ffn_grad = lax.dynamic_index_in_dim(grad_blocks, row_index, 0, keepdims=False).astype(jnp.float32)
    for k in range(1, row_count):
        route = [(i, (i + k) % row_count) for i in range(row_count)]
        sent = lax.dynamic_index_in_dim(grad_blocks, (row_index + k) % row_count, 0, keepdims=False)
        ffn_grad = ffn_grad + lax.ppermute(sent, "row", route).astype(jnp.float32)
    grad_w_gate = ffn_grad[:, :hid_width]
    grad_w_up = ffn_grad[:, hid_width : 2 * hid_width]
    grad_w_down = jnp.transpose(ffn_grad[:, 2 * hid_width :])
    gain_ffn_part = jnp.sum(grad_normed_ffn * middle * scale_two, axis=0)
    scaled_two = grad_normed_ffn * gain_ffn
    grad_middle = (
        cot_flat
        + scale_two * scaled_two
        - middle * scale_two**3 * jnp.mean(scaled_two * middle, axis=-1, keepdims=True)
    )
    grad_attn = grad_middle.astype(jnp.bfloat16)
    grad_attn_all = lax.all_gather(grad_attn, "seq", axis=0, tiled=True)
    ffn_part, grad_attn_all = lax.optimization_barrier((ffn_part, grad_attn_all))
    ffn_out = lax.psum_scatter(ffn_part, "seq", scatter_dimension=0, tiled=True).astype(jnp.float32)
    outputs = middle + ffn_out
    grad_attn_tail = jnp.pad(grad_attn_all, ((0, TQ * extra), (0, 0)))
    grad_heads_x = contract_cols(
        lax.dynamic_slice_in_dim(grad_attn_tail, q0, nb_all * TQ, 0), wo_g
    ).astype(jnp.bfloat16)
    gh_blocks = jnp.transpose(grad_heads_x.reshape(nb_all, TQ, 2, HD), (0, 2, 1, 3))
    grad_out_part = contract_rows(heads_own, lax.dynamic_slice_in_dim(grad_attn_all, q0, span, 0))
    gq_blk, gk_heads, gv_heads, tap_acc, mix_acc = attention_backward(
        toff, taps_flat, mix_flat, q_blocks, q_own, k_heads, v_heads, row_docs, key_docs,
        probs_blk, gh_blocks, nw, length, nb,
    )
    grad_q_own = jnp.transpose(gq_blk[:nb], (0, 2, 1, 3)).reshape(span, pw)
    grad_k_part = jnp.transpose(gk_heads, (2, 0, 1)).reshape(length, pw)
    grad_v_part = jnp.transpose(gv_heads, (2, 0, 1)).reshape(length, pw)
    grad_taps_part = jnp.sum(tap_acc, axis=(1, 2)).reshape(2, QCONV, KCONV)
    grad_mix_part = jnp.sum(mix_acc, axis=1).reshape(2, 2)

    def split_sum(values):
        if splits == 1:
            return values
        total = values
        for step in range(1, splits):
            route = []
            for s in range(seq_count):
                base = (s // splits) * splits
                route.append((s, base + (s - base + step) % splits))
            total = total + lax.ppermute(values, "seq", route)
        return total

    grad_k_low = split_sum(grad_k_part).astype(jnp.bfloat16)
    grad_v_low = split_sum(grad_v_part).astype(jnp.bfloat16)
    grad_k_own = lax.dynamic_slice_in_dim(grad_k_low, q0, span, 0)
    grad_v_own = lax.dynamic_slice_in_dim(grad_v_low, q0, span, 0)

    normed_own = lax.dynamic_slice_in_dim(normed_all, q0, span, 0)
    rows_per_dev = width // (row_count * seq_count)

    partials = jnp.stack(
        [
            contract_rows(normed_own, grad_q_own),
            contract_rows(normed_own, grad_k_own),
            contract_rows(normed_own, grad_v_own),
        ]
    )
    red = lax.psum_scatter(partials, "row", scatter_dimension=1, tiled=True)
    got = lax.all_to_all(red, "seq", 1, 1, tiled=True)
    got = got.reshape(3, groups, splits, rows_per_dev, pw).sum(axis=2)
    got = jnp.transpose(got, (0, 2, 1, 3)).reshape(3, rows_per_dev, width)
    grad_w_query, grad_w_key, grad_w_value = got[0], got[1], got[2]

    red_out = lax.psum_scatter(grad_out_part, "row", scatter_dimension=0, tiled=True)
    red_out = red_out.reshape(splits, rows_per_dev, width)
    grad_w_out = jnp.zeros((rows_per_dev, width), jnp.float32)
    for src_part in range(splits):
        for j in range(splits):
            route = []
            for r in range(row_count):
                for g in range(groups):
                    src = r * seq_count + g * splits + src_part
                    dst = g * row_count * splits + r * splits + j
                    route.append((src, dst))
            grad_w_out = grad_w_out + lax.ppermute(red_out[j], ("row", "seq"), route)

    grad_tok = to_tokens(jnp.concatenate([grad_q_own, grad_k_own, grad_v_own], axis=1))
    grad_tok = grad_tok.reshape(groups, blk, 3, pw)
    gq_tok = jnp.transpose(grad_tok[:, :, 0], (1, 0, 2)).reshape(blk, width)
    gk_tok = jnp.transpose(grad_tok[:, :, 1], (1, 0, 2)).reshape(blk, width)
    gv_tok = jnp.transpose(grad_tok[:, :, 2], (1, 0, 2)).reshape(blk, width)
    grad_normed = (
        contract_cols(gq_tok, w_query) + contract_cols(gk_tok, w_key) + contract_cols(gv_tok, w_value)
    )
    gain_attn_part = jnp.sum(grad_normed * flat_in * scale_one, axis=0)
    scaled_one = grad_normed * gain_attn
    grad_inputs = (
        grad_middle
        + scale_one * scaled_one
        - flat_in * scale_one**3 * jnp.mean(scaled_one * flat_in, axis=-1, keepdims=True)
    )
    taps_full = lax.dynamic_update_slice_in_dim(
        jnp.zeros((HEADS, QCONV, KCONV), jnp.float32), grad_taps_part, pair * 2, 0
    )
    mix_full = lax.dynamic_update_slice_in_dim(
        jnp.zeros((groups, 2, 2), jnp.float32), grad_mix_part[None], pair, 0
    )
    small = jnp.concatenate(
        [gain_attn_part, gain_ffn_part, taps_full.reshape(-1), mix_full.reshape(-1)]
    )
    devices = row_count * seq_count
    assert devices & (devices - 1) == 0
    mask = 1
    while mask < devices:
        route = [(i, i ^ mask) for i in range(devices)]
        small = small + lax.ppermute(small, ("row", "seq"), route)
        mask *= 2
    gain_rows = width // (row_count * seq_count)
    gain_at = (row_index * seq_count + seq_index) * gain_rows
    grad_gain_attn = lax.dynamic_slice_in_dim(small, gain_at, gain_rows, 0)
    grad_gain_ffn = lax.dynamic_slice_in_dim(small, width + gain_at, gain_rows, 0)
    grad_taps = small[2 * width : 2 * width + HEADS * TAPS].reshape(HEADS, QCONV, KCONV)
    grad_mix = small[2 * width + HEADS * TAPS :].reshape(groups, 2, 2)
    return (
        outputs.reshape(row_dev, blk, width),
        grad_inputs.reshape(row_dev, blk, width),
        grad_w_query,
        grad_w_key,
        grad_w_value,
        grad_w_out,
        grad_gain_attn,
        grad_gain_ffn,
        grad_taps,
        grad_mix,
        grad_w_gate,
        grad_w_up,
        grad_w_down,
    )


def solution(mesh):
    return jax.shard_map(
        shards_body,
        mesh=mesh,
        in_specs=(
            P("row", "seq", None),
            P("row", None),
            P(),
            P(),
            P(),
            P(),
            P(),
            P(),
            P(),
            P(),
            P("row", "seq"),
            P("row", "seq"),
            P("seq", "row"),
            P("row", "seq", None),
        ),
        out_specs=(
            P("row", "seq", None),
            P("row", "seq", None),
            P(("row", "seq"), None),
            P(("row", "seq"), None),
            P(("row", "seq"), None),
            P(("row", "seq"), None),
            P(("row", "seq")),
            P(("row", "seq")),
            P(),
            P(),
            P("row", "seq"),
            P("row", "seq"),
            P("seq", "row"),
        ),
        check_vma=False,
    )
```

```python
import jax
import jax.numpy as jnp
from jax import lax
from jax.sharding import PartitionSpec as P
from jax.experimental import pallas as pl
from jax.experimental.pallas import tpu as pltpu

HEADS = 16
HD = 96
QCONV = 6
KCONV = 11
PAD = 8
TQ = 128
EXT = TQ + PAD
SCALE = HD ** (-0.5)
TAPS = QCONV * KCONV

epsilon = 1e-06


def rms_scale(values):
    return lax.rsqrt(jnp.mean(values * values, axis=-1, keepdims=True) + epsilon)


def project(values, weight):
    return jnp.dot(values, weight, preferred_element_type=jnp.float32)


def contract_rows(left, right):
    return lax.dot_general(
        left, right, (((0,), (0,)), ((), ())), preferred_element_type=jnp.float32
    )


def contract_cols(left, right):
    return lax.dot_general(
        left, right, (((1,), (1,)), ((), ())), preferred_element_type=jnp.float32
    )


def normed_pad_tail(values, extra):
    return jnp.pad(values, ((PAD, TQ * extra), (0, 0)))


def window_start(block, nw, length):
    return pl.multiple_of(jnp.clip((block - nw + 1) * TQ, 0, length - nw * TQ), TQ)


def tap_accumulate(sh_ref, acc_ref, taps_ref, head, live):

    def body(col, carry):
        c0 = pl.multiple_of(col * 128, 128)
        for r0 in range(0, EXT, 8):
            tiles = [sh_ref[b, pl.ds(r0, 8), pl.ds(c0, 128)] for b in range(KCONV)]
            for a in range(QCONV):
                base = head * TAPS + a * KCONV
                total = taps_ref[base] * tiles[0]
                for b in range(1, KCONV):
                    total = total + taps_ref[base + b] * tiles[b]
                acc_ref[a, pl.ds(r0, 8), pl.ds(c0, 128)] = total
        return carry

    lax.fori_loop(0, live, body, 0)


def tap_products(sh_ref, g_ref, live):
    sums = {}
    for a0 in range(0, QCONV, 2):

        def body(col, accs):
            c0 = pl.multiple_of(col * 128, 128)
            out = list(accs)
            for r0 in range(0, EXT, 8):
                ga = [g_ref[a0 + k, pl.ds(r0, 8), pl.ds(c0, 128)] for k in range(2)]
                for b in range(KCONV):
                    tile = sh_ref[b, pl.ds(r0, 8), pl.ds(c0, 128)]
                    for k in range(2):
                        out[k * KCONV + b] = out[k * KCONV + b] + ga[k] * tile
            return tuple(out)

        start = tuple(jnp.zeros((8, 128), jnp.float32) for _ in range(2 * KCONV))
        res = lax.fori_loop(0, live, body, start)
        for k in range(2):
            for b in range(KCONV):
                sums[(a0 + k, b)] = res[k * KCONV + b]
    return sums


def live_tiles(block, kstart, nw):
    return jnp.clip(block + 1 - kstart // TQ, 1, nw)


def masks(block, kstart, width, rdoc_ref, kdoc_ref):
    keydoc = kdoc_ref[:, pl.ds(kstart, width)]
    ext_pos = block * TQ - PAD + lax.broadcasted_iota(jnp.int32, (EXT, width), 0)
    key_ext = kstart + lax.broadcasted_iota(jnp.int32, (EXT, width), 1)
    allowed_ext = (key_ext <= ext_pos) & (rdoc_ref[0] == keydoc)
    own_pos = block * TQ + lax.broadcasted_iota(jnp.int32, (TQ, width), 0)
    key_own = kstart + lax.broadcasted_iota(jnp.int32, (TQ, width), 1)
    allowed_own = (key_own <= own_pos) & (rdoc_ref[0, PAD:, :] == keydoc)
    return allowed_ext, allowed_own


def masked_shifts(q_ref, k_ref, head, kstart, width, allowed_ext, sh_ref):
    keys = k_ref[head, pl.ds(kstart, width), :]
    scores = lax.dot_general(
        q_ref[0, head], keys, (((1,), (1,)), ((), ())), preferred_element_type=jnp.float32
    ) * SCALE
    masked = jnp.where(allowed_ext, scores, 0.0)
    col = lax.broadcasted_iota(jnp.int32, (EXT, width), 1)
    sh_ref[0] = masked
    for b in range(1, KCONV):
        sh_ref[b] = jnp.where(col >= b, pltpu.roll(masked, b, 1), 0.0)


def fwd_kernel(toff_ref, taps_ref, mix_ref, q_ref, k_ref, v_ref, rdoc_ref, kdoc_ref,
               heads_ref, probs_ref, sh_ref, acc_ref, *, nw, length):
    width = nw * TQ
    block = toff_ref[0] + pl.program_id(0)
    kstart = window_start(block, nw, length)
    allowed_ext, allowed_own = masks(block, kstart, width, rdoc_ref, kdoc_ref)
    for head in range(2):
        masked_shifts(q_ref, k_ref, head, kstart, width, allowed_ext, sh_ref)
        tap_accumulate(sh_ref, acc_ref, taps_ref, head, live_tiles(block, kstart, nw))
        conv = acc_ref[0]
        for a in range(1, QCONV):
            conv = conv + pltpu.roll(acc_ref[a], a, 0)
        logits = jnp.where(allowed_own, conv[PAD:], -jnp.inf)
        highest = jnp.max(logits, axis=1, keepdims=True)
        highest = jnp.where(highest > -jnp.inf, highest, 0.0)
        expd = jnp.exp(logits - highest)
        denom = jnp.sum(expd, axis=1, keepdims=True)
        probs_ref[0, head] = expd / jnp.where(denom > 0.0, denom, 1.0)
    p0 = probs_ref[0, 0]
    p1 = probs_ref[0, 1]
    for c in range(2):
        mixed = (mix_ref[2 * c] * p0 + mix_ref[2 * c + 1] * p1).astype(jnp.bfloat16)
        heads_ref[0, c] = jnp.dot(
            mixed, v_ref[c, pl.ds(kstart, width), :], preferred_element_type=jnp.float32
        ).astype(jnp.bfloat16)


def attention_forward(toff, taps_flat, mix_flat, q_blocks, k_heads, v_heads, row_docs, key_docs, nw, length):
    nb_all = q_blocks.shape[0]
    width = nw * TQ
    smem = pl.BlockSpec(memory_space=pltpu.SMEM)
    flops = nb_all * 2 * (4 * EXT * width * HD + 2 * TAPS * EXT * width)
    return pl.pallas_call(
        lambda *refs: fwd_kernel(*refs, nw=nw, length=length),
        grid=(nb_all,),
        in_specs=[
            smem,
            smem,
            smem,
            pl.BlockSpec((1, 2, EXT, HD), lambda t: (t, 0, 0, 0)),
            pl.BlockSpec((2, length, HD), lambda t: (0, 0, 0)),
            pl.BlockSpec((2, length, HD), lambda t: (0, 0, 0)),
            pl.BlockSpec((1, EXT, 1), lambda t: (t, 0, 0)),
            pl.BlockSpec((1, length), lambda t: (0, 0)),
        ],
        out_specs=[
            pl.BlockSpec((1, 2, TQ, HD), lambda t: (t, 0, 0, 0)),
            pl.BlockSpec((1, 2, TQ, width), lambda t: (t, 0, 0, 0)),
        ],
        out_shape=[
            jax.ShapeDtypeStruct((nb_all, 2, TQ, HD), jnp.bfloat16),
            jax.ShapeDtypeStruct((nb_all, 2, TQ, width), jnp.float32),
        ],
        scratch_shapes=[
            pltpu.VMEM((KCONV, EXT, width), jnp.float32),
            pltpu.VMEM((QCONV, EXT, width), jnp.float32),
        ],
        compiler_params=pltpu.CompilerParams(
            dimension_semantics=("arbitrary",), vmem_limit_bytes=56 * 1024 * 1024
        ),
        cost_estimate=pl.CostEstimate(
            flops=flops, transcendentals=nb_all * 2 * TQ * width,
            bytes_accessed=nb_all * 2 * TQ * width * 4 + 4 * length * HD * 2,
        ),
    )(toff, taps_flat, mix_flat, q_blocks, k_heads, v_heads, row_docs, key_docs)


def bwd_kernel(toff_ref, taps_ref, mix_ref, q_ref, qo_ref, k_ref, v_ref, rdoc_ref, kdoc_ref,
               probs_ref, gh_ref, ght_ref, gq_ref, gk_ref, gv_ref, tacc_ref, macc_ref,
               carry_ref, sh_ref, acc_ref, g_ref, gx_ref, *, nw, length, nb, nb_all):
    width = nw * TQ
    step = pl.program_id(0)
    local = nb_all - 1 - step
    block = toff_ref[0] + local
    kstart = window_start(block, nw, length)

    @pl.when(step == 0)
    def _init():
        gk_ref[...] = jnp.zeros(gk_ref.shape, jnp.float32)
        gv_ref[...] = jnp.zeros(gv_ref.shape, jnp.float32)
        tacc_ref[...] = jnp.zeros(tacc_ref.shape, jnp.float32)
        macc_ref[...] = jnp.zeros(macc_ref.shape, jnp.float32)
        carry_ref[...] = jnp.zeros(carry_ref.shape, jnp.float32)

    allowed_ext, allowed_own = masks(block, kstart, width, rdoc_ref, kdoc_ref)
    gm = [
        lax.dot_general(
            gh_ref[0, c], v_ref[c, pl.ds(kstart, width), :], (((1,), (1,)), ((), ())),
            preferred_element_type=jnp.float32,
        )
        for c in range(2)
    ]
    probs = [probs_ref[0, 0], probs_ref[0, 1]]
    gc = []
    for e in range(2):
        gp = mix_ref[e] * gm[0] + mix_ref[2 + e] * gm[1]
        inner = jnp.sum(gp * probs[e], axis=1, keepdims=True)
        gc.append(probs[e] * (gp - inner))

    def own_sums():
        for c in range(2):
            for e in range(2):
                macc_ref[pl.ds(2 * c + e, 1), :] += jnp.sum(gm[c] * probs[e], axis=0, keepdims=True)
            mixed = (mix_ref[2 * c] * probs[0] + mix_ref[2 * c + 1] * probs[1]).astype(jnp.bfloat16)
            gv_ref[c, :, pl.ds(kstart, width)] += jnp.dot(
                ght_ref[0, c], mixed, preferred_element_type=jnp.float32
            )

    def head_taps(e):
        masked_shifts(q_ref, k_ref, e, kstart, width, allowed_ext, sh_ref)
        gcp = jnp.concatenate([jnp.zeros((PAD, width), jnp.float32), gc[e]], axis=0)
        g_ref[0] = gcp
        for a in range(1, QCONV):
            g_ref[a] = pltpu.roll(gcp, EXT - a, 0)
        sums = tap_products(sh_ref, g_ref, live_tiles(block, kstart, nw))
        for b in range(KCONV):
            for a in range(QCONV):
                tacc_ref[e * TAPS + a * KCONV + b] += sums[(a, b)]

    def head_keys(e, gs):
        gk_ref[e, :, pl.ds(kstart, width)] += jnp.dot(
            qo_ref[0, e], gs, preferred_element_type=jnp.float32
        ) * SCALE

    nxt = [carry_ref[e, :, pl.ds(kstart, width + TQ)] for e in range(2)]
    if nb < nb_all:
        pl.when(local < nb)(own_sums)
    else:
        own_sums()
    for e in range(2):
        if nb < nb_all:
            pl.when(local < nb)(lambda: head_taps(e))
        else:
            head_taps(e)
        gx_ref[pl.ds(0, TQ), pl.ds(0, width)] = gc[e]
        gx_ref[pl.ds(0, TQ), pl.ds(width, TQ)] = jnp.zeros((TQ, TQ), jnp.float32)
        gx_ref[pl.ds(TQ, PAD), :] = nxt[e]
        gxv = gx_ref[...]
        sh_ref[0] = gxv[:, :width]
        for b in range(1, KCONV):
            sh_ref[b] = pltpu.roll(gxv, width + TQ - b, 1)[:, :width]
        tap_accumulate(sh_ref, acc_ref, taps_ref, e, live_tiles(block, kstart, nw))
        gmk = acc_ref[0]
        for a in range(1, QCONV):
            gmk = gmk + pltpu.roll(acc_ref[a], EXT - a, 0)
        gs = jnp.where(allowed_own, gmk[:TQ], 0.0).astype(jnp.bfloat16)
        gq_ref[0, e] = (
            jnp.dot(gs, k_ref[e, pl.ds(kstart, width), :], preferred_element_type=jnp.float32) * SCALE
        ).astype(jnp.bfloat16)
        if nb < nb_all:
            pl.when(local < nb)(lambda: head_keys(e, gs))
        else:
            head_keys(e, gs)
    carry_ref[...] = jnp.zeros(carry_ref.shape, jnp.float32)
    for e in range(2):
        carry_ref[e, :, pl.ds(kstart, width)] = gc[e][:PAD]


def attention_backward(toff, taps_flat, mix_flat, q_blocks, q_own, k_heads, v_heads, row_docs, key_docs,
                       probs_blk, gh_blocks, nw, length, nb):
    q_own = jnp.swapaxes(q_own, 2, 3)
    gh_t = jnp.swapaxes(gh_blocks, 2, 3)
    nb_all = q_blocks.shape[0]
    width = nw * TQ
    smem = pl.BlockSpec(memory_space=pltpu.SMEM)
    rev = lambda s: nb_all - 1 - s
    flops = nb_all * 2 * (8 * TQ * width * HD + 6 * TAPS * EXT * width)
    return pl.pallas_call(
        lambda *refs: bwd_kernel(*refs, nw=nw, length=length, nb=nb, nb_all=nb_all),
        grid=(nb_all,),
        in_specs=[
            smem,
            smem,
            smem,
            pl.BlockSpec((1, 2, EXT, HD), lambda s: (rev(s), 0, 0, 0)),
            pl.BlockSpec((1, 2, HD, TQ), lambda s: (rev(s), 0, 0, 0)),
            pl.BlockSpec((2, length, HD), lambda s: (0, 0, 0)),
            pl.BlockSpec((2, length, HD), lambda s: (0, 0, 0)),
            pl.BlockSpec((1, EXT, 1), lambda s: (rev(s), 0, 0)),
            pl.BlockSpec((1, length), lambda s: (0, 0)),
            pl.BlockSpec((1, 2, TQ, width), lambda s: (rev(s), 0, 0, 0)),
            pl.BlockSpec((1, 2, TQ, HD), lambda s: (rev(s), 0, 0, 0)),
            pl.BlockSpec((1, 2, HD, TQ), lambda s: (rev(s), 0, 0, 0)),
        ],
        out_specs=[
            pl.BlockSpec((1, 2, TQ, HD), lambda s: (rev(s), 0, 0, 0)),
            pl.BlockSpec((2, HD, length), lambda s: (0, 0, 0)),
            pl.BlockSpec((2, HD, length), lambda s: (0, 0, 0)),
            pl.BlockSpec((2 * TAPS, 8, 128), lambda s: (0, 0, 0)),
            pl.BlockSpec((4, width), lambda s: (0, 0)),
        ],
        out_shape=[
            jax.ShapeDtypeStruct((nb_all, 2, TQ, HD), jnp.bfloat16),
            jax.ShapeDtypeStruct((2, HD, length), jnp.float32),
            jax.ShapeDtypeStruct((2, HD, length), jnp.float32),
            jax.ShapeDtypeStruct((2 * TAPS, 8, 128), jnp.float32),
            jax.ShapeDtypeStruct((4, width), jnp.float32),
        ],
        scratch_shapes=[
            pltpu.VMEM((2, PAD, length + TQ), jnp.float32),
            pltpu.VMEM((KCONV, EXT, width), jnp.float32),
            pltpu.VMEM((QCONV, EXT, width), jnp.float32),
            pltpu.VMEM((QCONV, EXT, width), jnp.float32),
            pltpu.VMEM((EXT, width + TQ), jnp.float32),
        ],
        compiler_params=pltpu.CompilerParams(
            dimension_semantics=("arbitrary",), vmem_limit_bytes=60 * 1024 * 1024
        ),
        cost_estimate=pl.CostEstimate(
            flops=flops, transcendentals=0,
            bytes_accessed=nb_all * 2 * TQ * width * 4 + 8 * length * HD * 4,
        ),
    )(toff, taps_flat, mix_flat, q_blocks, q_own, k_heads, v_heads, row_docs, key_docs, probs_blk, gh_blocks, gh_t)


def shards_body(
    inputs,
    doc_ids,
    w_query,
    w_key,
    w_value,
    w_out,
    gain_attn,
    gain_ffn,
    conv_taps,
    head_mix,
    w_gate,
    w_up,
    w_down,
    cotangent,
):
    row_dev, blk, width = inputs.shape
    assert row_dev == 1
    seq_count = lax.axis_size("seq")
    row_count = lax.axis_size("row")
    seq_index = lax.axis_index("seq")
    row_index = lax.axis_index("row")
    length = blk * seq_count
    groups = HEADS // 2
    assert seq_count % groups == 0
    splits = seq_count // groups
    span = length // splits
    pw = 2 * HD
    pair = seq_index // splits
    part = seq_index % splits
    q0 = part * span

    flat_in = inputs.reshape(blk, width)
    scale_one = rms_scale(flat_in)
    normed = (flat_in * scale_one * gain_attn).astype(jnp.bfloat16)
    normed_all = lax.all_gather(normed, "seq", axis=0, tiled=True)

    wq_g = lax.dynamic_slice_in_dim(w_query, pair * pw, pw, 1)
    wk_g = lax.dynamic_slice_in_dim(w_key, pair * pw, pw, 1)
    wv_g = lax.dynamic_slice_in_dim(w_value, pair * pw, pw, 1)
    wo_g = lax.dynamic_slice_in_dim(w_out, pair * pw, pw, 0)
    taps = lax.dynamic_slice_in_dim(conv_taps, pair * 2, 2, 0)
    mixing = lax.dynamic_index_in_dim(head_mix, pair, 0, keepdims=False)

    k_all = project(normed_all, wk_g).astype(jnp.bfloat16)
    v_all = project(normed_all, wv_g).astype(jnp.bfloat16)
    k3 = k_all.reshape(length, 2, HD)
    v3 = v_all.reshape(length, 2, HD)

    docs = doc_ids[0]
    nb = span // TQ
    extra = 1 if splits > 1 else 0
    nb_all = nb + extra
    doc_cap = length // 2
    nw = min(length // TQ, (doc_cap + QCONV - 2 + TQ - 1) // TQ + 1)
    q_tail = normed_pad_tail(normed_all, extra)
    q_rows = project(lax.dynamic_slice_in_dim(q_tail, q0, nb_all * TQ + PAD, 0), wq_g).astype(jnp.bfloat16)
    q_blocks = jnp.stack([q_rows[t * TQ : t * TQ + EXT] for t in range(nb_all)])
    q_blocks = jnp.transpose(q_blocks.reshape(nb_all, EXT, 2, HD), (0, 2, 1, 3))
    q_own = q_blocks[:, :, PAD:]
    k_heads = jnp.transpose(k3, (1, 0, 2))
    v_heads = jnp.transpose(v3, (1, 0, 2))
    docs_tail = jnp.pad(docs, (PAD, TQ * extra), constant_values=-1)
    doc_rows = lax.dynamic_slice_in_dim(docs_tail, q0, nb_all * TQ + PAD, 0)
    row_docs = jnp.stack([doc_rows[t * TQ : t * TQ + EXT] for t in range(nb_all)])[:, :, None]
    key_docs = docs[None, :]
    toff = (q0 // TQ).astype(jnp.int32).reshape(1)
    taps_flat = taps.reshape(2 * QCONV * KCONV)
    mix_flat = mixing.reshape(4)
    heads_blk, probs_blk = attention_forward(
        toff, taps_flat, mix_flat, q_blocks, k_heads, v_heads, row_docs, key_docs, nw, length
    )
    heads_own = jnp.transpose(heads_blk[:nb], (0, 2, 1, 3)).reshape(span, pw)

    def to_tokens(values):
        cols = values.shape[1]
        if splits == 1:
            full = values
        else:
            full = lax.dynamic_update_slice_in_dim(
                jnp.zeros((length, cols), values.dtype), values, q0, 0
            )
        got = lax.all_to_all(full, "seq", 0, 0, tiled=True)
        got = got.reshape(groups, splits, blk, cols)
        if splits > 1:
            got = jnp.sum(got.astype(jnp.float32), axis=1).astype(values.dtype)
        else:
            got = got[:, 0]
        return got

    heads_tok = jnp.transpose(to_tokens(heads_own), (1, 0, 2)).reshape(blk, width)
    middle = flat_in + project(heads_tok, w_out)
    scale_two = rms_scale(middle)
    normed_ffn = (middle * scale_two * gain_ffn).astype(jnp.bfloat16)
    hid_width = w_gate.shape[1]
    packed = jnp.concatenate([w_gate, w_up, jnp.transpose(w_down)], axis=1)
    pieces = [packed]
    for k in range(1, row_count):
        route = [(i, (i + k) % row_count) for i in range(row_count)]
        pieces.append(lax.ppermute(packed, "row", route))
    rev = jnp.stack(pieces[::-1] + pieces[::-1])
    full_w = lax.dynamic_slice_in_dim(rev, row_count - 1 - row_index, row_count, 0)
    full_w = full_w.reshape(row_count * packed.shape[0], packed.shape[1])
    joint = full_w[:, : 2 * hid_width]
    down_full = jnp.transpose(full_w[:, 2 * hid_width :])
    ffn_rows = lax.all_gather(normed_ffn, "seq", axis=0, tiled=True)
    gate_up = project(ffn_rows, joint)
    gate_vals = gate_up[:, :hid_width]
    up_vals = gate_up[:, hid_width:]
    hidden = (jax.nn.silu(gate_vals) * up_vals).astype(jnp.bfloat16)
    ffn_part = project(hidden, down_full).astype(jnp.bfloat16)
    cot_flat = cotangent.reshape(blk, width)
    cot_low = cot_flat.astype(jnp.bfloat16)
    cot_rows = lax.all_gather(cot_low, "seq", axis=0, tiled=True)
    grad_hidden = contract_cols(cot_rows, down_full)
    grad_down_part = contract_rows(hidden, cot_rows)
    sigmoid_gate = jax.nn.sigmoid(gate_vals)
    grad_gate_vals = grad_hidden * up_vals * sigmoid_gate * (1.0 + gate_vals * (1.0 - sigmoid_gate))
    grad_up_vals = grad_hidden * gate_vals * sigmoid_gate
    grad_joint = jnp.concatenate([grad_gate_vals, grad_up_vals], axis=1).astype(jnp.bfloat16)
    grad_joint_w = contract_rows(ffn_rows, grad_joint)
    grad_normed_ffn = lax.psum_scatter(
        contract_cols(grad_joint, joint).astype(jnp.bfloat16),
        "seq",
        scatter_dimension=0,
        tiled=True,
    ).astype(jnp.float32)
    grad_pack = jnp.concatenate([grad_joint_w, jnp.transpose(grad_down_part)], axis=1)
    band = grad_pack.shape[0] // row_count
    grad_blocks = grad_pack.reshape(row_count, band, grad_pack.shape[1]).astype(jnp.bfloat16)
    ffn_grad = lax.dynamic_index_in_dim(grad_blocks, row_index, 0, keepdims=False).astype(jnp.float32)
    for k in range(1, row_count):
        route = [(i, (i + k) % row_count) for i in range(row_count)]
        sent = lax.dynamic_index_in_dim(grad_blocks, (row_index + k) % row_count, 0, keepdims=False)
        ffn_grad = ffn_grad + lax.ppermute(sent, "row", route).astype(jnp.float32)
    grad_w_gate = ffn_grad[:, :hid_width]
    grad_w_up = ffn_grad[:, hid_width : 2 * hid_width]
    grad_w_down = jnp.transpose(ffn_grad[:, 2 * hid_width :])
    gain_ffn_part = jnp.sum(grad_normed_ffn * middle * scale_two, axis=0)
    scaled_two = grad_normed_ffn * gain_ffn
    grad_middle = (
        cot_flat
        + scale_two * scaled_two
        - middle * scale_two**3 * jnp.mean(scaled_two * middle, axis=-1, keepdims=True)
    )
    grad_attn = grad_middle.astype(jnp.bfloat16)
    grad_attn_all = lax.all_gather(grad_attn, "seq", axis=0, tiled=True)
    ffn_part, grad_attn_all = lax.optimization_barrier((ffn_part, grad_attn_all))
    ffn_out = lax.psum_scatter(ffn_part, "seq", scatter_dimension=0, tiled=True).astype(jnp.float32)
    outputs = middle + ffn_out
    grad_attn_tail = jnp.pad(grad_attn_all, ((0, TQ * extra), (0, 0)))
    grad_heads_x = contract_cols(
        lax.dynamic_slice_in_dim(grad_attn_tail, q0, nb_all * TQ, 0), wo_g
    ).astype(jnp.bfloat16)
    gh_blocks = jnp.transpose(grad_heads_x.reshape(nb_all, TQ, 2, HD), (0, 2, 1, 3))
    grad_out_part = contract_rows(heads_own, lax.dynamic_slice_in_dim(grad_attn_all, q0, span, 0))
    gq_blk, gk_heads, gv_heads, tap_acc, mix_acc = attention_backward(
        toff, taps_flat, mix_flat, q_blocks, q_own, k_heads, v_heads, row_docs, key_docs,
        probs_blk, gh_blocks, nw, length, nb,
    )
    grad_q_own = jnp.transpose(gq_blk[:nb], (0, 2, 1, 3)).reshape(span, pw)
    grad_k_part = jnp.transpose(gk_heads, (2, 0, 1)).reshape(length, pw)
    grad_v_part = jnp.transpose(gv_heads, (2, 0, 1)).reshape(length, pw)
    grad_taps_part = jnp.sum(tap_acc, axis=(1, 2)).reshape(2, QCONV, KCONV)
    grad_mix_part = jnp.sum(mix_acc, axis=1).reshape(2, 2)

    def split_sum(values):
        if splits == 1:
            return values
        total = values
        for step in range(1, splits):
            route = []
            for s in range(seq_count):
                base = (s // splits) * splits
                route.append((s, base + (s - base + step) % splits))
            total = total + lax.ppermute(values, "seq", route)
        return total

    grad_k_low = split_sum(grad_k_part).astype(jnp.bfloat16)
    grad_v_low = split_sum(grad_v_part).astype(jnp.bfloat16)
    grad_k_own = lax.dynamic_slice_in_dim(grad_k_low, q0, span, 0)
    grad_v_own = lax.dynamic_slice_in_dim(grad_v_low, q0, span, 0)

    normed_own = lax.dynamic_slice_in_dim(normed_all, q0, span, 0)
    rows_per_dev = width // (row_count * seq_count)

    partials = jnp.stack(
        [
            contract_rows(normed_own, grad_q_own),
            contract_rows(normed_own, grad_k_own),
            contract_rows(normed_own, grad_v_own),
        ]
    )
    red = lax.psum_scatter(partials.astype(jnp.bfloat16), "row", scatter_dimension=1, tiled=True)
    got = lax.all_to_all(red, "seq", 1, 1, tiled=True).astype(jnp.float32)
    got = got.reshape(3, groups, splits, rows_per_dev, pw).sum(axis=2)
    got = jnp.transpose(got, (0, 2, 1, 3)).reshape(3, rows_per_dev, width)
    grad_w_query, grad_w_key, grad_w_value = got[0], got[1], got[2]

    red_out = lax.psum_scatter(grad_out_part, "row", scatter_dimension=0, tiled=True)
    red_out = red_out.reshape(splits, rows_per_dev, width)
    grad_w_out = jnp.zeros((rows_per_dev, width), jnp.float32)
    for src_part in range(splits):
        for j in range(splits):
            route = []
            for r in range(row_count):
                for g in range(groups):
                    src = r * seq_count + g * splits + src_part
                    dst = g * row_count * splits + r * splits + j
                    route.append((src, dst))
            grad_w_out = grad_w_out + lax.ppermute(red_out[j], ("row", "seq"), route)

    grad_tok = to_tokens(jnp.concatenate([grad_q_own, grad_k_own, grad_v_own], axis=1))
    grad_tok = grad_tok.reshape(groups, blk, 3, pw)
    gq_tok = jnp.transpose(grad_tok[:, :, 0], (1, 0, 2)).reshape(blk, width)
    gk_tok = jnp.transpose(grad_tok[:, :, 1], (1, 0, 2)).reshape(blk, width)
    gv_tok = jnp.transpose(grad_tok[:, :, 2], (1, 0, 2)).reshape(blk, width)
    grad_normed = (
        contract_cols(gq_tok, w_query) + contract_cols(gk_tok, w_key) + contract_cols(gv_tok, w_value)
    )
    gain_attn_part = jnp.sum(grad_normed * flat_in * scale_one, axis=0)
    scaled_one = grad_normed * gain_attn
    grad_inputs = (
        grad_middle
        + scale_one * scaled_one
        - flat_in * scale_one**3 * jnp.mean(scaled_one * flat_in, axis=-1, keepdims=True)
    )
    taps_full = lax.dynamic_update_slice_in_dim(
        jnp.zeros((HEADS, QCONV, KCONV), jnp.float32), grad_taps_part, pair * 2, 0
    )
    mix_full = lax.dynamic_update_slice_in_dim(
        jnp.zeros((groups, 2, 2), jnp.float32), grad_mix_part[None], pair, 0
    )
    small = jnp.concatenate(
        [gain_attn_part, gain_ffn_part, taps_full.reshape(-1), mix_full.reshape(-1)]
    )
    devices = row_count * seq_count
    assert devices & (devices - 1) == 0
    mask = 1
    while mask < devices:
        route = [(i, i ^ mask) for i in range(devices)]
        small = small + lax.ppermute(small, ("row", "seq"), route)
        mask *= 2
    gain_rows = width // (row_count * seq_count)
    gain_at = (row_index * seq_count + seq_index) * gain_rows
    grad_gain_attn = lax.dynamic_slice_in_dim(small, gain_at, gain_rows, 0)
    grad_gain_ffn = lax.dynamic_slice_in_dim(small, width + gain_at, gain_rows, 0)
    grad_taps = small[2 * width : 2 * width + HEADS * TAPS].reshape(HEADS, QCONV, KCONV)
    grad_mix = small[2 * width + HEADS * TAPS :].reshape(groups, 2, 2)
    return (
        outputs.reshape(row_dev, blk, width),
        grad_inputs.reshape(row_dev, blk, width),
        grad_w_query,
        grad_w_key,
        grad_w_value,
        grad_w_out,
        grad_gain_attn,
        grad_gain_ffn,
        grad_taps,
        grad_mix,
        grad_w_gate,
        grad_w_up,
        grad_w_down,
    )


def solution(mesh):
    return jax.shard_map(
        shards_body,
        mesh=mesh,
        in_specs=(
            P("row", "seq", None),
            P("row", None),
            P(),
            P(),
            P(),
            P(),
            P(),
            P(),
            P(),
            P(),
            P("row", "seq"),
            P("row", "seq"),
            P("seq", "row"),
            P("row", "seq", None),
        ),
        out_specs=(
            P("row", "seq", None),
            P("row", "seq", None),
            P(("row", "seq"), None),
            P(("row", "seq"), None),
            P(("row", "seq"), None),
            P(("row", "seq"), None),
            P(("row", "seq")),
            P(("row", "seq")),
            P(),
            P(),
            P("row", "seq"),
            P("row", "seq"),
            P("seq", "row"),
        ),
        check_vma=False,
    )
```

```python
import jax
import jax.numpy as jnp
from jax import lax
from jax.sharding import PartitionSpec as P
from jax.experimental import pallas as pl
from jax.experimental.pallas import tpu as pltpu

HEADS = 16
HD = 96
QCONV = 6
KCONV = 11
PAD = 8
TQ = 128
EXT = TQ + PAD
SCALE = HD ** (-0.5)
TAPS = QCONV * KCONV

epsilon = 1e-06


def rms_scale(values):
    return lax.rsqrt(jnp.mean(values * values, axis=-1, keepdims=True) + epsilon)


def project(values, weight):
    return jnp.dot(values, weight, preferred_element_type=jnp.float32)


def contract_rows(left, right):
    return lax.dot_general(
        left, right, (((0,), (0,)), ((), ())), preferred_element_type=jnp.float32
    )


def contract_cols(left, right):
    return lax.dot_general(
        left, right, (((1,), (1,)), ((), ())), preferred_element_type=jnp.float32
    )


def normed_pad_tail(values, extra):
    return jnp.pad(values, ((PAD, TQ * extra), (0, 0)))


def window_start(block, nw, length):
    return pl.multiple_of(jnp.clip((block - nw + 1) * TQ, 0, length - nw * TQ), TQ)


def tap_accumulate(sh_ref, acc_ref, taps_ref, head, live):

    def body(col, carry):
        c0 = pl.multiple_of(col * 128, 128)
        for r0 in range(0, EXT, 8):
            tiles = [sh_ref[b, pl.ds(r0, 8), pl.ds(c0, 128)] for b in range(KCONV)]
            for a in range(QCONV):
                base = head * TAPS + a * KCONV
                total = taps_ref[base] * tiles[0]
                for b in range(1, KCONV):
                    total = total + taps_ref[base + b] * tiles[b]
                acc_ref[a, pl.ds(r0, 8), pl.ds(c0, 128)] = total
        return carry

    lax.fori_loop(0, live, body, 0)


def tap_products(sh_ref, g_ref, live):
    sums = {}
    for a0 in range(0, QCONV, 2):

        def body(col, accs):
            c0 = pl.multiple_of(col * 128, 128)
            out = list(accs)
            for r0 in range(0, EXT, 8):
                ga = [g_ref[a0 + k, pl.ds(r0, 8), pl.ds(c0, 128)] for k in range(2)]
                for b in range(KCONV):
                    tile = sh_ref[b, pl.ds(r0, 8), pl.ds(c0, 128)]
                    for k in range(2):
                        out[k * KCONV + b] = out[k * KCONV + b] + ga[k] * tile
            return tuple(out)

        start = tuple(jnp.zeros((8, 128), jnp.float32) for _ in range(2 * KCONV))
        res = lax.fori_loop(0, live, body, start)
        for k in range(2):
            for b in range(KCONV):
                sums[(a0 + k, b)] = res[k * KCONV + b]
    return sums


def live_tiles(block, kstart, nw):
    return jnp.clip(block + 1 - kstart // TQ, 1, nw)


def masks(block, kstart, width, rdoc_ref, kdoc_ref):
    keydoc = kdoc_ref[:, pl.ds(kstart, width)]
    ext_pos = block * TQ - PAD + lax.broadcasted_iota(jnp.int32, (EXT, width), 0)
    key_ext = kstart + lax.broadcasted_iota(jnp.int32, (EXT, width), 1)
    allowed_ext = (key_ext <= ext_pos) & (rdoc_ref[0] == keydoc)
    own_pos = block * TQ + lax.broadcasted_iota(jnp.int32, (TQ, width), 0)
    key_own = kstart + lax.broadcasted_iota(jnp.int32, (TQ, width), 1)
    allowed_own = (key_own <= own_pos) & (rdoc_ref[0, PAD:, :] == keydoc)
    return allowed_ext, allowed_own


def masked_shifts(q_ref, k_ref, head, kstart, width, allowed_ext, sh_ref):
    keys = k_ref[head, pl.ds(kstart, width), :]
    scores = lax.dot_general(
        q_ref[0, head], keys, (((1,), (1,)), ((), ())), preferred_element_type=jnp.float32
    ) * SCALE
    masked = jnp.where(allowed_ext, scores, 0.0)
    col = lax.broadcasted_iota(jnp.int32, (EXT, width), 1)
    sh_ref[0] = masked
    for b in range(1, KCONV):
        sh_ref[b] = jnp.where(col >= b, pltpu.roll(masked, b, 1), 0.0)


def fwd_kernel(toff_ref, taps_ref, mix_ref, q_ref, k_ref, v_ref, rdoc_ref, kdoc_ref,
               heads_ref, probs_ref, sh_ref, acc_ref, *, nw, length):
    width = nw * TQ
    block = toff_ref[0] + pl.program_id(0)
    kstart = window_start(block, nw, length)
    allowed_ext, allowed_own = masks(block, kstart, width, rdoc_ref, kdoc_ref)
    for head in range(2):
        masked_shifts(q_ref, k_ref, head, kstart, width, allowed_ext, sh_ref)
        tap_accumulate(sh_ref, acc_ref, taps_ref, head, live_tiles(block, kstart, nw))
        conv = acc_ref[0]
        for a in range(1, QCONV):
            conv = conv + pltpu.roll(acc_ref[a], a, 0)
        logits = jnp.where(allowed_own, conv[PAD:], -jnp.inf)
        highest = jnp.max(logits, axis=1, keepdims=True)
        highest = jnp.where(highest > -jnp.inf, highest, 0.0)
        expd = jnp.exp(logits - highest)
        denom = jnp.sum(expd, axis=1, keepdims=True)
        probs_ref[0, head] = expd / jnp.where(denom > 0.0, denom, 1.0)
    p0 = probs_ref[0, 0]
    p1 = probs_ref[0, 1]
    for c in range(2):
        mixed = (mix_ref[2 * c] * p0 + mix_ref[2 * c + 1] * p1).astype(jnp.bfloat16)
        heads_ref[0, c] = jnp.dot(
            mixed, v_ref[c, pl.ds(kstart, width), :], preferred_element_type=jnp.float32
        ).astype(jnp.bfloat16)


def attention_forward(toff, taps_flat, mix_flat, q_blocks, k_heads, v_heads, row_docs, key_docs, nw, length):
    nb_all = q_blocks.shape[0]
    width = nw * TQ
    smem = pl.BlockSpec(memory_space=pltpu.SMEM)
    flops = nb_all * 2 * (4 * EXT * width * HD + 2 * TAPS * EXT * width)
    return pl.pallas_call(
        lambda *refs: fwd_kernel(*refs, nw=nw, length=length),
        grid=(nb_all,),
        in_specs=[
            smem,
            smem,
            smem,
            pl.BlockSpec((1, 2, EXT, HD), lambda t: (t, 0, 0, 0)),
            pl.BlockSpec((2, length, HD), lambda t: (0, 0, 0)),
            pl.BlockSpec((2, length, HD), lambda t: (0, 0, 0)),
            pl.BlockSpec((1, EXT, 1), lambda t: (t, 0, 0)),
            pl.BlockSpec((1, length), lambda t: (0, 0)),
        ],
        out_specs=[
            pl.BlockSpec((1, 2, TQ, HD), lambda t: (t, 0, 0, 0)),
            pl.BlockSpec((1, 2, TQ, width), lambda t: (t, 0, 0, 0)),
        ],
        out_shape=[
            jax.ShapeDtypeStruct((nb_all, 2, TQ, HD), jnp.bfloat16),
            jax.ShapeDtypeStruct((nb_all, 2, TQ, width), jnp.float32),
        ],
        scratch_shapes=[
            pltpu.VMEM((KCONV, EXT, width), jnp.float32),
            pltpu.VMEM((QCONV, EXT, width), jnp.float32),
        ],
        compiler_params=pltpu.CompilerParams(
            dimension_semantics=("arbitrary",), vmem_limit_bytes=56 * 1024 * 1024
        ),
        cost_estimate=pl.CostEstimate(
            flops=flops, transcendentals=nb_all * 2 * TQ * width,
            bytes_accessed=nb_all * 2 * TQ * width * 4 + 4 * length * HD * 2,
        ),
    )(toff, taps_flat, mix_flat, q_blocks, k_heads, v_heads, row_docs, key_docs)


def bwd_kernel(toff_ref, taps_ref, mix_ref, q_ref, qo_ref, k_ref, v_ref, rdoc_ref, kdoc_ref,
               probs_ref, gh_ref, ght_ref, gq_ref, gk_ref, gv_ref, tacc_ref, macc_ref,
               carry_ref, sh_ref, acc_ref, g_ref, gx_ref, *, nw, length, nb, nb_all):
    width = nw * TQ
    step = pl.program_id(0)
    local = nb_all - 1 - step
    block = toff_ref[0] + local
    kstart = window_start(block, nw, length)

    @pl.when(step == 0)
    def _init():
        gk_ref[...] = jnp.zeros(gk_ref.shape, jnp.float32)
        gv_ref[...] = jnp.zeros(gv_ref.shape, jnp.float32)
        tacc_ref[...] = jnp.zeros(tacc_ref.shape, jnp.float32)
        macc_ref[...] = jnp.zeros(macc_ref.shape, jnp.float32)
        carry_ref[...] = jnp.zeros(carry_ref.shape, jnp.float32)

    allowed_ext, allowed_own = masks(block, kstart, width, rdoc_ref, kdoc_ref)
    gm = [
        lax.dot_general(
            gh_ref[0, c], v_ref[c, pl.ds(kstart, width), :], (((1,), (1,)), ((), ())),
            preferred_element_type=jnp.float32,
        )
        for c in range(2)
    ]
    probs = [probs_ref[0, 0], probs_ref[0, 1]]
    gc = []
    for e in range(2):
        gp = mix_ref[e] * gm[0] + mix_ref[2 + e] * gm[1]
        inner = jnp.sum(gp * probs[e], axis=1, keepdims=True)
        gc.append(probs[e] * (gp - inner))

    def own_sums():
        for c in range(2):
            for e in range(2):
                macc_ref[pl.ds(2 * c + e, 1), :] += jnp.sum(gm[c] * probs[e], axis=0, keepdims=True)
            mixed = (mix_ref[2 * c] * probs[0] + mix_ref[2 * c + 1] * probs[1]).astype(jnp.bfloat16)
            gv_ref[c, :, pl.ds(kstart, width)] += jnp.dot(
                ght_ref[0, c], mixed, preferred_element_type=jnp.float32
            )

    def head_taps(e):
        masked_shifts(q_ref, k_ref, e, kstart, width, allowed_ext, sh_ref)
        gcp = jnp.concatenate([jnp.zeros((PAD, width), jnp.float32), gc[e]], axis=0)
        g_ref[0] = gcp
        for a in range(1, QCONV):
            g_ref[a] = pltpu.roll(gcp, EXT - a, 0)
        sums = tap_products(sh_ref, g_ref, live_tiles(block, kstart, nw))
        for b in range(KCONV):
            for a in range(QCONV):
                tacc_ref[e * TAPS + a * KCONV + b] += sums[(a, b)]

    def head_keys(e, gs):
        gk_ref[e, :, pl.ds(kstart, width)] += jnp.dot(
            qo_ref[0, e], gs, preferred_element_type=jnp.float32
        ) * SCALE

    nxt = [carry_ref[e, :, pl.ds(kstart, width + TQ)] for e in range(2)]
    if nb < nb_all:
        pl.when(local < nb)(own_sums)
    else:
        own_sums()
    for e in range(2):
        if nb < nb_all:
            pl.when(local < nb)(lambda: head_taps(e))
        else:
            head_taps(e)
        gx_ref[pl.ds(0, TQ), pl.ds(0, width)] = gc[e]
        gx_ref[pl.ds(0, TQ), pl.ds(width, TQ)] = jnp.zeros((TQ, TQ), jnp.float32)
        gx_ref[pl.ds(TQ, PAD), :] = nxt[e]
        gxv = gx_ref[...]
        sh_ref[0] = gxv[:, :width]
        for b in range(1, KCONV):
            sh_ref[b] = pltpu.roll(gxv, width + TQ - b, 1)[:, :width]
        tap_accumulate(sh_ref, acc_ref, taps_ref, e, live_tiles(block, kstart, nw))
        gmk = acc_ref[0]
        for a in range(1, QCONV):
            gmk = gmk + pltpu.roll(acc_ref[a], EXT - a, 0)
        gs = jnp.where(allowed_own, gmk[:TQ], 0.0).astype(jnp.bfloat16)
        gq_ref[0, e] = (
            jnp.dot(gs, k_ref[e, pl.ds(kstart, width), :], preferred_element_type=jnp.float32) * SCALE
        ).astype(jnp.bfloat16)
        if nb < nb_all:
            pl.when(local < nb)(lambda: head_keys(e, gs))
        else:
            head_keys(e, gs)
    carry_ref[...] = jnp.zeros(carry_ref.shape, jnp.float32)
    for e in range(2):
        carry_ref[e, :, pl.ds(kstart, width)] = gc[e][:PAD]


def attention_backward(toff, taps_flat, mix_flat, q_blocks, q_own, k_heads, v_heads, row_docs, key_docs,
                       probs_blk, gh_blocks, nw, length, nb):
    q_own = jnp.swapaxes(q_own, 2, 3)
    gh_t = jnp.swapaxes(gh_blocks, 2, 3)
    nb_all = q_blocks.shape[0]
    width = nw * TQ
    smem = pl.BlockSpec(memory_space=pltpu.SMEM)
    rev = lambda s: nb_all - 1 - s
    flops = nb_all * 2 * (8 * TQ * width * HD + 6 * TAPS * EXT * width)
    return pl.pallas_call(
        lambda *refs: bwd_kernel(*refs, nw=nw, length=length, nb=nb, nb_all=nb_all),
        grid=(nb_all,),
        in_specs=[
            smem,
            smem,
            smem,
            pl.BlockSpec((1, 2, EXT, HD), lambda s: (rev(s), 0, 0, 0)),
            pl.BlockSpec((1, 2, HD, TQ), lambda s: (rev(s), 0, 0, 0)),
            pl.BlockSpec((2, length, HD), lambda s: (0, 0, 0)),
            pl.BlockSpec((2, length, HD), lambda s: (0, 0, 0)),
            pl.BlockSpec((1, EXT, 1), lambda s: (rev(s), 0, 0)),
            pl.BlockSpec((1, length), lambda s: (0, 0)),
            pl.BlockSpec((1, 2, TQ, width), lambda s: (rev(s), 0, 0, 0)),
            pl.BlockSpec((1, 2, TQ, HD), lambda s: (rev(s), 0, 0, 0)),
            pl.BlockSpec((1, 2, HD, TQ), lambda s: (rev(s), 0, 0, 0)),
        ],
        out_specs=[
            pl.BlockSpec((1, 2, TQ, HD), lambda s: (rev(s), 0, 0, 0)),
            pl.BlockSpec((2, HD, length), lambda s: (0, 0, 0)),
            pl.BlockSpec((2, HD, length), lambda s: (0, 0, 0)),
            pl.BlockSpec((2 * TAPS, 8, 128), lambda s: (0, 0, 0)),
            pl.BlockSpec((4, width), lambda s: (0, 0)),
        ],
        out_shape=[
            jax.ShapeDtypeStruct((nb_all, 2, TQ, HD), jnp.bfloat16),
            jax.ShapeDtypeStruct((2, HD, length), jnp.float32),
            jax.ShapeDtypeStruct((2, HD, length), jnp.float32),
            jax.ShapeDtypeStruct((2 * TAPS, 8, 128), jnp.float32),
            jax.ShapeDtypeStruct((4, width), jnp.float32),
        ],
        scratch_shapes=[
            pltpu.VMEM((2, PAD, length + TQ), jnp.float32),
            pltpu.VMEM((KCONV, EXT, width), jnp.float32),
            pltpu.VMEM((QCONV, EXT, width), jnp.float32),
            pltpu.VMEM((QCONV, EXT, width), jnp.float32),
            pltpu.VMEM((EXT, width + TQ), jnp.float32),
        ],
        compiler_params=pltpu.CompilerParams(
            dimension_semantics=("arbitrary",), vmem_limit_bytes=60 * 1024 * 1024
        ),
        cost_estimate=pl.CostEstimate(
            flops=flops, transcendentals=0,
            bytes_accessed=nb_all * 2 * TQ * width * 4 + 8 * length * HD * 4,
        ),
    )(toff, taps_flat, mix_flat, q_blocks, q_own, k_heads, v_heads, row_docs, key_docs, probs_blk, gh_blocks, gh_t)


def shards_body(
    inputs,
    doc_ids,
    w_query,
    w_key,
    w_value,
    w_out,
    gain_attn,
    gain_ffn,
    conv_taps,
    head_mix,
    w_gate,
    w_up,
    w_down,
    cotangent,
):
    row_dev, blk, width = inputs.shape
    assert row_dev == 1
    seq_count = lax.axis_size("seq")
    row_count = lax.axis_size("row")
    seq_index = lax.axis_index("seq")
    row_index = lax.axis_index("row")
    length = blk * seq_count
    groups = HEADS // 2
    assert seq_count % groups == 0
    splits = seq_count // groups
    span = length // splits
    pw = 2 * HD
    pair = seq_index // splits
    part = seq_index % splits
    q0 = part * span

    flat_in = inputs.reshape(blk, width)
    scale_one = rms_scale(flat_in)
    normed = (flat_in * scale_one * gain_attn).astype(jnp.bfloat16)
    normed_all = lax.all_gather(normed, "seq", axis=0, tiled=True)

    wq_g = lax.dynamic_slice_in_dim(w_query, pair * pw, pw, 1)
    wk_g = lax.dynamic_slice_in_dim(w_key, pair * pw, pw, 1)
    wv_g = lax.dynamic_slice_in_dim(w_value, pair * pw, pw, 1)
    wo_g = lax.dynamic_slice_in_dim(w_out, pair * pw, pw, 0)
    taps = lax.dynamic_slice_in_dim(conv_taps, pair * 2, 2, 0)
    mixing = lax.dynamic_index_in_dim(head_mix, pair, 0, keepdims=False)

    k_all = project(normed_all, wk_g).astype(jnp.bfloat16)
    v_all = project(normed_all, wv_g).astype(jnp.bfloat16)
    k3 = k_all.reshape(length, 2, HD)
    v3 = v_all.reshape(length, 2, HD)

    docs = doc_ids[0]
    nb = span // TQ
    extra = 1 if splits > 1 else 0
    nb_all = nb + extra
    doc_cap = length // 2
    nw = min(length // TQ, (doc_cap + QCONV - 2 + TQ - 1) // TQ + 1)
    q_tail = normed_pad_tail(normed_all, extra)
    q_rows = project(lax.dynamic_slice_in_dim(q_tail, q0, nb_all * TQ + PAD, 0), wq_g).astype(jnp.bfloat16)
    q_blocks = jnp.stack([q_rows[t * TQ : t * TQ + EXT] for t in range(nb_all)])
    q_blocks = jnp.transpose(q_blocks.reshape(nb_all, EXT, 2, HD), (0, 2, 1, 3))
    q_own = q_blocks[:, :, PAD:]
    k_heads = jnp.transpose(k3, (1, 0, 2))
    v_heads = jnp.transpose(v3, (1, 0, 2))
    docs_tail = jnp.pad(docs, (PAD, TQ * extra), constant_values=-1)
    doc_rows = lax.dynamic_slice_in_dim(docs_tail, q0, nb_all * TQ + PAD, 0)
    row_docs = jnp.stack([doc_rows[t * TQ : t * TQ + EXT] for t in range(nb_all)])[:, :, None]
    key_docs = docs[None, :]
    toff = (q0 // TQ).astype(jnp.int32).reshape(1)
    taps_flat = taps.reshape(2 * QCONV * KCONV)
    mix_flat = mixing.reshape(4)
    heads_blk, probs_blk = attention_forward(
        toff, taps_flat, mix_flat, q_blocks, k_heads, v_heads, row_docs, key_docs, nw, length
    )
    heads_own = jnp.transpose(heads_blk[:nb], (0, 2, 1, 3)).reshape(span, pw)

    def to_tokens(values):
        cols = values.shape[1]
        if splits == 1:
            full = values
        else:
            full = lax.dynamic_update_slice_in_dim(
                jnp.zeros((length, cols), values.dtype), values, q0, 0
            )
        got = lax.all_to_all(full, "seq", 0, 0, tiled=True)
        got = got.reshape(groups, splits, blk, cols)
        if splits > 1:
            got = jnp.sum(got.astype(jnp.float32), axis=1).astype(values.dtype)
        else:
            got = got[:, 0]
        return got

    heads_tok = jnp.transpose(to_tokens(heads_own), (1, 0, 2)).reshape(blk, width)
    middle = flat_in + project(heads_tok, w_out)
    scale_two = rms_scale(middle)
    normed_ffn = (middle * scale_two * gain_ffn).astype(jnp.bfloat16)
    hid_width = w_gate.shape[1]
    packed = jnp.concatenate([w_gate, w_up, jnp.transpose(w_down)], axis=1)
    pieces = [packed]
    for k in range(1, row_count):
        route = [(i, (i + k) % row_count) for i in range(row_count)]
        pieces.append(lax.ppermute(packed, "row", route))
    rev = jnp.stack(pieces[::-1] + pieces[::-1])
    full_w = lax.dynamic_slice_in_dim(rev, row_count - 1 - row_index, row_count, 0)
    full_w = full_w.reshape(row_count * packed.shape[0], packed.shape[1])
    joint = full_w[:, : 2 * hid_width]
    down_full = jnp.transpose(full_w[:, 2 * hid_width :])
    ffn_rows = lax.all_gather(normed_ffn, "seq", axis=0, tiled=True)
    gate_up = project(ffn_rows, joint)
    gate_vals = gate_up[:, :hid_width]
    up_vals = gate_up[:, hid_width:]
    hidden = (jax.nn.silu(gate_vals) * up_vals).astype(jnp.bfloat16)
    ffn_part = project(hidden, down_full).astype(jnp.bfloat16)
    cot_flat = cotangent.reshape(blk, width)
    cot_low = cot_flat.astype(jnp.bfloat16)
    cot_rows = lax.all_gather(cot_low, "seq", axis=0, tiled=True)
    grad_hidden = contract_cols(cot_rows, down_full)
    grad_down_part = contract_rows(hidden, cot_rows)
    sigmoid_gate = jax.nn.sigmoid(gate_vals)
    grad_gate_vals = grad_hidden * up_vals * sigmoid_gate * (1.0 + gate_vals * (1.0 - sigmoid_gate))
    grad_up_vals = grad_hidden * gate_vals * sigmoid_gate
    grad_joint = jnp.concatenate([grad_gate_vals, grad_up_vals], axis=1).astype(jnp.bfloat16)
    gnf_part = contract_cols(grad_joint, joint).astype(jnp.bfloat16)
    grad_normed_ffn = lax.psum_scatter(gnf_part, "seq", scatter_dimension=0, tiled=True).astype(jnp.float32)
    grad_joint_w = contract_rows(ffn_rows, grad_joint)
    grad_pack = jnp.concatenate([grad_joint_w, jnp.transpose(grad_down_part)], axis=1)
    band = grad_pack.shape[0] // row_count
    grad_blocks = grad_pack.reshape(row_count, band, grad_pack.shape[1]).astype(jnp.bfloat16)
    ffn_grad = lax.dynamic_index_in_dim(grad_blocks, row_index, 0, keepdims=False).astype(jnp.float32)
    for k in range(1, row_count):
        route = [(i, (i + k) % row_count) for i in range(row_count)]
        sent = lax.dynamic_index_in_dim(grad_blocks, (row_index + k) % row_count, 0, keepdims=False)
        ffn_grad = ffn_grad + lax.ppermute(sent, "row", route).astype(jnp.float32)
    grad_w_gate = ffn_grad[:, :hid_width]
    grad_w_up = ffn_grad[:, hid_width : 2 * hid_width]
    grad_w_down = jnp.transpose(ffn_grad[:, 2 * hid_width :])
    gain_ffn_part = jnp.sum(grad_normed_ffn * middle * scale_two, axis=0)
    scaled_two = grad_normed_ffn * gain_ffn
    grad_middle = (
        cot_flat
        + scale_two * scaled_two
        - middle * scale_two**3 * jnp.mean(scaled_two * middle, axis=-1, keepdims=True)
    )
    grad_attn = grad_middle.astype(jnp.bfloat16)
    grad_attn_all = lax.all_gather(grad_attn, "seq", axis=0, tiled=True)
    ffn_part, grad_attn_all = lax.optimization_barrier((ffn_part, grad_attn_all))
    ffn_out = lax.psum_scatter(ffn_part, "seq", scatter_dimension=0, tiled=True).astype(jnp.float32)
    outputs = middle + ffn_out
    grad_attn_tail = jnp.pad(grad_attn_all, ((0, TQ * extra), (0, 0)))
    grad_heads_x = contract_cols(
        lax.dynamic_slice_in_dim(grad_attn_tail, q0, nb_all * TQ, 0), wo_g
    ).astype(jnp.bfloat16)
    gh_blocks = jnp.transpose(grad_heads_x.reshape(nb_all, TQ, 2, HD), (0, 2, 1, 3))
    grad_out_part = contract_rows(heads_own, lax.dynamic_slice_in_dim(grad_attn_all, q0, span, 0))
    gq_blk, gk_heads, gv_heads, tap_acc, mix_acc = attention_backward(
        toff, taps_flat, mix_flat, q_blocks, q_own, k_heads, v_heads, row_docs, key_docs,
        probs_blk, gh_blocks, nw, length, nb,
    )
    grad_q_own = jnp.transpose(gq_blk[:nb], (0, 2, 1, 3)).reshape(span, pw)
    grad_k_part = jnp.transpose(gk_heads, (2, 0, 1)).reshape(length, pw)
    grad_v_part = jnp.transpose(gv_heads, (2, 0, 1)).reshape(length, pw)
    grad_taps_part = jnp.sum(tap_acc, axis=(1, 2)).reshape(2, QCONV, KCONV)
    grad_mix_part = jnp.sum(mix_acc, axis=1).reshape(2, 2)

    def split_sum(values):
        if splits == 1:
            return values
        total = values
        for step in range(1, splits):
            route = []
            for s in range(seq_count):
                base = (s // splits) * splits
                route.append((s, base + (s - base + step) % splits))
            total = total + lax.ppermute(values, "seq", route)
        return total

    grad_k_low = split_sum(grad_k_part).astype(jnp.bfloat16)
    grad_v_low = split_sum(grad_v_part).astype(jnp.bfloat16)
    grad_k_own = lax.dynamic_slice_in_dim(grad_k_low, q0, span, 0)
    grad_v_own = lax.dynamic_slice_in_dim(grad_v_low, q0, span, 0)

    normed_own = lax.dynamic_slice_in_dim(normed_all, q0, span, 0)
    rows_per_dev = width // (row_count * seq_count)

    partials = jnp.stack(
        [
            contract_rows(normed_own, grad_q_own),
            contract_rows(normed_own, grad_k_own),
            contract_rows(normed_own, grad_v_own),
        ]
    )
    red = lax.psum_scatter(partials.astype(jnp.bfloat16), "row", scatter_dimension=1, tiled=True)
    got = lax.all_to_all(red, "seq", 1, 1, tiled=True).astype(jnp.float32)
    got = got.reshape(3, groups, splits, rows_per_dev, pw).sum(axis=2)
    got = jnp.transpose(got, (0, 2, 1, 3)).reshape(3, rows_per_dev, width)
    grad_w_query, grad_w_key, grad_w_value = got[0], got[1], got[2]

    red_out = lax.psum_scatter(grad_out_part, "row", scatter_dimension=0, tiled=True)
    red_out = red_out.reshape(splits, rows_per_dev, width)
    grad_w_out = jnp.zeros((rows_per_dev, width), jnp.float32)
    for src_part in range(splits):
        for j in range(splits):
            route = []
            for r in range(row_count):
                for g in range(groups):
                    src = r * seq_count + g * splits + src_part
                    dst = g * row_count * splits + r * splits + j
                    route.append((src, dst))
            grad_w_out = grad_w_out + lax.ppermute(red_out[j], ("row", "seq"), route)

    grad_tok = to_tokens(jnp.concatenate([grad_q_own, grad_k_own, grad_v_own], axis=1))
    grad_tok = grad_tok.reshape(groups, blk, 3, pw)
    gq_tok = jnp.transpose(grad_tok[:, :, 0], (1, 0, 2)).reshape(blk, width)
    gk_tok = jnp.transpose(grad_tok[:, :, 1], (1, 0, 2)).reshape(blk, width)
    gv_tok = jnp.transpose(grad_tok[:, :, 2], (1, 0, 2)).reshape(blk, width)
    grad_normed = (
        contract_cols(gq_tok, w_query) + contract_cols(gk_tok, w_key) + contract_cols(gv_tok, w_value)
    )
    gain_attn_part = jnp.sum(grad_normed * flat_in * scale_one, axis=0)
    scaled_one = grad_normed * gain_attn
    grad_inputs = (
        grad_middle
        + scale_one * scaled_one
        - flat_in * scale_one**3 * jnp.mean(scaled_one * flat_in, axis=-1, keepdims=True)
    )
    taps_full = lax.dynamic_update_slice_in_dim(
        jnp.zeros((HEADS, QCONV, KCONV), jnp.float32), grad_taps_part, pair * 2, 0
    )
    mix_full = lax.dynamic_update_slice_in_dim(
        jnp.zeros((groups, 2, 2), jnp.float32), grad_mix_part[None], pair, 0
    )
    small = jnp.concatenate(
        [gain_attn_part, gain_ffn_part, taps_full.reshape(-1), mix_full.reshape(-1)]
    )
    devices = row_count * seq_count
    assert devices & (devices - 1) == 0
    mask = 1
    while mask < devices:
        route = [(i, i ^ mask) for i in range(devices)]
        small = small + lax.ppermute(small, ("row", "seq"), route)
        mask *= 2
    gain_rows = width // (row_count * seq_count)
    gain_at = (row_index * seq_count + seq_index) * gain_rows
    grad_gain_attn = lax.dynamic_slice_in_dim(small, gain_at, gain_rows, 0)
    grad_gain_ffn = lax.dynamic_slice_in_dim(small, width + gain_at, gain_rows, 0)
    grad_taps = small[2 * width : 2 * width + HEADS * TAPS].reshape(HEADS, QCONV, KCONV)
    grad_mix = small[2 * width + HEADS * TAPS :].reshape(groups, 2, 2)
    return (
        outputs.reshape(row_dev, blk, width),
        grad_inputs.reshape(row_dev, blk, width),
        grad_w_query,
        grad_w_key,
        grad_w_value,
        grad_w_out,
        grad_gain_attn,
        grad_gain_ffn,
        grad_taps,
        grad_mix,
        grad_w_gate,
        grad_w_up,
        grad_w_down,
    )


def solution(mesh):
    return jax.shard_map(
        shards_body,
        mesh=mesh,
        in_specs=(
            P("row", "seq", None),
            P("row", None),
            P(),
            P(),
            P(),
            P(),
            P(),
            P(),
            P(),
            P(),
            P("row", "seq"),
            P("row", "seq"),
            P("seq", "row"),
            P("row", "seq", None),
        ),
        out_specs=(
            P("row", "seq", None),
            P("row", "seq", None),
            P(("row", "seq"), None),
            P(("row", "seq"), None),
            P(("row", "seq"), None),
            P(("row", "seq"), None),
            P(("row", "seq")),
            P(("row", "seq")),
            P(),
            P(),
            P("row", "seq"),
            P("row", "seq"),
            P("seq", "row"),
        ),
        check_vma=False,
    )
```

```python
import jax
import jax.numpy as jnp
from jax import lax
from jax.sharding import PartitionSpec as P
from jax.experimental import pallas as pl
from jax.experimental.pallas import tpu as pltpu

HEADS = 16
HD = 96
QCONV = 6
KCONV = 11
PAD = 8
TQ = 128
EXT = TQ + PAD
SCALE = HD ** (-0.5)
TAPS = QCONV * KCONV

epsilon = 1e-06


def rms_scale(values):
    return lax.rsqrt(jnp.mean(values * values, axis=-1, keepdims=True) + epsilon)


def project(values, weight):
    return jnp.dot(values, weight, preferred_element_type=jnp.float32)


def contract_rows(left, right):
    return lax.dot_general(
        left, right, (((0,), (0,)), ((), ())), preferred_element_type=jnp.float32
    )


def contract_cols(left, right):
    return lax.dot_general(
        left, right, (((1,), (1,)), ((), ())), preferred_element_type=jnp.float32
    )


def normed_pad_tail(values, extra):
    return jnp.pad(values, ((PAD, TQ * extra), (0, 0)))


def window_start(block, nw, length):
    return pl.multiple_of(jnp.clip((block - nw + 1) * TQ, 0, length - nw * TQ), TQ)


def tap_accumulate(sh_ref, acc_ref, taps_ref, head, live):

    def body(col, carry):
        c0 = pl.multiple_of(col * 128, 128)
        for r0 in range(0, EXT, 8):
            tiles = [sh_ref[b, pl.ds(r0, 8), pl.ds(c0, 128)] for b in range(KCONV)]
            for a in range(QCONV):
                base = head * TAPS + a * KCONV
                total = taps_ref[base] * tiles[0]
                for b in range(1, KCONV):
                    total = total + taps_ref[base + b] * tiles[b]
                acc_ref[a, pl.ds(r0, 8), pl.ds(c0, 128)] = total
        return carry

    lax.fori_loop(0, live, body, 0)


def tap_products(sh_ref, g_ref, live):
    sums = {}
    for a0 in range(0, QCONV, 2):

        def body(col, accs):
            c0 = pl.multiple_of(col * 128, 128)
            out = list(accs)
            for r0 in range(0, EXT, 8):
                ga = [g_ref[a0 + k, pl.ds(r0, 8), pl.ds(c0, 128)] for k in range(2)]
                for b in range(KCONV):
                    tile = sh_ref[b, pl.ds(r0, 8), pl.ds(c0, 128)]
                    for k in range(2):
                        out[k * KCONV + b] = out[k * KCONV + b] + ga[k] * tile
            return tuple(out)

        start = tuple(jnp.zeros((8, 128), jnp.float32) for _ in range(2 * KCONV))
        res = lax.fori_loop(0, live, body, start)
        for k in range(2):
            for b in range(KCONV):
                sums[(a0 + k, b)] = res[k * KCONV + b]
    return sums


def live_tiles(block, kstart, nw):
    return jnp.clip(block + 1 - kstart // TQ, 1, nw)


def masks(block, kstart, width, rdoc_ref, kdoc_ref):
    keydoc = kdoc_ref[:, pl.ds(kstart, width)]
    ext_pos = block * TQ - PAD + lax.broadcasted_iota(jnp.int32, (EXT, width), 0)
    key_ext = kstart + lax.broadcasted_iota(jnp.int32, (EXT, width), 1)
    allowed_ext = (key_ext <= ext_pos) & (rdoc_ref[0] == keydoc)
    own_pos = block * TQ + lax.broadcasted_iota(jnp.int32, (TQ, width), 0)
    key_own = kstart + lax.broadcasted_iota(jnp.int32, (TQ, width), 1)
    allowed_own = (key_own <= own_pos) & (rdoc_ref[0, PAD:, :] == keydoc)
    return allowed_ext, allowed_own


def masked_shifts(q_ref, k_ref, head, kstart, width, allowed_ext, sh_ref):
    keys = k_ref[head, pl.ds(kstart, width), :]
    scores = lax.dot_general(
        q_ref[0, head], keys, (((1,), (1,)), ((), ())), preferred_element_type=jnp.float32
    ) * SCALE
    masked = jnp.where(allowed_ext, scores, 0.0)
    col = lax.broadcasted_iota(jnp.int32, (EXT, width), 1)
    sh_ref[0] = masked
    for b in range(1, KCONV):
        sh_ref[b] = jnp.where(col >= b, pltpu.roll(masked, b, 1), 0.0)


def fwd_kernel(toff_ref, taps_ref, mix_ref, q_ref, k_ref, v_ref, rdoc_ref, kdoc_ref,
               heads_ref, probs_ref, sh_ref, acc_ref, *, nw, length):
    width = nw * TQ
    block = toff_ref[0] + pl.program_id(0)
    kstart = window_start(block, nw, length)
    allowed_ext, allowed_own = masks(block, kstart, width, rdoc_ref, kdoc_ref)
    for head in range(2):
        masked_shifts(q_ref, k_ref, head, kstart, width, allowed_ext, sh_ref)
        tap_accumulate(sh_ref, acc_ref, taps_ref, head, live_tiles(block, kstart, nw))
        conv = acc_ref[0]
        for a in range(1, QCONV):
            conv = conv + pltpu.roll(acc_ref[a], a, 0)
        logits = jnp.where(allowed_own, conv[PAD:], -jnp.inf)
        highest = jnp.max(logits, axis=1, keepdims=True)
        highest = jnp.where(highest > -jnp.inf, highest, 0.0)
        expd = jnp.exp(logits - highest)
        denom = jnp.sum(expd, axis=1, keepdims=True)
        probs_ref[0, head] = expd / jnp.where(denom > 0.0, denom, 1.0)
    p0 = probs_ref[0, 0]
    p1 = probs_ref[0, 1]
    for c in range(2):
        mixed = (mix_ref[2 * c] * p0 + mix_ref[2 * c + 1] * p1).astype(jnp.bfloat16)
        heads_ref[0, c] = jnp.dot(
            mixed, v_ref[c, pl.ds(kstart, width), :], preferred_element_type=jnp.float32
        ).astype(jnp.bfloat16)


def attention_forward(toff, taps_flat, mix_flat, q_blocks, k_heads, v_heads, row_docs, key_docs, nw, length):
    nb_all = q_blocks.shape[0]
    width = nw * TQ
    smem = pl.BlockSpec(memory_space=pltpu.SMEM)
    flops = nb_all * 2 * (4 * EXT * width * HD + 2 * TAPS * EXT * width)
    return pl.pallas_call(
        lambda *refs: fwd_kernel(*refs, nw=nw, length=length),
        grid=(nb_all,),
        in_specs=[
            smem,
            smem,
            smem,
            pl.BlockSpec((1, 2, EXT, HD), lambda t: (t, 0, 0, 0)),
            pl.BlockSpec((2, length, HD), lambda t: (0, 0, 0)),
            pl.BlockSpec((2, length, HD), lambda t: (0, 0, 0)),
            pl.BlockSpec((1, EXT, 1), lambda t: (t, 0, 0)),
            pl.BlockSpec((1, length), lambda t: (0, 0)),
        ],
        out_specs=[
            pl.BlockSpec((1, 2, TQ, HD), lambda t: (t, 0, 0, 0)),
            pl.BlockSpec((1, 2, TQ, width), lambda t: (t, 0, 0, 0)),
        ],
        out_shape=[
            jax.ShapeDtypeStruct((nb_all, 2, TQ, HD), jnp.bfloat16),
            jax.ShapeDtypeStruct((nb_all, 2, TQ, width), jnp.float32),
        ],
        scratch_shapes=[
            pltpu.VMEM((KCONV, EXT, width), jnp.float32),
            pltpu.VMEM((QCONV, EXT, width), jnp.float32),
        ],
        compiler_params=pltpu.CompilerParams(
            dimension_semantics=("arbitrary",), vmem_limit_bytes=56 * 1024 * 1024
        ),
        cost_estimate=pl.CostEstimate(
            flops=flops, transcendentals=nb_all * 2 * TQ * width,
            bytes_accessed=nb_all * 2 * TQ * width * 4 + 4 * length * HD * 2,
        ),
    )(toff, taps_flat, mix_flat, q_blocks, k_heads, v_heads, row_docs, key_docs)


def bwd_kernel(toff_ref, taps_ref, mix_ref, q_ref, qo_ref, k_ref, v_ref, rdoc_ref, kdoc_ref,
               probs_ref, gh_ref, ght_ref, gq_ref, gk_ref, gv_ref, tacc_ref, macc_ref,
               carry_ref, sh_ref, acc_ref, g_ref, gx_ref, *, nw, length, nb, nb_all):
    width = nw * TQ
    step = pl.program_id(0)
    local = nb_all - 1 - step
    block = toff_ref[0] + local
    kstart = window_start(block, nw, length)

    @pl.when(step == 0)
    def _init():
        gk_ref[...] = jnp.zeros(gk_ref.shape, jnp.float32)
        gv_ref[...] = jnp.zeros(gv_ref.shape, jnp.float32)
        tacc_ref[...] = jnp.zeros(tacc_ref.shape, jnp.float32)
        macc_ref[...] = jnp.zeros(macc_ref.shape, jnp.float32)
        carry_ref[...] = jnp.zeros(carry_ref.shape, jnp.float32)

    allowed_ext, allowed_own = masks(block, kstart, width, rdoc_ref, kdoc_ref)
    gm = [
        lax.dot_general(
            gh_ref[0, c], v_ref[c, pl.ds(kstart, width), :], (((1,), (1,)), ((), ())),
            preferred_element_type=jnp.float32,
        )
        for c in range(2)
    ]
    probs = [probs_ref[0, 0], probs_ref[0, 1]]
    gc = []
    for e in range(2):
        gp = mix_ref[e] * gm[0] + mix_ref[2 + e] * gm[1]
        inner = jnp.sum(gp * probs[e], axis=1, keepdims=True)
        gc.append(probs[e] * (gp - inner))

    def own_sums():
        for c in range(2):
            for e in range(2):
                macc_ref[pl.ds(2 * c + e, 1), :] += jnp.sum(gm[c] * probs[e], axis=0, keepdims=True)
            mixed = (mix_ref[2 * c] * probs[0] + mix_ref[2 * c + 1] * probs[1]).astype(jnp.bfloat16)
            gv_ref[c, :, pl.ds(kstart, width)] += jnp.dot(
                ght_ref[0, c], mixed, preferred_element_type=jnp.float32
            )

    def head_taps(e):
        masked_shifts(q_ref, k_ref, e, kstart, width, allowed_ext, sh_ref)
        gcp = jnp.concatenate([jnp.zeros((PAD, width), jnp.float32), gc[e]], axis=0)
        g_ref[0] = gcp
        for a in range(1, QCONV):
            g_ref[a] = pltpu.roll(gcp, EXT - a, 0)
        sums = tap_products(sh_ref, g_ref, live_tiles(block, kstart, nw))
        for b in range(KCONV):
            for a in range(QCONV):
                tacc_ref[e * TAPS + a * KCONV + b] += sums[(a, b)]

    def head_keys(e, gs):
        gk_ref[e, :, pl.ds(kstart, width)] += jnp.dot(
            qo_ref[0, e], gs, preferred_element_type=jnp.float32
        ) * SCALE

    nxt = [carry_ref[e, :, pl.ds(kstart, width + TQ)] for e in range(2)]
    if nb < nb_all:
        pl.when(local < nb)(own_sums)
    else:
        own_sums()
    for e in range(2):
        if nb < nb_all:
            pl.when(local < nb)(lambda: head_taps(e))
        else:
            head_taps(e)
        gx_ref[pl.ds(0, TQ), pl.ds(0, width)] = gc[e]
        gx_ref[pl.ds(0, TQ), pl.ds(width, TQ)] = jnp.zeros((TQ, TQ), jnp.float32)
        gx_ref[pl.ds(TQ, PAD), :] = nxt[e]
        gxv = gx_ref[...]
        sh_ref[0] = gxv[:, :width]
        for b in range(1, KCONV):
            sh_ref[b] = pltpu.roll(gxv, width + TQ - b, 1)[:, :width]
        tap_accumulate(sh_ref, acc_ref, taps_ref, e, live_tiles(block, kstart, nw))
        gmk = acc_ref[0]
        for a in range(1, QCONV):
            gmk = gmk + pltpu.roll(acc_ref[a], EXT - a, 0)
        gs = jnp.where(allowed_own, gmk[:TQ], 0.0).astype(jnp.bfloat16)
        gq_ref[0, e] = (
            jnp.dot(gs, k_ref[e, pl.ds(kstart, width), :], preferred_element_type=jnp.float32) * SCALE
        ).astype(jnp.bfloat16)
        if nb < nb_all:
            pl.when(local < nb)(lambda: head_keys(e, gs))
        else:
            head_keys(e, gs)
    carry_ref[...] = jnp.zeros(carry_ref.shape, jnp.float32)
    for e in range(2):
        carry_ref[e, :, pl.ds(kstart, width)] = gc[e][:PAD]


def attention_backward(toff, taps_flat, mix_flat, q_blocks, q_own, k_heads, v_heads, row_docs, key_docs,
                       probs_blk, gh_blocks, nw, length, nb):
    q_own = jnp.swapaxes(q_own, 2, 3)
    gh_t = jnp.swapaxes(gh_blocks, 2, 3)
    nb_all = q_blocks.shape[0]
    width = nw * TQ
    smem = pl.BlockSpec(memory_space=pltpu.SMEM)
    rev = lambda s: nb_all - 1 - s
    flops = nb_all * 2 * (8 * TQ * width * HD + 6 * TAPS * EXT * width)
    return pl.pallas_call(
        lambda *refs: bwd_kernel(*refs, nw=nw, length=length, nb=nb, nb_all=nb_all),
        grid=(nb_all,),
        in_specs=[
            smem,
            smem,
            smem,
            pl.BlockSpec((1, 2, EXT, HD), lambda s: (rev(s), 0, 0, 0)),
            pl.BlockSpec((1, 2, HD, TQ), lambda s: (rev(s), 0, 0, 0)),
            pl.BlockSpec((2, length, HD), lambda s: (0, 0, 0)),
            pl.BlockSpec((2, length, HD), lambda s: (0, 0, 0)),
            pl.BlockSpec((1, EXT, 1), lambda s: (rev(s), 0, 0)),
            pl.BlockSpec((1, length), lambda s: (0, 0)),
            pl.BlockSpec((1, 2, TQ, width), lambda s: (rev(s), 0, 0, 0)),
            pl.BlockSpec((1, 2, TQ, HD), lambda s: (rev(s), 0, 0, 0)),
            pl.BlockSpec((1, 2, HD, TQ), lambda s: (rev(s), 0, 0, 0)),
        ],
        out_specs=[
            pl.BlockSpec((1, 2, TQ, HD), lambda s: (rev(s), 0, 0, 0)),
            pl.BlockSpec((2, HD, length), lambda s: (0, 0, 0)),
            pl.BlockSpec((2, HD, length), lambda s: (0, 0, 0)),
            pl.BlockSpec((2 * TAPS, 8, 128), lambda s: (0, 0, 0)),
            pl.BlockSpec((4, width), lambda s: (0, 0)),
        ],
        out_shape=[
            jax.ShapeDtypeStruct((nb_all, 2, TQ, HD), jnp.bfloat16),
            jax.ShapeDtypeStruct((2, HD, length), jnp.float32),
            jax.ShapeDtypeStruct((2, HD, length), jnp.float32),
            jax.ShapeDtypeStruct((2 * TAPS, 8, 128), jnp.float32),
            jax.ShapeDtypeStruct((4, width), jnp.float32),
        ],
        scratch_shapes=[
            pltpu.VMEM((2, PAD, length + TQ), jnp.float32),
            pltpu.VMEM((KCONV, EXT, width), jnp.float32),
            pltpu.VMEM((QCONV, EXT, width), jnp.float32),
            pltpu.VMEM((QCONV, EXT, width), jnp.float32),
            pltpu.VMEM((EXT, width + TQ), jnp.float32),
        ],
        compiler_params=pltpu.CompilerParams(
            dimension_semantics=("arbitrary",), vmem_limit_bytes=60 * 1024 * 1024
        ),
        cost_estimate=pl.CostEstimate(
            flops=flops, transcendentals=0,
            bytes_accessed=nb_all * 2 * TQ * width * 4 + 8 * length * HD * 4,
        ),
    )(toff, taps_flat, mix_flat, q_blocks, q_own, k_heads, v_heads, row_docs, key_docs, probs_blk, gh_blocks, gh_t)


def shards_body(
    inputs,
    doc_ids,
    w_query,
    w_key,
    w_value,
    w_out,
    gain_attn,
    gain_ffn,
    conv_taps,
    head_mix,
    w_gate,
    w_up,
    w_down,
    cotangent,
):
    row_dev, blk, width = inputs.shape
    assert row_dev == 1
    seq_count = lax.axis_size("seq")
    row_count = lax.axis_size("row")
    seq_index = lax.axis_index("seq")
    row_index = lax.axis_index("row")
    length = blk * seq_count
    groups = HEADS // 2
    assert seq_count % groups == 0
    splits = seq_count // groups
    span = length // splits
    pw = 2 * HD
    pair = seq_index // splits
    part = seq_index % splits
    q0 = part * span

    flat_in = inputs.reshape(blk, width)
    scale_one = rms_scale(flat_in)
    normed = (flat_in * scale_one * gain_attn).astype(jnp.bfloat16)
    normed_all = lax.all_gather(normed, "seq", axis=0, tiled=True)

    wq_g = lax.dynamic_slice_in_dim(w_query, pair * pw, pw, 1)
    wk_g = lax.dynamic_slice_in_dim(w_key, pair * pw, pw, 1)
    wv_g = lax.dynamic_slice_in_dim(w_value, pair * pw, pw, 1)
    wo_g = lax.dynamic_slice_in_dim(w_out, pair * pw, pw, 0)
    taps = lax.dynamic_slice_in_dim(conv_taps, pair * 2, 2, 0)
    mixing = lax.dynamic_index_in_dim(head_mix, pair, 0, keepdims=False)

    k_all = project(normed_all, wk_g).astype(jnp.bfloat16)
    v_all = project(normed_all, wv_g).astype(jnp.bfloat16)
    k3 = k_all.reshape(length, 2, HD)
    v3 = v_all.reshape(length, 2, HD)

    docs = doc_ids[0]
    nb = span // TQ
    extra = 1 if splits > 1 else 0
    nb_all = nb + extra
    doc_cap = length // 2
    nw = min(length // TQ, (doc_cap + QCONV - 2 + TQ - 1) // TQ + 1)
    q_tail = normed_pad_tail(normed_all, extra)
    q_rows = project(lax.dynamic_slice_in_dim(q_tail, q0, nb_all * TQ + PAD, 0), wq_g).astype(jnp.bfloat16)
    q_blocks = jnp.stack([q_rows[t * TQ : t * TQ + EXT] for t in range(nb_all)])
    q_blocks = jnp.transpose(q_blocks.reshape(nb_all, EXT, 2, HD), (0, 2, 1, 3))
    q_own = q_blocks[:, :, PAD:]
    k_heads = jnp.transpose(k3, (1, 0, 2))
    v_heads = jnp.transpose(v3, (1, 0, 2))
    docs_tail = jnp.pad(docs, (PAD, TQ * extra), constant_values=-1)
    doc_rows = lax.dynamic_slice_in_dim(docs_tail, q0, nb_all * TQ + PAD, 0)
    row_docs = jnp.stack([doc_rows[t * TQ : t * TQ + EXT] for t in range(nb_all)])[:, :, None]
    key_docs = docs[None, :]
    toff = (q0 // TQ).astype(jnp.int32).reshape(1)
    taps_flat = taps.reshape(2 * QCONV * KCONV)
    mix_flat = mixing.reshape(4)
    heads_blk, probs_blk = attention_forward(
        toff, taps_flat, mix_flat, q_blocks, k_heads, v_heads, row_docs, key_docs, nw, length
    )
    heads_own = jnp.transpose(heads_blk[:nb], (0, 2, 1, 3)).reshape(span, pw)

    def to_tokens(values):
        cols = values.shape[1]
        if splits == 1:
            full = values
        else:
            full = lax.dynamic_update_slice_in_dim(
                jnp.zeros((length, cols), values.dtype), values, q0, 0
            )
        got = lax.all_to_all(full, "seq", 0, 0, tiled=True)
        got = got.reshape(groups, splits, blk, cols)
        if splits > 1:
            got = jnp.sum(got.astype(jnp.float32), axis=1).astype(values.dtype)
        else:
            got = got[:, 0]
        return got

    heads_tok = jnp.transpose(to_tokens(heads_own), (1, 0, 2)).reshape(blk, width)
    middle = flat_in + project(heads_tok, w_out)
    scale_two = rms_scale(middle)
    normed_ffn = (middle * scale_two * gain_ffn).astype(jnp.bfloat16)
    hid_width = w_gate.shape[1]
    packed = jnp.concatenate([w_gate, w_up, jnp.transpose(w_down)], axis=1)
    pieces = [packed]
    for k in range(1, row_count):
        route = [(i, (i + k) % row_count) for i in range(row_count)]
        pieces.append(lax.ppermute(packed, "row", route))
    rev = jnp.stack(pieces[::-1] + pieces[::-1])
    full_w = lax.dynamic_slice_in_dim(rev, row_count - 1 - row_index, row_count, 0)
    full_w = full_w.reshape(row_count * packed.shape[0], packed.shape[1])
    joint = full_w[:, : 2 * hid_width]
    down_full = jnp.transpose(full_w[:, 2 * hid_width :])
    ffn_rows = lax.all_gather(normed_ffn, "seq", axis=0, tiled=True)
    gate_up = project(ffn_rows, joint)
    gate_vals = gate_up[:, :hid_width]
    up_vals = gate_up[:, hid_width:]
    hidden = (jax.nn.silu(gate_vals) * up_vals).astype(jnp.bfloat16)
    ffn_part = project(hidden, down_full).astype(jnp.bfloat16)
    cot_flat = cotangent.reshape(blk, width)
    cot_low = cot_flat.astype(jnp.bfloat16)
    cot_rows = lax.all_gather(cot_low, "seq", axis=0, tiled=True)
    grad_hidden = contract_cols(cot_rows, down_full)
    grad_down_part = contract_rows(hidden, cot_rows)
    sigmoid_gate = jax.nn.sigmoid(gate_vals)
    grad_gate_vals = grad_hidden * up_vals * sigmoid_gate * (1.0 + gate_vals * (1.0 - sigmoid_gate))
    grad_up_vals = grad_hidden * gate_vals * sigmoid_gate
    grad_joint = jnp.concatenate([grad_gate_vals, grad_up_vals], axis=1).astype(jnp.bfloat16)
    gnf_part = contract_cols(grad_joint, joint).astype(jnp.bfloat16)
    grad_normed_ffn = lax.psum_scatter(gnf_part, "seq", scatter_dimension=0, tiled=True).astype(jnp.float32)
    grad_joint_w = contract_rows(ffn_rows, grad_joint)
    grad_pack = jnp.concatenate([grad_joint_w, jnp.transpose(grad_down_part)], axis=1)
    band = grad_pack.shape[0] // row_count
    grad_blocks = grad_pack.reshape(row_count, band, grad_pack.shape[1]).astype(jnp.bfloat16)
    ffn_grad = lax.dynamic_index_in_dim(grad_blocks, row_index, 0, keepdims=False).astype(jnp.float32)
    for k in range(1, row_count):
        route = [(i, (i + k) % row_count) for i in range(row_count)]
        sent = lax.dynamic_index_in_dim(grad_blocks, (row_index + k) % row_count, 0, keepdims=False)
        ffn_grad = ffn_grad + lax.ppermute(sent, "row", route).astype(jnp.float32)
    grad_w_gate = ffn_grad[:, :hid_width]
    grad_w_up = ffn_grad[:, hid_width : 2 * hid_width]
    grad_w_down = jnp.transpose(ffn_grad[:, 2 * hid_width :])
    gain_ffn_part = jnp.sum(grad_normed_ffn * middle * scale_two, axis=0)
    scaled_two = grad_normed_ffn * gain_ffn
    grad_middle = (
        cot_flat
        + scale_two * scaled_two
        - middle * scale_two**3 * jnp.mean(scaled_two * middle, axis=-1, keepdims=True)
    )
    grad_attn = grad_middle.astype(jnp.bfloat16)
    grad_attn_all = lax.all_gather(grad_attn, "seq", axis=0, tiled=True)
    ffn_part, grad_attn_all = lax.optimization_barrier((ffn_part, grad_attn_all))
    ffn_out = lax.psum_scatter(ffn_part, "seq", scatter_dimension=0, tiled=True).astype(jnp.float32)
    outputs = middle + ffn_out
    grad_attn_tail = jnp.pad(grad_attn_all, ((0, TQ * extra), (0, 0)))
    grad_heads_x = contract_cols(
        lax.dynamic_slice_in_dim(grad_attn_tail, q0, nb_all * TQ, 0), wo_g
    ).astype(jnp.bfloat16)
    gh_blocks = jnp.transpose(grad_heads_x.reshape(nb_all, TQ, 2, HD), (0, 2, 1, 3))
    grad_out_part = contract_rows(heads_own, lax.dynamic_slice_in_dim(grad_attn_all, q0, span, 0))
    gq_blk, gk_heads, gv_heads, tap_acc, mix_acc = attention_backward(
        toff, taps_flat, mix_flat, q_blocks, q_own, k_heads, v_heads, row_docs, key_docs,
        probs_blk, gh_blocks, nw, length, nb,
    )
    grad_q_own = jnp.transpose(gq_blk[:nb], (0, 2, 1, 3)).reshape(span, pw)
    grad_k_part = jnp.transpose(gk_heads, (2, 0, 1)).reshape(length, pw)
    grad_v_part = jnp.transpose(gv_heads, (2, 0, 1)).reshape(length, pw)
    grad_taps_part = jnp.sum(tap_acc, axis=(1, 2)).reshape(2, QCONV, KCONV)
    grad_mix_part = jnp.sum(mix_acc, axis=1).reshape(2, 2)

    def split_sum(values):
        if splits == 1:
            return values
        total = values
        for step in range(1, splits):
            route = []
            for s in range(seq_count):
                base = (s // splits) * splits
                route.append((s, base + (s - base + step) % splits))
            total = total + lax.ppermute(values, "seq", route)
        return total

    grad_k_low = split_sum(grad_k_part).astype(jnp.bfloat16)
    grad_v_low = split_sum(grad_v_part).astype(jnp.bfloat16)
    grad_k_own = lax.dynamic_slice_in_dim(grad_k_low, q0, span, 0)
    grad_v_own = lax.dynamic_slice_in_dim(grad_v_low, q0, span, 0)

    normed_own = lax.dynamic_slice_in_dim(normed_all, q0, span, 0)
    rows_per_dev = width // (row_count * seq_count)

    partials = jnp.stack(
        [
            contract_rows(normed_own, grad_q_own),
            contract_rows(normed_own, grad_k_own),
            contract_rows(normed_own, grad_v_own),
        ]
    )
    devices = row_count * seq_count
    send = partials.astype(jnp.bfloat16).reshape(3, devices, rows_per_dev, pw)
    send = jnp.transpose(send, (1, 0, 2, 3)).reshape(devices * 3 * rows_per_dev, pw)
    got = lax.all_to_all(send, ("row", "seq"), 0, 0, tiled=True).astype(jnp.float32)
    got = got.reshape(row_count, groups, splits, 3, rows_per_dev, pw).sum(axis=(0, 2))
    got = jnp.transpose(got, (1, 2, 0, 3)).reshape(3, rows_per_dev, width)
    grad_w_query, grad_w_key, grad_w_value = got[0], got[1], got[2]

    red_out = lax.psum_scatter(grad_out_part, "row", scatter_dimension=0, tiled=True)
    red_out = red_out.reshape(splits, rows_per_dev, width)
    grad_w_out = jnp.zeros((rows_per_dev, width), jnp.float32)
    for src_part in range(splits):
        for j in range(splits):
            route = []
            for r in range(row_count):
                for g in range(groups):
                    src = r * seq_count + g * splits + src_part
                    dst = g * row_count * splits + r * splits + j
                    route.append((src, dst))
            grad_w_out = grad_w_out + lax.ppermute(red_out[j], ("row", "seq"), route)

    grad_tok = to_tokens(jnp.concatenate([grad_q_own, grad_k_own, grad_v_own], axis=1))
    grad_tok = grad_tok.reshape(groups, blk, 3, pw)
    gq_tok = jnp.transpose(grad_tok[:, :, 0], (1, 0, 2)).reshape(blk, width)
    gk_tok = jnp.transpose(grad_tok[:, :, 1], (1, 0, 2)).reshape(blk, width)
    gv_tok = jnp.transpose(grad_tok[:, :, 2], (1, 0, 2)).reshape(blk, width)
    grad_normed = (
        contract_cols(gq_tok, w_query) + contract_cols(gk_tok, w_key) + contract_cols(gv_tok, w_value)
    )
    gain_attn_part = jnp.sum(grad_normed * flat_in * scale_one, axis=0)
    scaled_one = grad_normed * gain_attn
    grad_inputs = (
        grad_middle
        + scale_one * scaled_one
        - flat_in * scale_one**3 * jnp.mean(scaled_one * flat_in, axis=-1, keepdims=True)
    )
    taps_full = lax.dynamic_update_slice_in_dim(
        jnp.zeros((HEADS, QCONV, KCONV), jnp.float32), grad_taps_part, pair * 2, 0
    )
    mix_full = lax.dynamic_update_slice_in_dim(
        jnp.zeros((groups, 2, 2), jnp.float32), grad_mix_part[None], pair, 0
    )
    small = jnp.concatenate(
        [gain_attn_part, gain_ffn_part, taps_full.reshape(-1), mix_full.reshape(-1)]
    )
    assert devices & (devices - 1) == 0
    mask = 1
    while mask < devices:
        route = [(i, i ^ mask) for i in range(devices)]
        small = small + lax.ppermute(small, ("row", "seq"), route)
        mask *= 2
    gain_rows = width // (row_count * seq_count)
    gain_at = (row_index * seq_count + seq_index) * gain_rows
    grad_gain_attn = lax.dynamic_slice_in_dim(small, gain_at, gain_rows, 0)
    grad_gain_ffn = lax.dynamic_slice_in_dim(small, width + gain_at, gain_rows, 0)
    grad_taps = small[2 * width : 2 * width + HEADS * TAPS].reshape(HEADS, QCONV, KCONV)
    grad_mix = small[2 * width + HEADS * TAPS :].reshape(groups, 2, 2)
    return (
        outputs.reshape(row_dev, blk, width),
        grad_inputs.reshape(row_dev, blk, width),
        grad_w_query,
        grad_w_key,
        grad_w_value,
        grad_w_out,
        grad_gain_attn,
        grad_gain_ffn,
        grad_taps,
        grad_mix,
        grad_w_gate,
        grad_w_up,
        grad_w_down,
    )


def solution(mesh):
    return jax.shard_map(
        shards_body,
        mesh=mesh,
        in_specs=(
            P("row", "seq", None),
            P("row", None),
            P(),
            P(),
            P(),
            P(),
            P(),
            P(),
            P(),
            P(),
            P("row", "seq"),
            P("row", "seq"),
            P("seq", "row"),
            P("row", "seq", None),
        ),
        out_specs=(
            P("row", "seq", None),
            P("row", "seq", None),
            P(("row", "seq"), None),
            P(("row", "seq"), None),
            P(("row", "seq"), None),
            P(("row", "seq"), None),
            P(("row", "seq")),
            P(("row", "seq")),
            P(),
            P(),
            P("row", "seq"),
            P("row", "seq"),
            P("seq", "row"),
        ),
        check_vma=False,
    )
```

```python
import jax
import jax.numpy as jnp
from jax import lax
from jax.sharding import PartitionSpec as P
from jax.experimental import pallas as pl
from jax.experimental.pallas import tpu as pltpu

HEADS = 16
HD = 96
QCONV = 6
KCONV = 11
PAD = 8
TQ = 128
EXT = TQ + PAD
SCALE = HD ** (-0.5)
TAPS = QCONV * KCONV

epsilon = 1e-06


def rms_scale(values):
    return lax.rsqrt(jnp.mean(values * values, axis=-1, keepdims=True) + epsilon)


def project(values, weight):
    return jnp.dot(values, weight, preferred_element_type=jnp.float32)


def contract_rows(left, right):
    return lax.dot_general(
        left, right, (((0,), (0,)), ((), ())), preferred_element_type=jnp.float32
    )


def contract_cols(left, right):
    return lax.dot_general(
        left, right, (((1,), (1,)), ((), ())), preferred_element_type=jnp.float32
    )


def normed_pad_tail(values, extra):
    return jnp.pad(values, ((PAD, TQ * extra), (0, 0)))


def window_start(block, nw, length):
    return pl.multiple_of(jnp.clip((block - nw + 1) * TQ, 0, length - nw * TQ), TQ)


def tap_accumulate(sh_ref, acc_ref, taps_ref, head, live):

    def body(col, carry):
        c0 = pl.multiple_of(col * 128, 128)
        for r0 in range(0, EXT, 8):
            tiles = [sh_ref[b, pl.ds(r0, 8), pl.ds(c0, 128)] for b in range(KCONV)]
            for a in range(QCONV):
                base = head * TAPS + a * KCONV
                total = taps_ref[base] * tiles[0]
                for b in range(1, KCONV):
                    total = total + taps_ref[base + b] * tiles[b]
                acc_ref[a, pl.ds(r0, 8), pl.ds(c0, 128)] = total
        return carry

    lax.fori_loop(0, live, body, 0)


def tap_products(sh_ref, g_ref, live):
    sums = {}
    for a0 in range(0, QCONV, 2):

        def body(col, accs):
            c0 = pl.multiple_of(col * 128, 128)
            out = list(accs)
            for r0 in range(0, EXT, 8):
                ga = [g_ref[a0 + k, pl.ds(r0, 8), pl.ds(c0, 128)] for k in range(2)]
                for b in range(KCONV):
                    tile = sh_ref[b, pl.ds(r0, 8), pl.ds(c0, 128)]
                    for k in range(2):
                        out[k * KCONV + b] = out[k * KCONV + b] + ga[k] * tile
            return tuple(out)

        start = tuple(jnp.zeros((8, 128), jnp.float32) for _ in range(2 * KCONV))
        res = lax.fori_loop(0, live, body, start)
        for k in range(2):
            for b in range(KCONV):
                sums[(a0 + k, b)] = res[k * KCONV + b]
    return sums


def live_tiles(block, kstart, nw):
    return jnp.clip(block + 1 - kstart // TQ, 1, nw)


def masks(block, kstart, width, rdoc_ref, kdoc_ref):
    keydoc = kdoc_ref[:, pl.ds(kstart, width)]
    ext_pos = block * TQ - PAD + lax.broadcasted_iota(jnp.int32, (EXT, width), 0)
    key_ext = kstart + lax.broadcasted_iota(jnp.int32, (EXT, width), 1)
    allowed_ext = (key_ext <= ext_pos) & (rdoc_ref[0] == keydoc)
    own_pos = block * TQ + lax.broadcasted_iota(jnp.int32, (TQ, width), 0)
    key_own = kstart + lax.broadcasted_iota(jnp.int32, (TQ, width), 1)
    allowed_own = (key_own <= own_pos) & (rdoc_ref[0, PAD:, :] == keydoc)
    return allowed_ext, allowed_own


def masked_shifts(q_ref, k_ref, head, kstart, width, allowed_ext, sh_ref):
    keys = k_ref[head, pl.ds(kstart, width), :]
    scores = lax.dot_general(
        q_ref[0, head], keys, (((1,), (1,)), ((), ())), preferred_element_type=jnp.float32
    ) * SCALE
    masked = jnp.where(allowed_ext, scores, 0.0)
    col = lax.broadcasted_iota(jnp.int32, (EXT, width), 1)
    sh_ref[0] = masked
    for b in range(1, KCONV):
        sh_ref[b] = jnp.where(col >= b, pltpu.roll(masked, b, 1), 0.0)


def fwd_kernel(toff_ref, taps_ref, mix_ref, q_ref, k_ref, v_ref, rdoc_ref, kdoc_ref,
               heads_ref, probs_ref, sh_ref, acc_ref, *, nw, length):
    width = nw * TQ
    block = toff_ref[0] + pl.program_id(0)
    kstart = window_start(block, nw, length)
    allowed_ext, allowed_own = masks(block, kstart, width, rdoc_ref, kdoc_ref)
    for head in range(2):
        masked_shifts(q_ref, k_ref, head, kstart, width, allowed_ext, sh_ref)
        tap_accumulate(sh_ref, acc_ref, taps_ref, head, live_tiles(block, kstart, nw))
        conv = acc_ref[0]
        for a in range(1, QCONV):
            conv = conv + pltpu.roll(acc_ref[a], a, 0)
        logits = jnp.where(allowed_own, conv[PAD:], -jnp.inf)
        highest = jnp.max(logits, axis=1, keepdims=True)
        highest = jnp.where(highest > -jnp.inf, highest, 0.0)
        expd = jnp.exp(logits - highest)
        denom = jnp.sum(expd, axis=1, keepdims=True)
        probs_ref[0, head] = expd / jnp.where(denom > 0.0, denom, 1.0)
    p0 = probs_ref[0, 0]
    p1 = probs_ref[0, 1]
    for c in range(2):
        mixed = (mix_ref[2 * c] * p0 + mix_ref[2 * c + 1] * p1).astype(jnp.bfloat16)
        heads_ref[0, c] = jnp.dot(
            mixed, v_ref[c, pl.ds(kstart, width), :], preferred_element_type=jnp.float32
        ).astype(jnp.bfloat16)


def attention_forward(toff, taps_flat, mix_flat, q_blocks, k_heads, v_heads, row_docs, key_docs, nw, length):
    nb_all = q_blocks.shape[0]
    width = nw * TQ
    smem = pl.BlockSpec(memory_space=pltpu.SMEM)
    flops = nb_all * 2 * (4 * EXT * width * HD + 2 * TAPS * EXT * width)
    return pl.pallas_call(
        lambda *refs: fwd_kernel(*refs, nw=nw, length=length),
        grid=(nb_all,),
        in_specs=[
            smem,
            smem,
            smem,
            pl.BlockSpec((1, 2, EXT, HD), lambda t: (t, 0, 0, 0)),
            pl.BlockSpec((2, length, HD), lambda t: (0, 0, 0)),
            pl.BlockSpec((2, length, HD), lambda t: (0, 0, 0)),
            pl.BlockSpec((1, EXT, 1), lambda t: (t, 0, 0)),
            pl.BlockSpec((1, length), lambda t: (0, 0)),
        ],
        out_specs=[
            pl.BlockSpec((1, 2, TQ, HD), lambda t: (t, 0, 0, 0)),
            pl.BlockSpec((1, 2, TQ, width), lambda t: (t, 0, 0, 0)),
        ],
        out_shape=[
            jax.ShapeDtypeStruct((nb_all, 2, TQ, HD), jnp.bfloat16),
            jax.ShapeDtypeStruct((nb_all, 2, TQ, width), jnp.float32),
        ],
        scratch_shapes=[
            pltpu.VMEM((KCONV, EXT, width), jnp.float32),
            pltpu.VMEM((QCONV, EXT, width), jnp.float32),
        ],
        compiler_params=pltpu.CompilerParams(
            dimension_semantics=("arbitrary",), vmem_limit_bytes=56 * 1024 * 1024
        ),
        cost_estimate=pl.CostEstimate(
            flops=flops, transcendentals=nb_all * 2 * TQ * width,
            bytes_accessed=nb_all * 2 * TQ * width * 4 + 4 * length * HD * 2,
        ),
    )(toff, taps_flat, mix_flat, q_blocks, k_heads, v_heads, row_docs, key_docs)


def bwd_kernel(toff_ref, taps_ref, mix_ref, q_ref, qo_ref, k_ref, v_ref, rdoc_ref, kdoc_ref,
               probs_ref, gh_ref, ght_ref, gq_ref, gk_ref, gv_ref, tacc_ref, macc_ref,
               carry_ref, sh_ref, acc_ref, g_ref, gx_ref, *, nw, length, nb, nb_all):
    width = nw * TQ
    step = pl.program_id(0)
    local = nb_all - 1 - step
    block = toff_ref[0] + local
    kstart = window_start(block, nw, length)

    @pl.when(step == 0)
    def _init():
        gk_ref[...] = jnp.zeros(gk_ref.shape, jnp.float32)
        gv_ref[...] = jnp.zeros(gv_ref.shape, jnp.float32)
        tacc_ref[...] = jnp.zeros(tacc_ref.shape, jnp.float32)
        macc_ref[...] = jnp.zeros(macc_ref.shape, jnp.float32)
        carry_ref[...] = jnp.zeros(carry_ref.shape, jnp.float32)

    allowed_ext, allowed_own = masks(block, kstart, width, rdoc_ref, kdoc_ref)
    gm = [
        lax.dot_general(
            gh_ref[0, c], v_ref[c, pl.ds(kstart, width), :], (((1,), (1,)), ((), ())),
            preferred_element_type=jnp.float32,
        )
        for c in range(2)
    ]
    probs = [probs_ref[0, 0], probs_ref[0, 1]]
    gc = []
    for e in range(2):
        gp = mix_ref[e] * gm[0] + mix_ref[2 + e] * gm[1]
        inner = jnp.sum(gp * probs[e], axis=1, keepdims=True)
        gc.append(probs[e] * (gp - inner))

    def own_sums():
        for c in range(2):
            for e in range(2):
                macc_ref[pl.ds(2 * c + e, 1), :] += jnp.sum(gm[c] * probs[e], axis=0, keepdims=True)
            mixed = (mix_ref[2 * c] * probs[0] + mix_ref[2 * c + 1] * probs[1]).astype(jnp.bfloat16)
            gv_ref[c, :, pl.ds(kstart, width)] += jnp.dot(
                ght_ref[0, c], mixed, preferred_element_type=jnp.float32
            )

    def head_taps(e):
        masked_shifts(q_ref, k_ref, e, kstart, width, allowed_ext, sh_ref)
        gcp = jnp.concatenate([jnp.zeros((PAD, width), jnp.float32), gc[e]], axis=0)
        g_ref[0] = gcp
        for a in range(1, QCONV):
            g_ref[a] = pltpu.roll(gcp, EXT - a, 0)
        sums = tap_products(sh_ref, g_ref, live_tiles(block, kstart, nw))
        for b in range(KCONV):
            for a in range(QCONV):
                tacc_ref[e * TAPS + a * KCONV + b] += sums[(a, b)]

    def head_keys(e, gs):
        gk_ref[e, :, pl.ds(kstart, width)] += jnp.dot(
            qo_ref[0, e], gs, preferred_element_type=jnp.float32
        ) * SCALE

    nxt = [carry_ref[e, :, pl.ds(kstart, width + TQ)] for e in range(2)]
    if nb < nb_all:
        pl.when(local < nb)(own_sums)
    else:
        own_sums()
    for e in range(2):
        if nb < nb_all:
            pl.when(local < nb)(lambda: head_taps(e))
        else:
            head_taps(e)
        gx_ref[pl.ds(0, TQ), pl.ds(0, width)] = gc[e]
        gx_ref[pl.ds(0, TQ), pl.ds(width, TQ)] = jnp.zeros((TQ, TQ), jnp.float32)
        gx_ref[pl.ds(TQ, PAD), :] = nxt[e]
        gxv = gx_ref[...]
        sh_ref[0] = gxv[:, :width]
        for b in range(1, KCONV):
            sh_ref[b] = pltpu.roll(gxv, width + TQ - b, 1)[:, :width]
        tap_accumulate(sh_ref, acc_ref, taps_ref, e, live_tiles(block, kstart, nw))
        gmk = acc_ref[0]
        for a in range(1, QCONV):
            gmk = gmk + pltpu.roll(acc_ref[a], EXT - a, 0)
        gs = jnp.where(allowed_own, gmk[:TQ], 0.0).astype(jnp.bfloat16)
        gq_ref[0, e] = (
            jnp.dot(gs, k_ref[e, pl.ds(kstart, width), :], preferred_element_type=jnp.float32) * SCALE
        ).astype(jnp.bfloat16)
        if nb < nb_all:
            pl.when(local < nb)(lambda: head_keys(e, gs))
        else:
            head_keys(e, gs)
    carry_ref[...] = jnp.zeros(carry_ref.shape, jnp.float32)
    for e in range(2):
        carry_ref[e, :, pl.ds(kstart, width)] = gc[e][:PAD]


def attention_backward(toff, taps_flat, mix_flat, q_blocks, q_own, k_heads, v_heads, row_docs, key_docs,
                       probs_blk, gh_blocks, nw, length, nb):
    q_own = jnp.swapaxes(q_own, 2, 3)
    gh_t = jnp.swapaxes(gh_blocks, 2, 3)
    nb_all = q_blocks.shape[0]
    width = nw * TQ
    smem = pl.BlockSpec(memory_space=pltpu.SMEM)
    rev = lambda s: nb_all - 1 - s
    flops = nb_all * 2 * (8 * TQ * width * HD + 6 * TAPS * EXT * width)
    return pl.pallas_call(
        lambda *refs: bwd_kernel(*refs, nw=nw, length=length, nb=nb, nb_all=nb_all),
        grid=(nb_all,),
        in_specs=[
            smem,
            smem,
            smem,
            pl.BlockSpec((1, 2, EXT, HD), lambda s: (rev(s), 0, 0, 0)),
            pl.BlockSpec((1, 2, HD, TQ), lambda s: (rev(s), 0, 0, 0)),
            pl.BlockSpec((2, length, HD), lambda s: (0, 0, 0)),
            pl.BlockSpec((2, length, HD), lambda s: (0, 0, 0)),
            pl.BlockSpec((1, EXT, 1), lambda s: (rev(s), 0, 0)),
            pl.BlockSpec((1, length), lambda s: (0, 0)),
            pl.BlockSpec((1, 2, TQ, width), lambda s: (rev(s), 0, 0, 0)),
            pl.BlockSpec((1, 2, TQ, HD), lambda s: (rev(s), 0, 0, 0)),
            pl.BlockSpec((1, 2, HD, TQ), lambda s: (rev(s), 0, 0, 0)),
        ],
        out_specs=[
            pl.BlockSpec((1, 2, TQ, HD), lambda s: (rev(s), 0, 0, 0)),
            pl.BlockSpec((2, HD, length), lambda s: (0, 0, 0)),
            pl.BlockSpec((2, HD, length), lambda s: (0, 0, 0)),
            pl.BlockSpec((2 * TAPS, 8, 128), lambda s: (0, 0, 0)),
            pl.BlockSpec((4, width), lambda s: (0, 0)),
        ],
        out_shape=[
            jax.ShapeDtypeStruct((nb_all, 2, TQ, HD), jnp.bfloat16),
            jax.ShapeDtypeStruct((2, HD, length), jnp.float32),
            jax.ShapeDtypeStruct((2, HD, length), jnp.float32),
            jax.ShapeDtypeStruct((2 * TAPS, 8, 128), jnp.float32),
            jax.ShapeDtypeStruct((4, width), jnp.float32),
        ],
        scratch_shapes=[
            pltpu.VMEM((2, PAD, length + TQ), jnp.float32),
            pltpu.VMEM((KCONV, EXT, width), jnp.float32),
            pltpu.VMEM((QCONV, EXT, width), jnp.float32),
            pltpu.VMEM((QCONV, EXT, width), jnp.float32),
            pltpu.VMEM((EXT, width + TQ), jnp.float32),
        ],
        compiler_params=pltpu.CompilerParams(
            dimension_semantics=("arbitrary",), vmem_limit_bytes=60 * 1024 * 1024
        ),
        cost_estimate=pl.CostEstimate(
            flops=flops, transcendentals=0,
            bytes_accessed=nb_all * 2 * TQ * width * 4 + 8 * length * HD * 4,
        ),
    )(toff, taps_flat, mix_flat, q_blocks, q_own, k_heads, v_heads, row_docs, key_docs, probs_blk, gh_blocks, gh_t)


def shards_body(
    inputs,
    doc_ids,
    w_query,
    w_key,
    w_value,
    w_out,
    gain_attn,
    gain_ffn,
    conv_taps,
    head_mix,
    w_gate,
    w_up,
    w_down,
    cotangent,
):
    row_dev, blk, width = inputs.shape
    assert row_dev == 1
    seq_count = lax.axis_size("seq")
    row_count = lax.axis_size("row")
    seq_index = lax.axis_index("seq")
    row_index = lax.axis_index("row")
    length = blk * seq_count
    groups = HEADS // 2
    assert seq_count % groups == 0
    splits = seq_count // groups
    span = length // splits
    pw = 2 * HD
    pair = seq_index // splits
    part = seq_index % splits
    q0 = part * span

    flat_in = inputs.reshape(blk, width)
    scale_one = rms_scale(flat_in)
    normed = (flat_in * scale_one * gain_attn).astype(jnp.bfloat16)
    normed_all = lax.all_gather(normed, "seq", axis=0, tiled=True)

    wq_g = lax.dynamic_slice_in_dim(w_query, pair * pw, pw, 1)
    wk_g = lax.dynamic_slice_in_dim(w_key, pair * pw, pw, 1)
    wv_g = lax.dynamic_slice_in_dim(w_value, pair * pw, pw, 1)
    wo_g = lax.dynamic_slice_in_dim(w_out, pair * pw, pw, 0)
    taps = lax.dynamic_slice_in_dim(conv_taps, pair * 2, 2, 0)
    mixing = lax.dynamic_index_in_dim(head_mix, pair, 0, keepdims=False)

    k_all = project(normed_all, wk_g).astype(jnp.bfloat16)
    v_all = project(normed_all, wv_g).astype(jnp.bfloat16)
    k3 = k_all.reshape(length, 2, HD)
    v3 = v_all.reshape(length, 2, HD)

    docs = doc_ids[0]
    nb = span // TQ
    extra = 1 if splits > 1 else 0
    nb_all = nb + extra
    doc_cap = length // 2
    nw = min(length // TQ, (doc_cap + QCONV - 2 + TQ - 1) // TQ + 1)
    q_tail = normed_pad_tail(normed_all, extra)
    q_rows = project(lax.dynamic_slice_in_dim(q_tail, q0, nb_all * TQ + PAD, 0), wq_g).astype(jnp.bfloat16)
    q_blocks = jnp.stack([q_rows[t * TQ : t * TQ + EXT] for t in range(nb_all)])
    q_blocks = jnp.transpose(q_blocks.reshape(nb_all, EXT, 2, HD), (0, 2, 1, 3))
    q_own = q_blocks[:, :, PAD:]
    k_heads = jnp.transpose(k3, (1, 0, 2))
    v_heads = jnp.transpose(v3, (1, 0, 2))
    docs_tail = jnp.pad(docs, (PAD, TQ * extra), constant_values=-1)
    doc_rows = lax.dynamic_slice_in_dim(docs_tail, q0, nb_all * TQ + PAD, 0)
    row_docs = jnp.stack([doc_rows[t * TQ : t * TQ + EXT] for t in range(nb_all)])[:, :, None]
    key_docs = docs[None, :]
    toff = (q0 // TQ).astype(jnp.int32).reshape(1)
    taps_flat = taps.reshape(2 * QCONV * KCONV)
    mix_flat = mixing.reshape(4)
    heads_blk, probs_blk = attention_forward(
        toff, taps_flat, mix_flat, q_blocks, k_heads, v_heads, row_docs, key_docs, nw, length
    )
    heads_own = jnp.transpose(heads_blk[:nb], (0, 2, 1, 3)).reshape(span, pw)

    def to_tokens(values):
        cols = values.shape[1]
        if splits == 1:
            full = values
        else:
            full = lax.dynamic_update_slice_in_dim(
                jnp.zeros((length, cols), values.dtype), values, q0, 0
            )
        got = lax.all_to_all(full, "seq", 0, 0, tiled=True)
        got = got.reshape(groups, splits, blk, cols)
        if splits > 1:
            got = jnp.sum(got.astype(jnp.float32), axis=1).astype(values.dtype)
        else:
            got = got[:, 0]
        return got

    heads_tok = jnp.transpose(to_tokens(heads_own), (1, 0, 2)).reshape(blk, width)
    middle = flat_in + project(heads_tok, w_out)
    scale_two = rms_scale(middle)
    normed_ffn = (middle * scale_two * gain_ffn).astype(jnp.bfloat16)
    hid_width = w_gate.shape[1]
    packed = jnp.concatenate([w_gate, w_up, jnp.transpose(w_down)], axis=1)
    pieces = [packed]
    for k in range(1, row_count):
        route = [(i, (i + k) % row_count) for i in range(row_count)]
        pieces.append(lax.ppermute(packed, "row", route))
    rev = jnp.stack(pieces[::-1] + pieces[::-1])
    full_w = lax.dynamic_slice_in_dim(rev, row_count - 1 - row_index, row_count, 0)
    full_w = full_w.reshape(row_count * packed.shape[0], packed.shape[1])
    joint = full_w[:, : 2 * hid_width]
    down_full = jnp.transpose(full_w[:, 2 * hid_width :])
    ffn_rows = lax.all_gather(normed_ffn, "seq", axis=0, tiled=True)
    gate_up = project(ffn_rows, joint)
    gate_vals = gate_up[:, :hid_width]
    up_vals = gate_up[:, hid_width:]
    hidden = (jax.nn.silu(gate_vals) * up_vals).astype(jnp.bfloat16)
    ffn_part = project(hidden, down_full).astype(jnp.bfloat16)
    cot_flat = cotangent.reshape(blk, width)
    cot_low = cot_flat.astype(jnp.bfloat16)
    cot_rows = lax.all_gather(cot_low, "seq", axis=0, tiled=True)
    grad_hidden = contract_cols(cot_rows, down_full)
    grad_down_part = contract_rows(hidden, cot_rows)
    sigmoid_gate = jax.nn.sigmoid(gate_vals)
    grad_gate_vals = grad_hidden * up_vals * sigmoid_gate * (1.0 + gate_vals * (1.0 - sigmoid_gate))
    grad_up_vals = grad_hidden * gate_vals * sigmoid_gate
    grad_joint = jnp.concatenate([grad_gate_vals, grad_up_vals], axis=1).astype(jnp.bfloat16)
    gnf_part = contract_cols(grad_joint, joint).astype(jnp.bfloat16)
    grad_normed_ffn = lax.psum_scatter(gnf_part, "seq", scatter_dimension=0, tiled=True).astype(jnp.float32)
    grad_joint_w = contract_rows(ffn_rows, grad_joint)
    grad_pack = jnp.concatenate([grad_joint_w, jnp.transpose(grad_down_part)], axis=1)
    band = grad_pack.shape[0] // row_count
    grad_blocks = grad_pack.reshape(row_count, band, grad_pack.shape[1]).astype(jnp.bfloat16)
    ffn_grad = lax.dynamic_index_in_dim(grad_blocks, row_index, 0, keepdims=False).astype(jnp.float32)
    for k in range(1, row_count):
        route = [(i, (i + k) % row_count) for i in range(row_count)]
        sent = lax.dynamic_index_in_dim(grad_blocks, (row_index + k) % row_count, 0, keepdims=False)
        ffn_grad = ffn_grad + lax.ppermute(sent, "row", route).astype(jnp.float32)
    grad_w_gate = ffn_grad[:, :hid_width]
    grad_w_up = ffn_grad[:, hid_width : 2 * hid_width]
    grad_w_down = jnp.transpose(ffn_grad[:, 2 * hid_width :])
    gain_ffn_part = jnp.sum(grad_normed_ffn * middle * scale_two, axis=0)
    scaled_two = grad_normed_ffn * gain_ffn
    grad_middle = (
        cot_flat
        + scale_two * scaled_two
        - middle * scale_two**3 * jnp.mean(scaled_two * middle, axis=-1, keepdims=True)
    )
    grad_attn = grad_middle.astype(jnp.bfloat16)
    grad_attn_all = lax.all_gather(grad_attn, "seq", axis=0, tiled=True)
    ffn_part, grad_attn = lax.optimization_barrier((ffn_part, grad_attn))
    ffn_out = lax.psum_scatter(ffn_part, "seq", scatter_dimension=0, tiled=True).astype(jnp.float32)
    outputs = middle + ffn_out
    gh_tok = contract_cols(grad_attn, w_out).astype(jnp.bfloat16)
    gh_send = jnp.repeat(gh_tok.reshape(blk, groups, pw), splits, axis=1)
    gh_send = jnp.transpose(gh_send, (1, 0, 2)).reshape(seq_count * blk, pw)
    gh_all = lax.all_to_all(gh_send, "seq", 0, 0, tiled=True)
    gh_tail = jnp.pad(gh_all, ((0, TQ * extra), (0, 0)))
    grad_heads_x = lax.dynamic_slice_in_dim(gh_tail, q0, nb_all * TQ, 0)
    gh_blocks = jnp.transpose(grad_heads_x.reshape(nb_all, TQ, 2, HD), (0, 2, 1, 3))
    grad_out_part = contract_rows(heads_own, lax.dynamic_slice_in_dim(grad_attn_all, q0, span, 0))
    gq_blk, gk_heads, gv_heads, tap_acc, mix_acc = attention_backward(
        toff, taps_flat, mix_flat, q_blocks, q_own, k_heads, v_heads, row_docs, key_docs,
        probs_blk, gh_blocks, nw, length, nb,
    )
    grad_q_own = jnp.transpose(gq_blk[:nb], (0, 2, 1, 3)).reshape(span, pw)
    grad_k_part = jnp.transpose(gk_heads, (2, 0, 1)).reshape(length, pw)
    grad_v_part = jnp.transpose(gv_heads, (2, 0, 1)).reshape(length, pw)
    grad_taps_part = jnp.sum(tap_acc, axis=(1, 2)).reshape(2, QCONV, KCONV)
    grad_mix_part = jnp.sum(mix_acc, axis=1).reshape(2, 2)

    def split_sum(values):
        if splits == 1:
            return values
        total = values
        for step in range(1, splits):
            route = []
            for s in range(seq_count):
                base = (s // splits) * splits
                route.append((s, base + (s - base + step) % splits))
            total = total + lax.ppermute(values, "seq", route)
        return total

    grad_k_low = split_sum(grad_k_part).astype(jnp.bfloat16)
    grad_v_low = split_sum(grad_v_part).astype(jnp.bfloat16)
    grad_k_own = lax.dynamic_slice_in_dim(grad_k_low, q0, span, 0)
    grad_v_own = lax.dynamic_slice_in_dim(grad_v_low, q0, span, 0)

    normed_own = lax.dynamic_slice_in_dim(normed_all, q0, span, 0)
    rows_per_dev = width // (row_count * seq_count)

    partials = jnp.stack(
        [
            contract_rows(normed_own, grad_q_own),
            contract_rows(normed_own, grad_k_own),
            contract_rows(normed_own, grad_v_own),
        ]
    )
    devices = row_count * seq_count
    send = partials.astype(jnp.bfloat16).reshape(3, devices, rows_per_dev, pw)
    send = jnp.transpose(send, (1, 0, 2, 3)).reshape(devices * 3 * rows_per_dev, pw)
    got = lax.all_to_all(send, ("row", "seq"), 0, 0, tiled=True).astype(jnp.float32)
    got = got.reshape(row_count, groups, splits, 3, rows_per_dev, pw).sum(axis=(0, 2))
    got = jnp.transpose(got, (1, 2, 0, 3)).reshape(3, rows_per_dev, width)
    grad_w_query, grad_w_key, grad_w_value = got[0], got[1], got[2]

    nchunk = row_count * splits
    out_chunks = grad_out_part.reshape(nchunk, rows_per_dev, width)
    own_slot = row_index * splits + part
    grad_w_out = jnp.zeros((rows_per_dev, width), jnp.float32)
    for k in range(nchunk):
        piece = lax.dynamic_index_in_dim(out_chunks, (own_slot + k) % nchunk, 0, keepdims=False)
        route = []
        for r in range(row_count):
            for g in range(groups):
                for h in range(splits):
                    src_dev = r * seq_count + g * splits + h
                    route.append((src_dev, g * nchunk + (r * splits + h + k) % nchunk))
        grad_w_out = grad_w_out + lax.ppermute(piece, ("row", "seq"), route)

    grad_tok = to_tokens(jnp.concatenate([grad_q_own, grad_k_own, grad_v_own], axis=1))
    grad_tok = grad_tok.reshape(groups, blk, 3, pw)
    gq_tok = jnp.transpose(grad_tok[:, :, 0], (1, 0, 2)).reshape(blk, width)
    gk_tok = jnp.transpose(grad_tok[:, :, 1], (1, 0, 2)).reshape(blk, width)
    gv_tok = jnp.transpose(grad_tok[:, :, 2], (1, 0, 2)).reshape(blk, width)
    grad_normed = (
        contract_cols(gq_tok, w_query) + contract_cols(gk_tok, w_key) + contract_cols(gv_tok, w_value)
    )
    gain_attn_part = jnp.sum(grad_normed * flat_in * scale_one, axis=0)
    scaled_one = grad_normed * gain_attn
    grad_inputs = (
        grad_middle
        + scale_one * scaled_one
        - flat_in * scale_one**3 * jnp.mean(scaled_one * flat_in, axis=-1, keepdims=True)
    )
    taps_full = lax.dynamic_update_slice_in_dim(
        jnp.zeros((HEADS, QCONV, KCONV), jnp.float32), grad_taps_part, pair * 2, 0
    )
    mix_full = lax.dynamic_update_slice_in_dim(
        jnp.zeros((groups, 2, 2), jnp.float32), grad_mix_part[None], pair, 0
    )
    small = jnp.concatenate(
        [gain_attn_part, gain_ffn_part, taps_full.reshape(-1), mix_full.reshape(-1)]
    )
    assert devices & (devices - 1) == 0
    mask = 1
    while mask < devices:
        route = [(i, i ^ mask) for i in range(devices)]
        small = small + lax.ppermute(small, ("row", "seq"), route)
        mask *= 2
    gain_rows = width // (row_count * seq_count)
    gain_at = (row_index * seq_count + seq_index) * gain_rows
    grad_gain_attn = lax.dynamic_slice_in_dim(small, gain_at, gain_rows, 0)
    grad_gain_ffn = lax.dynamic_slice_in_dim(small, width + gain_at, gain_rows, 0)
    grad_taps = small[2 * width : 2 * width + HEADS * TAPS].reshape(HEADS, QCONV, KCONV)
    grad_mix = small[2 * width + HEADS * TAPS :].reshape(groups, 2, 2)
    return (
        outputs.reshape(row_dev, blk, width),
        grad_inputs.reshape(row_dev, blk, width),
        grad_w_query,
        grad_w_key,
        grad_w_value,
        grad_w_out,
        grad_gain_attn,
        grad_gain_ffn,
        grad_taps,
        grad_mix,
        grad_w_gate,
        grad_w_up,
        grad_w_down,
    )


def solution(mesh):
    return jax.shard_map(
        shards_body,
        mesh=mesh,
        in_specs=(
            P("row", "seq", None),
            P("row", None),
            P(),
            P(),
            P(),
            P(),
            P(),
            P(),
            P(),
            P(),
            P("row", "seq"),
            P("row", "seq"),
            P("seq", "row"),
            P("row", "seq", None),
        ),
        out_specs=(
            P("row", "seq", None),
            P("row", "seq", None),
            P(("row", "seq"), None),
            P(("row", "seq"), None),
            P(("row", "seq"), None),
            P(("row", "seq"), None),
            P(("row", "seq")),
            P(("row", "seq")),
            P(),
            P(),
            P("row", "seq"),
            P("row", "seq"),
            P("seq", "row"),
        ),
        check_vma=False,
    )
```

```python
import jax
import jax.numpy as jnp
from jax import lax
from jax.sharding import PartitionSpec as P
from jax.experimental import pallas as pl
from jax.experimental.pallas import tpu as pltpu

HEADS = 16
HD = 96
QCONV = 6
KCONV = 11
PAD = 8
TQ = 128
EXT = TQ + PAD
SCALE = HD ** (-0.5)
TAPS = QCONV * KCONV

epsilon = 1e-06


def rms_scale(values):
    return lax.rsqrt(jnp.mean(values * values, axis=-1, keepdims=True) + epsilon)


def project(values, weight):
    return jnp.dot(values, weight, preferred_element_type=jnp.float32)


def contract_rows(left, right):
    return lax.dot_general(
        left, right, (((0,), (0,)), ((), ())), preferred_element_type=jnp.float32
    )


def contract_cols(left, right):
    return lax.dot_general(
        left, right, (((1,), (1,)), ((), ())), preferred_element_type=jnp.float32
    )


def normed_pad_tail(values, extra):
    return jnp.pad(values, ((PAD, TQ * extra), (0, 0)))


def window_start(block, nw, length):
    return pl.multiple_of(jnp.clip((block - nw + 1) * TQ, 0, length - nw * TQ), TQ)


def tap_accumulate(sh_ref, acc_ref, taps_ref, head, live):

    def body(col, carry):
        c0 = pl.multiple_of(col * 128, 128)
        for r0 in range(0, EXT, 8):
            tiles = [sh_ref[b, pl.ds(r0, 8), pl.ds(c0, 128)] for b in range(KCONV)]
            for a in range(QCONV):
                base = head * TAPS + a * KCONV
                total = taps_ref[base] * tiles[0]
                for b in range(1, KCONV):
                    total = total + taps_ref[base + b] * tiles[b]
                acc_ref[a, pl.ds(r0, 8), pl.ds(c0, 128)] = total
        return carry

    lax.fori_loop(0, live, body, 0)


def tap_products(sh_ref, g_ref, live):
    sums = {}
    for a0 in range(0, QCONV, 2):

        def body(col, accs):
            c0 = pl.multiple_of(col * 128, 128)
            out = list(accs)
            for r0 in range(0, EXT, 8):
                ga = [g_ref[a0 + k, pl.ds(r0, 8), pl.ds(c0, 128)] for k in range(2)]
                for b in range(KCONV):
                    tile = sh_ref[b, pl.ds(r0, 8), pl.ds(c0, 128)]
                    for k in range(2):
                        out[k * KCONV + b] = out[k * KCONV + b] + ga[k] * tile
            return tuple(out)

        start = tuple(jnp.zeros((8, 128), jnp.float32) for _ in range(2 * KCONV))
        res = lax.fori_loop(0, live, body, start)
        for k in range(2):
            for b in range(KCONV):
                sums[(a0 + k, b)] = res[k * KCONV + b]
    return sums


def live_tiles(block, kstart, nw):
    return jnp.clip(block + 1 - kstart // TQ, 1, nw)


def masks(block, kstart, width, rdoc_ref, kdoc_ref):
    keydoc = kdoc_ref[:, pl.ds(kstart, width)]
    ext_pos = block * TQ - PAD + lax.broadcasted_iota(jnp.int32, (EXT, width), 0)
    key_ext = kstart + lax.broadcasted_iota(jnp.int32, (EXT, width), 1)
    allowed_ext = (key_ext <= ext_pos) & (rdoc_ref[0] == keydoc)
    own_pos = block * TQ + lax.broadcasted_iota(jnp.int32, (TQ, width), 0)
    key_own = kstart + lax.broadcasted_iota(jnp.int32, (TQ, width), 1)
    allowed_own = (key_own <= own_pos) & (rdoc_ref[0, PAD:, :] == keydoc)
    return allowed_ext, allowed_own


def masked_shifts(q_ref, k_ref, head, kstart, width, allowed_ext, sh_ref):
    keys = k_ref[head, pl.ds(kstart, width), :]
    scores = lax.dot_general(
        q_ref[0, head], keys, (((1,), (1,)), ((), ())), preferred_element_type=jnp.float32
    ) * SCALE
    masked = jnp.where(allowed_ext, scores, 0.0)
    col = lax.broadcasted_iota(jnp.int32, (EXT, width), 1)
    sh_ref[0] = masked
    for b in range(1, KCONV):
        sh_ref[b] = jnp.where(col >= b, pltpu.roll(masked, b, 1), 0.0)


def fwd_kernel(toff_ref, taps_ref, mix_ref, q_ref, k_ref, v_ref, rdoc_ref, kdoc_ref,
               heads_ref, probs_ref, sh_ref, acc_ref, *, nw, length):
    width = nw * TQ
    block = toff_ref[0] + pl.program_id(0)
    kstart = window_start(block, nw, length)
    allowed_ext, allowed_own = masks(block, kstart, width, rdoc_ref, kdoc_ref)
    for head in range(2):
        masked_shifts(q_ref, k_ref, head, kstart, width, allowed_ext, sh_ref)
        tap_accumulate(sh_ref, acc_ref, taps_ref, head, live_tiles(block, kstart, nw))
        conv = acc_ref[0]
        for a in range(1, QCONV):
            conv = conv + pltpu.roll(acc_ref[a], a, 0)
        logits = jnp.where(allowed_own, conv[PAD:], -jnp.inf)
        highest = jnp.max(logits, axis=1, keepdims=True)
        highest = jnp.where(highest > -jnp.inf, highest, 0.0)
        expd = jnp.exp(logits - highest)
        denom = jnp.sum(expd, axis=1, keepdims=True)
        probs_ref[0, head] = expd / jnp.where(denom > 0.0, denom, 1.0)
    p0 = probs_ref[0, 0]
    p1 = probs_ref[0, 1]
    for c in range(2):
        mixed = (mix_ref[2 * c] * p0 + mix_ref[2 * c + 1] * p1).astype(jnp.bfloat16)
        heads_ref[0, c] = jnp.dot(
            mixed, v_ref[c, pl.ds(kstart, width), :], preferred_element_type=jnp.float32
        ).astype(jnp.bfloat16)


def attention_forward(toff, taps_flat, mix_flat, q_blocks, k_heads, v_heads, row_docs, key_docs, nw, length):
    nb_all = q_blocks.shape[0]
    width = nw * TQ
    smem = pl.BlockSpec(memory_space=pltpu.SMEM)
    flops = nb_all * 2 * (4 * EXT * width * HD + 2 * TAPS * EXT * width)
    return pl.pallas_call(
        lambda *refs: fwd_kernel(*refs, nw=nw, length=length),
        grid=(nb_all,),
        in_specs=[
            smem,
            smem,
            smem,
            pl.BlockSpec((1, 2, EXT, HD), lambda t: (t, 0, 0, 0)),
            pl.BlockSpec((2, length, HD), lambda t: (0, 0, 0)),
            pl.BlockSpec((2, length, HD), lambda t: (0, 0, 0)),
            pl.BlockSpec((1, EXT, 1), lambda t: (t, 0, 0)),
            pl.BlockSpec((1, length), lambda t: (0, 0)),
        ],
        out_specs=[
            pl.BlockSpec((1, 2, TQ, HD), lambda t: (t, 0, 0, 0)),
            pl.BlockSpec((1, 2, TQ, width), lambda t: (t, 0, 0, 0)),
        ],
        out_shape=[
            jax.ShapeDtypeStruct((nb_all, 2, TQ, HD), jnp.bfloat16),
            jax.ShapeDtypeStruct((nb_all, 2, TQ, width), jnp.float32),
        ],
        scratch_shapes=[
            pltpu.VMEM((KCONV, EXT, width), jnp.float32),
            pltpu.VMEM((QCONV, EXT, width), jnp.float32),
        ],
        compiler_params=pltpu.CompilerParams(
            dimension_semantics=("arbitrary",), vmem_limit_bytes=56 * 1024 * 1024
        ),
        cost_estimate=pl.CostEstimate(
            flops=flops, transcendentals=nb_all * 2 * TQ * width,
            bytes_accessed=nb_all * 2 * TQ * width * 4 + 4 * length * HD * 2,
        ),
    )(toff, taps_flat, mix_flat, q_blocks, k_heads, v_heads, row_docs, key_docs)


def bwd_kernel(toff_ref, taps_ref, mix_ref, q_ref, qo_ref, k_ref, v_ref, rdoc_ref, kdoc_ref,
               probs_ref, gh_ref, ght_ref, gq_ref, gk_ref, gv_ref, tacc_ref, macc_ref,
               carry_ref, sh_ref, acc_ref, g_ref, gx_ref, *, nw, length, nb, nb_all):
    width = nw * TQ
    step = pl.program_id(0)
    local = nb_all - 1 - step
    block = toff_ref[0] + local
    kstart = window_start(block, nw, length)

    @pl.when(step == 0)
    def _init():
        gk_ref[...] = jnp.zeros(gk_ref.shape, jnp.float32)
        gv_ref[...] = jnp.zeros(gv_ref.shape, jnp.float32)
        tacc_ref[...] = jnp.zeros(tacc_ref.shape, jnp.float32)
        macc_ref[...] = jnp.zeros(macc_ref.shape, jnp.float32)
        carry_ref[...] = jnp.zeros(carry_ref.shape, jnp.float32)

    allowed_ext, allowed_own = masks(block, kstart, width, rdoc_ref, kdoc_ref)
    gm = [
        lax.dot_general(
            gh_ref[0, c], v_ref[c, pl.ds(kstart, width), :], (((1,), (1,)), ((), ())),
            preferred_element_type=jnp.float32,
        )
        for c in range(2)
    ]
    probs = [probs_ref[0, 0], probs_ref[0, 1]]
    gc = []
    for e in range(2):
        gp = mix_ref[e] * gm[0] + mix_ref[2 + e] * gm[1]
        inner = jnp.sum(gp * probs[e], axis=1, keepdims=True)
        gc.append(probs[e] * (gp - inner))

    def own_sums():
        for c in range(2):
            for e in range(2):
                macc_ref[pl.ds(2 * c + e, 1), :] += jnp.sum(gm[c] * probs[e], axis=0, keepdims=True)
            mixed = (mix_ref[2 * c] * probs[0] + mix_ref[2 * c + 1] * probs[1]).astype(jnp.bfloat16)
            gv_ref[c, :, pl.ds(kstart, width)] += jnp.dot(
                ght_ref[0, c], mixed, preferred_element_type=jnp.float32
            )

    def head_taps(e):
        masked_shifts(q_ref, k_ref, e, kstart, width, allowed_ext, sh_ref)
        gcp = jnp.concatenate([jnp.zeros((PAD, width), jnp.float32), gc[e]], axis=0)
        g_ref[0] = gcp
        for a in range(1, QCONV):
            g_ref[a] = pltpu.roll(gcp, EXT - a, 0)
        sums = tap_products(sh_ref, g_ref, live_tiles(block, kstart, nw))
        for b in range(KCONV):
            for a in range(QCONV):
                tacc_ref[e * TAPS + a * KCONV + b] += sums[(a, b)]

    def head_keys(e, gs):
        gk_ref[e, :, pl.ds(kstart, width)] += jnp.dot(
            qo_ref[0, e], gs, preferred_element_type=jnp.float32
        ) * SCALE

    nxt = [carry_ref[e, :, pl.ds(kstart, width + TQ)] for e in range(2)]
    if nb < nb_all:
        pl.when(local < nb)(own_sums)
    else:
        own_sums()
    for e in range(2):
        if nb < nb_all:
            pl.when(local < nb)(lambda: head_taps(e))
        else:
            head_taps(e)
        gx_ref[pl.ds(0, TQ), pl.ds(0, width)] = gc[e]
        gx_ref[pl.ds(0, TQ), pl.ds(width, TQ)] = jnp.zeros((TQ, TQ), jnp.float32)
        gx_ref[pl.ds(TQ, PAD), :] = nxt[e]
        gxv = gx_ref[...]
        sh_ref[0] = gxv[:, :width]
        for b in range(1, KCONV):
            sh_ref[b] = pltpu.roll(gxv, width + TQ - b, 1)[:, :width]
        tap_accumulate(sh_ref, acc_ref, taps_ref, e, live_tiles(block, kstart, nw))
        gmk = acc_ref[0]
        for a in range(1, QCONV):
            gmk = gmk + pltpu.roll(acc_ref[a], EXT - a, 0)
        gs = jnp.where(allowed_own, gmk[:TQ], 0.0).astype(jnp.bfloat16)
        gq_ref[0, e] = (
            jnp.dot(gs, k_ref[e, pl.ds(kstart, width), :], preferred_element_type=jnp.float32) * SCALE
        ).astype(jnp.bfloat16)
        if nb < nb_all:
            pl.when(local < nb)(lambda: head_keys(e, gs))
        else:
            head_keys(e, gs)
    carry_ref[...] = jnp.zeros(carry_ref.shape, jnp.float32)
    for e in range(2):
        carry_ref[e, :, pl.ds(kstart, width)] = gc[e][:PAD]


def attention_backward(toff, taps_flat, mix_flat, q_blocks, q_own, k_heads, v_heads, row_docs, key_docs,
                       probs_blk, gh_blocks, nw, length, nb):
    q_own = jnp.swapaxes(q_own, 2, 3)
    gh_t = jnp.swapaxes(gh_blocks, 2, 3)
    nb_all = q_blocks.shape[0]
    width = nw * TQ
    smem = pl.BlockSpec(memory_space=pltpu.SMEM)
    rev = lambda s: nb_all - 1 - s
    flops = nb_all * 2 * (8 * TQ * width * HD + 6 * TAPS * EXT * width)
    return pl.pallas_call(
        lambda *refs: bwd_kernel(*refs, nw=nw, length=length, nb=nb, nb_all=nb_all),
        grid=(nb_all,),
        in_specs=[
            smem,
            smem,
            smem,
            pl.BlockSpec((1, 2, EXT, HD), lambda s: (rev(s), 0, 0, 0)),
            pl.BlockSpec((1, 2, HD, TQ), lambda s: (rev(s), 0, 0, 0)),
            pl.BlockSpec((2, length, HD), lambda s: (0, 0, 0)),
            pl.BlockSpec((2, length, HD), lambda s: (0, 0, 0)),
            pl.BlockSpec((1, EXT, 1), lambda s: (rev(s), 0, 0)),
            pl.BlockSpec((1, length), lambda s: (0, 0)),
            pl.BlockSpec((1, 2, TQ, width), lambda s: (rev(s), 0, 0, 0)),
            pl.BlockSpec((1, 2, TQ, HD), lambda s: (rev(s), 0, 0, 0)),
            pl.BlockSpec((1, 2, HD, TQ), lambda s: (rev(s), 0, 0, 0)),
        ],
        out_specs=[
            pl.BlockSpec((1, 2, TQ, HD), lambda s: (rev(s), 0, 0, 0)),
            pl.BlockSpec((2, HD, length), lambda s: (0, 0, 0)),
            pl.BlockSpec((2, HD, length), lambda s: (0, 0, 0)),
            pl.BlockSpec((2 * TAPS, 8, 128), lambda s: (0, 0, 0)),
            pl.BlockSpec((4, width), lambda s: (0, 0)),
        ],
        out_shape=[
            jax.ShapeDtypeStruct((nb_all, 2, TQ, HD), jnp.bfloat16),
            jax.ShapeDtypeStruct((2, HD, length), jnp.float32),
            jax.ShapeDtypeStruct((2, HD, length), jnp.float32),
            jax.ShapeDtypeStruct((2 * TAPS, 8, 128), jnp.float32),
            jax.ShapeDtypeStruct((4, width), jnp.float32),
        ],
        scratch_shapes=[
            pltpu.VMEM((2, PAD, length + TQ), jnp.float32),
            pltpu.VMEM((KCONV, EXT, width), jnp.float32),
            pltpu.VMEM((QCONV, EXT, width), jnp.float32),
            pltpu.VMEM((QCONV, EXT, width), jnp.float32),
            pltpu.VMEM((EXT, width + TQ), jnp.float32),
        ],
        compiler_params=pltpu.CompilerParams(
            dimension_semantics=("arbitrary",), vmem_limit_bytes=60 * 1024 * 1024
        ),
        cost_estimate=pl.CostEstimate(
            flops=flops, transcendentals=0,
            bytes_accessed=nb_all * 2 * TQ * width * 4 + 8 * length * HD * 4,
        ),
    )(toff, taps_flat, mix_flat, q_blocks, q_own, k_heads, v_heads, row_docs, key_docs, probs_blk, gh_blocks, gh_t)


def shards_body(
    inputs,
    doc_ids,
    w_query,
    w_key,
    w_value,
    w_out,
    gain_attn,
    gain_ffn,
    conv_taps,
    head_mix,
    w_gate,
    w_up,
    w_down,
    cotangent,
):
    row_dev, blk, width = inputs.shape
    assert row_dev == 1
    seq_count = lax.axis_size("seq")
    row_count = lax.axis_size("row")
    seq_index = lax.axis_index("seq")
    row_index = lax.axis_index("row")
    length = blk * seq_count
    groups = HEADS // 2
    assert seq_count % groups == 0
    splits = seq_count // groups
    span = length // splits
    pw = 2 * HD
    pair = seq_index // splits
    part = seq_index % splits
    q0 = part * span

    flat_in = inputs.reshape(blk, width)
    scale_one = rms_scale(flat_in)
    normed = (flat_in * scale_one * gain_attn).astype(jnp.bfloat16)
    normed_all = lax.all_gather(normed, "seq", axis=0, tiled=True)

    wq_g = lax.dynamic_slice_in_dim(w_query, pair * pw, pw, 1)
    wk_g = lax.dynamic_slice_in_dim(w_key, pair * pw, pw, 1)
    wv_g = lax.dynamic_slice_in_dim(w_value, pair * pw, pw, 1)
    wo_g = lax.dynamic_slice_in_dim(w_out, pair * pw, pw, 0)
    taps = lax.dynamic_slice_in_dim(conv_taps, pair * 2, 2, 0)
    mixing = lax.dynamic_index_in_dim(head_mix, pair, 0, keepdims=False)

    k_all = project(normed_all, wk_g).astype(jnp.bfloat16)
    v_all = project(normed_all, wv_g).astype(jnp.bfloat16)
    k3 = k_all.reshape(length, 2, HD)
    v3 = v_all.reshape(length, 2, HD)

    docs = doc_ids[0]
    nb = span // TQ
    extra = 1 if splits > 1 else 0
    nb_all = nb + extra
    doc_cap = length // 2
    nw = min(length // TQ, (doc_cap + QCONV - 2 + TQ - 1) // TQ + 1)
    q_tail = normed_pad_tail(normed_all, extra)
    q_rows = project(lax.dynamic_slice_in_dim(q_tail, q0, nb_all * TQ + PAD, 0), wq_g).astype(jnp.bfloat16)
    q_blocks = jnp.stack([q_rows[t * TQ : t * TQ + EXT] for t in range(nb_all)])
    q_blocks = jnp.transpose(q_blocks.reshape(nb_all, EXT, 2, HD), (0, 2, 1, 3))
    q_own = q_blocks[:, :, PAD:]
    k_heads = jnp.transpose(k3, (1, 0, 2))
    v_heads = jnp.transpose(v3, (1, 0, 2))
    docs_tail = jnp.pad(docs, (PAD, TQ * extra), constant_values=-1)
    doc_rows = lax.dynamic_slice_in_dim(docs_tail, q0, nb_all * TQ + PAD, 0)
    row_docs = jnp.stack([doc_rows[t * TQ : t * TQ + EXT] for t in range(nb_all)])[:, :, None]
    key_docs = docs[None, :]
    toff = (q0 // TQ).astype(jnp.int32).reshape(1)
    taps_flat = taps.reshape(2 * QCONV * KCONV)
    mix_flat = mixing.reshape(4)
    heads_blk, probs_blk = attention_forward(
        toff, taps_flat, mix_flat, q_blocks, k_heads, v_heads, row_docs, key_docs, nw, length
    )
    heads_own = jnp.transpose(heads_blk[:nb], (0, 2, 1, 3)).reshape(span, pw)

    def to_tokens(values):
        cols = values.shape[1]
        if splits == 1:
            full = values
        else:
            full = lax.dynamic_update_slice_in_dim(
                jnp.zeros((length, cols), values.dtype), values, q0, 0
            )
        got = lax.all_to_all(full, "seq", 0, 0, tiled=True)
        got = got.reshape(groups, splits, blk, cols)
        if splits > 1:
            got = jnp.sum(got.astype(jnp.float32), axis=1).astype(values.dtype)
        else:
            got = got[:, 0]
        return got

    heads_tok = jnp.transpose(to_tokens(heads_own), (1, 0, 2)).reshape(blk, width)
    middle = flat_in + project(heads_tok, w_out)
    scale_two = rms_scale(middle)
    normed_ffn = (middle * scale_two * gain_ffn).astype(jnp.bfloat16)
    hid_width = w_gate.shape[1]
    packed = jnp.concatenate([w_gate, w_up, jnp.transpose(w_down)], axis=1)
    pieces = [packed]
    for k in range(1, row_count):
        route = [(i, (i + k) % row_count) for i in range(row_count)]
        pieces.append(lax.ppermute(packed, "row", route))
    rev = jnp.stack(pieces[::-1] + pieces[::-1])
    full_w = lax.dynamic_slice_in_dim(rev, row_count - 1 - row_index, row_count, 0)
    full_w = full_w.reshape(row_count * packed.shape[0], packed.shape[1])
    joint = full_w[:, : 2 * hid_width]
    down_full = jnp.transpose(full_w[:, 2 * hid_width :])
    ffn_rows = lax.all_gather(normed_ffn, "seq", axis=0, tiled=True)
    gate_up = project(ffn_rows, joint)
    gate_vals = gate_up[:, :hid_width]
    up_vals = gate_up[:, hid_width:]
    hidden = (jax.nn.silu(gate_vals) * up_vals).astype(jnp.bfloat16)
    ffn_part = project(hidden, down_full).astype(jnp.bfloat16)
    cot_flat = cotangent.reshape(blk, width)
    cot_low = cot_flat.astype(jnp.bfloat16)
    cot_rows = lax.all_gather(cot_low, "seq", axis=0, tiled=True)
    grad_hidden = contract_cols(cot_rows, down_full)
    grad_down_part = contract_rows(hidden, cot_rows)
    sigmoid_gate = jax.nn.sigmoid(gate_vals)
    grad_gate_vals = grad_hidden * up_vals * sigmoid_gate * (1.0 + gate_vals * (1.0 - sigmoid_gate))
    grad_up_vals = grad_hidden * gate_vals * sigmoid_gate
    grad_joint = jnp.concatenate([grad_gate_vals, grad_up_vals], axis=1).astype(jnp.bfloat16)
    gnf_part = contract_cols(grad_joint, joint).astype(jnp.bfloat16)
    grad_normed_ffn = lax.psum_scatter(gnf_part, "seq", scatter_dimension=0, tiled=True).astype(jnp.float32)
    grad_joint_w = contract_rows(ffn_rows, grad_joint)
    grad_pack = jnp.concatenate([grad_joint_w, jnp.transpose(grad_down_part)], axis=1)
    band = grad_pack.shape[0] // row_count
    grad_blocks = grad_pack.reshape(row_count, band, grad_pack.shape[1]).astype(jnp.bfloat16)
    ffn_grad = lax.dynamic_index_in_dim(grad_blocks, row_index, 0, keepdims=False).astype(jnp.float32)
    for k in range(1, row_count):
        route = [(i, (i + k) % row_count) for i in range(row_count)]
        sent = lax.dynamic_index_in_dim(grad_blocks, (row_index + k) % row_count, 0, keepdims=False)
        ffn_grad = ffn_grad + lax.ppermute(sent, "row", route).astype(jnp.float32)
    grad_w_gate = ffn_grad[:, :hid_width]
    grad_w_up = ffn_grad[:, hid_width : 2 * hid_width]
    grad_w_down = jnp.transpose(ffn_grad[:, 2 * hid_width :])
    gain_ffn_part = jnp.sum(grad_normed_ffn * middle * scale_two, axis=0)
    scaled_two = grad_normed_ffn * gain_ffn
    grad_middle = (
        cot_flat
        + scale_two * scaled_two
        - middle * scale_two**3 * jnp.mean(scaled_two * middle, axis=-1, keepdims=True)
    )
    grad_attn = grad_middle.astype(jnp.bfloat16)
    grad_attn_all = lax.all_gather(grad_attn, "seq", axis=0, tiled=True)
    ffn_part, grad_attn = lax.optimization_barrier((ffn_part, grad_attn))
    ffn_out = lax.psum_scatter(ffn_part, "seq", scatter_dimension=0, tiled=True).astype(jnp.float32)
    outputs = middle + ffn_out
    gh_tok = contract_cols(grad_attn, w_out).astype(jnp.bfloat16)
    gh_send = jnp.repeat(gh_tok.reshape(blk, groups, pw), splits, axis=1)
    gh_send = jnp.transpose(gh_send, (1, 0, 2)).reshape(seq_count * blk, pw)
    gh_all = lax.all_to_all(gh_send, "seq", 0, 0, tiled=True)
    gh_tail = jnp.pad(gh_all, ((0, TQ * extra), (0, 0)))
    grad_heads_x = lax.dynamic_slice_in_dim(gh_tail, q0, nb_all * TQ, 0)
    gh_blocks = jnp.transpose(grad_heads_x.reshape(nb_all, TQ, 2, HD), (0, 2, 1, 3))
    grad_out_part = contract_rows(heads_own, lax.dynamic_slice_in_dim(grad_attn_all, q0, span, 0))
    gq_blk, gk_heads, gv_heads, tap_acc, mix_acc = attention_backward(
        toff, taps_flat, mix_flat, q_blocks, q_own, k_heads, v_heads, row_docs, key_docs,
        probs_blk, gh_blocks, nw, length, nb,
    )
    grad_q_own = jnp.transpose(gq_blk[:nb], (0, 2, 1, 3)).reshape(span, pw)
    grad_k_part = jnp.transpose(gk_heads, (2, 0, 1)).reshape(length, pw)
    grad_v_part = jnp.transpose(gv_heads, (2, 0, 1)).reshape(length, pw)
    grad_taps_part = jnp.sum(tap_acc, axis=(1, 2)).reshape(2, QCONV, KCONV)
    grad_mix_part = jnp.sum(mix_acc, axis=1).reshape(2, 2)

    def split_sum(values):
        if splits == 1:
            return values
        total = values
        for step in range(1, splits):
            route = []
            for s in range(seq_count):
                base = (s // splits) * splits
                route.append((s, base + (s - base + step) % splits))
            total = total + lax.ppermute(values, "seq", route)
        return total

    grad_k_low = split_sum(grad_k_part).astype(jnp.bfloat16)
    grad_v_low = split_sum(grad_v_part).astype(jnp.bfloat16)
    grad_k_own = lax.dynamic_slice_in_dim(grad_k_low, q0, span, 0)
    grad_v_own = lax.dynamic_slice_in_dim(grad_v_low, q0, span, 0)

    normed_own = lax.dynamic_slice_in_dim(normed_all, q0, span, 0)
    rows_per_dev = width // (row_count * seq_count)

    partials = jnp.stack(
        [
            contract_rows(normed_own, grad_q_own),
            contract_rows(normed_own, grad_k_own),
            contract_rows(normed_own, grad_v_own),
        ]
    )
    devices = row_count * seq_count
    send = partials.astype(jnp.bfloat16).reshape(3, devices, rows_per_dev, pw)
    send = jnp.transpose(send, (1, 0, 2, 3)).reshape(devices * 3 * rows_per_dev, pw)
    got = lax.all_to_all(send, ("row", "seq"), 0, 0, tiled=True).astype(jnp.float32)
    got = got.reshape(row_count, groups, splits, 3, rows_per_dev, pw).sum(axis=(0, 2))
    got = jnp.transpose(got, (1, 2, 0, 3)).reshape(3, rows_per_dev, width)
    grad_w_query, grad_w_key, grad_w_value = got[0], got[1], got[2]

    red_out = lax.psum_scatter(grad_out_part, "row", scatter_dimension=0, tiled=True)
    red_out = red_out.reshape(splits, rows_per_dev, width)
    grad_w_out = jnp.zeros((rows_per_dev, width), jnp.float32)
    for src_part in range(splits):
        for j in range(splits):
            route = []
            for r in range(row_count):
                for g in range(groups):
                    src = r * seq_count + g * splits + src_part
                    dst = g * row_count * splits + r * splits + j
                    route.append((src, dst))
            grad_w_out = grad_w_out + lax.ppermute(red_out[j], ("row", "seq"), route)

    grad_tok = to_tokens(jnp.concatenate([grad_q_own, grad_k_own, grad_v_own], axis=1))
    grad_tok = grad_tok.reshape(groups, blk, 3, pw)
    gq_tok = jnp.transpose(grad_tok[:, :, 0], (1, 0, 2)).reshape(blk, width)
    gk_tok = jnp.transpose(grad_tok[:, :, 1], (1, 0, 2)).reshape(blk, width)
    gv_tok = jnp.transpose(grad_tok[:, :, 2], (1, 0, 2)).reshape(blk, width)
    grad_normed = (
        contract_cols(gq_tok, w_query) + contract_cols(gk_tok, w_key) + contract_cols(gv_tok, w_value)
    )
    gain_attn_part = jnp.sum(grad_normed * flat_in * scale_one, axis=0)
    scaled_one = grad_normed * gain_attn
    grad_inputs = (
        grad_middle
        + scale_one * scaled_one
        - flat_in * scale_one**3 * jnp.mean(scaled_one * flat_in, axis=-1, keepdims=True)
    )
    taps_full = lax.dynamic_update_slice_in_dim(
        jnp.zeros((HEADS, QCONV, KCONV), jnp.float32), grad_taps_part, pair * 2, 0
    )
    mix_full = lax.dynamic_update_slice_in_dim(
        jnp.zeros((groups, 2, 2), jnp.float32), grad_mix_part[None], pair, 0
    )
    small = jnp.concatenate(
        [gain_attn_part, gain_ffn_part, taps_full.reshape(-1), mix_full.reshape(-1)]
    )
    assert devices & (devices - 1) == 0
    mask = 1
    while mask < devices:
        route = [(i, i ^ mask) for i in range(devices)]
        small = small + lax.ppermute(small, ("row", "seq"), route)
        mask *= 2
    gain_rows = width // (row_count * seq_count)
    gain_at = (row_index * seq_count + seq_index) * gain_rows
    grad_gain_attn = lax.dynamic_slice_in_dim(small, gain_at, gain_rows, 0)
    grad_gain_ffn = lax.dynamic_slice_in_dim(small, width + gain_at, gain_rows, 0)
    grad_taps = small[2 * width : 2 * width + HEADS * TAPS].reshape(HEADS, QCONV, KCONV)
    grad_mix = small[2 * width + HEADS * TAPS :].reshape(groups, 2, 2)
    return (
        outputs.reshape(row_dev, blk, width),
        grad_inputs.reshape(row_dev, blk, width),
        grad_w_query,
        grad_w_key,
        grad_w_value,
        grad_w_out,
        grad_gain_attn,
        grad_gain_ffn,
        grad_taps,
        grad_mix,
        grad_w_gate,
        grad_w_up,
        grad_w_down,
    )


def solution(mesh):
    return jax.shard_map(
        shards_body,
        mesh=mesh,
        in_specs=(
            P("row", "seq", None),
            P("row", None),
            P(),
            P(),
            P(),
            P(),
            P(),
            P(),
            P(),
            P(),
            P("row", "seq"),
            P("row", "seq"),
            P("seq", "row"),
            P("row", "seq", None),
        ),
        out_specs=(
            P("row", "seq", None),
            P("row", "seq", None),
            P(("row", "seq"), None),
            P(("row", "seq"), None),
            P(("row", "seq"), None),
            P(("row", "seq"), None),
            P(("row", "seq")),
            P(("row", "seq")),
            P(),
            P(),
            P("row", "seq"),
            P("row", "seq"),
            P("seq", "row"),
        ),
        check_vma=False,
    )
```
